128 devices in a mesh: gx: 8 (over z, core), gy: 16 (over y, x).
Axes of the slice: x: 4, y: 4, z: 4, core: 2. Of those that a mesh axis runs over, the one named last changes fastest.
Arguments:
- atm_state: float32 [128, 512, 4096], P(None, 'gy', 'gx'), may hold values from -6 to 6
- atm_kappa: float32 [128], replicated, may hold values from 0.05 to 0.24
- vert_weight: float32 [4, 128], replicated, may hold values from -0.5 to 0.5
- remap_src: int32 [4096, 4], replicated, may hold values from 0 to 16383, as said below
- remap_count: int32 [4096], replicated, may hold values from 2 to 4, as said below
- remap_weight: bfloat16 [4096, 4, 128, 128], P(('gx', 'gy')), may hold values from -1 to 1
- land_mask: int32 [256, 2048], P('gy', 'gx'), may hold values from 0 to 1
- ocean_term: float32 [256, 2048], P('gy', 'gx'), may hold values from 0.5 to 8
Outputs:
- atm_out: float32 [128, 512, 4096], P(None, 'gy', 'gx')
- ocean_flux: float32 [4, 256, 2048], P(None, 'gy', 'gx')
- surface_height: float32 [256, 2048], P('gy', 'gx')
- residual: float32 [256, 2048], P('gy', 'gx')
The draws below stay inside these ranges and needn't reach their ends.
Inputs may be any that keep to these rules, and one draw needn't show every extreme that they name: `remap_src`: entries are global atmosphere block numbers covering the ocean block's area: each names a block of the atmosphere device with the same tile indices or of the next device along gx (gx index plus one, the last wrapping to 0, same gy index). Among the live entries of the 32 ocean blocks of one device, exactly 32 name blocks of the next device. `remap_count`: the first ocean block of every device has all 4 entries live.
All inputs are finite; a program needn't handle non-finite values.
Results may differ from the reference program's by a relative error of at most 0.003.
Values may be sent and summed in bfloat16 or wider, within the bound.
No kernel may reach another device: no remote copies, remote signals or barrier semaphores. Data moves between devices by JAX's collectives and lax.ppermute only.
A program may use at most 128 MiB of HBM per device.

```python
import math
import jax
import jax.numpy as jnp
from jax import lax

LEV = 128
FC = 4
BLK = 128
K = 4
STEPS = 4
ITERS = 3
AX = 512
AY = 32
NDEV = 128
ALON = 4096
ALAT = 512
OX = 256
OY = 16
OLON = 2048
OLAT = 256
ABLK = 128
OB = 32
OBG = 4096
N_GX = 8
N_GY = 16


def draw_remap_src(key, part):
    ids = jnp.arange(NDEV * OB, dtype=jnp.int32)
    device = ids // OB
    local = ids % OB
    col_i = device // N_GY
    row_j = device % N_GY
    per_row = OX // BLK
    segs = AX // BLK
    ocean_row = local // per_row
    segment = local % per_row
    west_seg = 2 * segment + 1
    east_raw = 2 * segment + 2
    crosses = east_raw >= segs
    east_seg = jnp.where(crosses, east_raw - segs, east_raw)
    east_dev = jnp.where(crosses, (col_i + 1) % N_GX * N_GY + row_j, device)
    upper = 2 * ocean_row
    lower = 2 * ocean_row + 1
    e_up = east_dev * ABLK + upper * segs + east_seg
    e_low = east_dev * ABLK + lower * segs + east_seg
    w_up = device * ABLK + upper * segs + west_seg
    w_low = device * ABLK + lower * segs + west_seg
    flips = jax.random.randint(jax.random.fold_in(key, 11), (NDEV * OB, 2), 0, 2).astype(jnp.int32)
    first_pair = jnp.where(flips[:, 0:1] == 1, jnp.stack([e_low, e_up], 1), jnp.stack([e_up, e_low], 1))
    second_pair = jnp.where(flips[:, 1:2] == 1, jnp.stack([w_low, w_up], 1), jnp.stack([w_up, w_low], 1))
    return jnp.concatenate([first_pair, second_pair], axis=1).astype(jnp.int32)


def draw_remap_count(key, part):
    drawn = jax.random.randint(jax.random.fold_in(key, 23), (NDEV, OB), (K + 1) // 2, K + 1).astype(jnp.int32)
    first_block = jnp.arange(OB)[None, :] == 0
    return jnp.where(first_block, K, drawn).reshape(NDEV * OB).astype(jnp.int32)


def draw_land_mask(key, part):
    drawn = jax.random.randint(jax.random.fold_in(key, 37), (OLAT, OLON), 0, 4 * OLAT).astype(jnp.int32)
    limit = OLAT + 3 * jnp.arange(OLAT, dtype=jnp.int32)[:, None]
    return (drawn < limit).astype(jnp.int32)


def block_levels(stream_key, shape, shards, low, high):
    def one(position, shards_of):
        heights = jax.random.uniform(jax.random.fold_in(jax.random.fold_in(stream_key, 6), position), (shards_of,), jnp.float32, low / len(shards), high / len(shards))
        return jnp.repeat(jnp.exp(heights), shape[position] // shards_of).reshape((-1,) + (1,) * (len(shape) - position - 1))

    loudness = one(*shards[0])
    for cut in shards[1:]:
        loudness = loudness * one(*cut)
    return loudness


def normal_values(own_key, shape, deviation, reach, pieces=(), held_as=jnp.bfloat16):
    entries = jax.random.normal(own_key, shape, jnp.float32) * deviation
    if len(pieces) > 0:
        entries = block_levels(own_key, shape, pieces, -0.22, 0.18) * entries
    return jnp.clip(entries, min=-reach, max=reach).astype(held_as)


def setup_inputs(seed: int = 0) -> dict:
    streams_of = jax.random.split(jax.random.key(seed), 9)
    return {
        "atm_state": normal_values(streams_of[0], (LEV, ALAT, ALON), 1.0, 6.0, ((1, 16), (2, 8)), jnp.float32),
        "atm_kappa": jnp.clip(jnp.exp(jax.random.uniform(streams_of[1], (LEV,), jnp.float32, math.log(0.05), math.log(0.24))), 0.05, 0.24),
        "vert_weight": normal_values(streams_of[2], (FC, LEV), LEV ** -0.5, 0.5, (), jnp.float32),
        "remap_src": draw_remap_src(jax.random.fold_in(streams_of[8], 71), 0),
        "remap_count": draw_remap_count(jax.random.fold_in(streams_of[8], 71), 0),
        "remap_weight": normal_values(streams_of[5], (OBG, K, BLK, BLK), (4.0 / (BLK * K) ** 0.5), 1.0, ((0, 128),)),
        "land_mask": draw_land_mask(jax.random.fold_in(streams_of[8], 71), 0),
        "ocean_term": jnp.clip(0.5 + 7.5 * jax.random.uniform(streams_of[7], (OLAT, OLON), jnp.float32) ** block_levels(streams_of[7], (OLAT, OLON), ((0, 16), (1, 8)), -0.2, 0.2), 0.5, 8.0),
    }


def diffuse_level(args):
    field, kappa = args
    for step in range(STEPS):
        padded = jnp.pad(field, 1)
        lap = padded[2:, 1:-1] + padded[:-2, 1:-1] + padded[1:-1, 2:] + padded[1:-1, :-2] - 4.0 * field
        field = field + kappa * lap
    return field


def ocean_operator(vector, maskf, ocean_term):
    padded = jnp.pad(maskf * vector, 1)
    beside = padded[2:, 1:-1] + padded[:-2, 1:-1] + padded[1:-1, 2:] + padded[1:-1, :-2]
    return maskf * ((4.0 + ocean_term) * vector - beside) + (1.0 - maskf) * vector


def remap_device(args):
    weights, sources = args
    return jnp.einsum("bkij,bkcj->bci", weights.astype(jnp.float32), sources.astype(jnp.float32), precision=lax.Precision.HIGHEST)


def reference(atm_state, atm_kappa, vert_weight, remap_src, remap_count, remap_weight, land_mask, ocean_term):
    atm_out = lax.map(diffuse_level, (atm_state, atm_kappa))
    flux = jnp.einsum("cl,lyx->cyx", vert_weight, atm_out, precision=lax.Precision.HIGHEST).astype(jnp.bfloat16)
    tiles = flux.reshape(FC, N_GY, AY, N_GX, AX).transpose(3, 1, 0, 2, 4)
    blocks = tiles.reshape(NDEV, FC, ABLK, BLK).transpose(0, 2, 1, 3).reshape(NDEV * ABLK, FC, BLK)
    live = (jnp.arange(K, dtype=jnp.int32)[None, :] < remap_count[:, None]).astype(jnp.bfloat16)
    sources = blocks[remap_src] * live[:, :, None, None]
    ocean_blocks = lax.map(remap_device, (remap_weight.reshape(NDEV, OB, K, BLK, BLK), sources.reshape(NDEV, OB, K, FC, BLK)))
    cells = ocean_blocks.transpose(0, 2, 1, 3).reshape(N_GX, N_GY, FC, OY, OX)
    ocean_flux = cells.transpose(2, 1, 3, 0, 4).reshape(FC, OLAT, OLON)
    maskf = land_mask.astype(jnp.float32)
    rhs = maskf * (ocean_flux[0] + ocean_flux[1])
    height = jnp.zeros_like(rhs)
    residual = rhs
    direction = rhs
    norm_now = jnp.sum(residual * residual)
    for step in range(ITERS):
        image = ocean_operator(direction, maskf, ocean_term)
        alpha = norm_now / jnp.sum(direction * image)
        height = height + alpha * direction
        residual = residual - alpha * image
        norm_next = jnp.sum(residual * residual)
        direction = residual + (norm_next / norm_now) * direction
        norm_now = norm_next
    return (atm_out, ocean_flux, height, residual)
```

```python
import jax
import jax.numpy as jnp
from jax import lax
from jax.sharding import PartitionSpec as P

STEPS = 4
ITERS = 3


def with_halo(x, sides, width):
    for axis, dim in sides:
        size, length = (lax.axis_size(axis), x.shape[dim])
        up = [(i, (i + 1) % size) for i in range(size - 1)]
        down = [(j, i) for i, j in up]
        last = lax.slice_in_dim(x, length - width, length, axis=dim)
        first = lax.slice_in_dim(x, 0, width, axis=dim)
        before = lax.ppermute(last, axis, up)
        after = lax.ppermute(first, axis, down)
        x = jnp.concatenate([before, x, after], axis=dim)
    return x


def shifted(x, axis, by):
    size = lax.axis_size(axis)
    return lax.ppermute(x, axis, [(i, (i + by) % size) for i in range(size)])


def ocean_operator(vector, maskf, ocean_term):
    padded = with_halo(maskf * vector, (("gx", 1), ("gy", 0)), 1)
    beside = padded[2:, 1:-1] + padded[:-2, 1:-1] + padded[1:-1, 2:] + padded[1:-1, :-2]
    return maskf * ((4.0 + ocean_term) * vector - beside) + (1.0 - maskf) * vector


def square_total(residual):
    return lax.psum(jnp.sum(residual * residual), ("gx", "gy"))


def whole_grid(tile):
    rows, cols = tile.shape
    count_gx = lax.axis_size("gx")
    count_gy = lax.axis_size("gy")
    stacked = lax.all_gather(tile, ("gy", "gx"), axis=0, tiled=False)
    stacked = stacked.reshape(count_gy, count_gx, rows, cols).transpose(0, 2, 1, 3)
    return stacked.reshape(count_gy * rows, count_gx * cols)


def grid_operator(vector, maskf, ocean_term):
    padded = jnp.pad(maskf * vector, 1)
    beside = padded[2:, 1:-1] + padded[:-2, 1:-1] + padded[1:-1, 2:] + padded[1:-1, :-2]
    return maskf * ((4.0 + ocean_term) * vector - beside) + (1.0 - maskf) * vector


def body(
    atm_state, atm_kappa, vert_weight, remap_src, remap_count, remap_weight, land_mask, ocean_term
):
    levels, tile_lat, tile_lon = atm_state.shape
    kappa = atm_kappa[:, None, None]
    count_gx = lax.axis_size("gx")
    count_gy = lax.axis_size("gy")
    field = atm_state
    for step in range(STEPS):
        padded = with_halo(field, (("gx", 2), ("gy", 1)), 1)
        lap = (
            padded[:, 2:, 1:-1]
            + padded[:, :-2, 1:-1]
            + padded[:, 1:-1, 2:]
            + padded[:, 1:-1, :-2]
            - 4.0 * field
        )
        field = field + kappa * lap
    flux = jnp.dot(
        vert_weight,
        field.reshape(levels, tile_lat * tile_lon),
        precision=lax.Precision.HIGHEST,
        preferred_element_type=jnp.float32,
    )
    ocean_blocks, lists, width, _ = remap_weight.shape
    comps = vert_weight.shape[0]
    own_blocks = tile_lat * tile_lon // width
    blocks = flux.astype(jnp.bfloat16).reshape(comps, own_blocks, width).transpose(1, 0, 2)
    devices = count_gx * count_gy
    gx_index = lax.axis_index("gx")
    gy_index = lax.axis_index("gy")
    me_index = gx_index * count_gy + gy_index
    east_index = (gx_index + 1) % count_gx * count_gy + gy_index
    west_index = (gx_index + count_gx - 1) % count_gx * count_gy + gy_index
    entries = ocean_blocks * lists
    slots = 2 * land_mask.shape[0]
    src_all = remap_src.reshape(devices, entries)
    live_all = (
        jnp.arange(lists, dtype=jnp.int32)[None, None, :]
        < remap_count.reshape(devices, ocean_blocks)[:, :, None]
    ).reshape(devices, entries)
    owner_all = src_all // own_blocks
    inside_all = src_all % own_blocks
    mine_owner = lax.dynamic_slice_in_dim(owner_all, me_index, 1, 0)[0]
    mine_inside = lax.dynamic_slice_in_dim(inside_all, me_index, 1, 0)[0]
    mine_live = lax.dynamic_slice_in_dim(live_all, me_index, 1, 0)[0]
    from_east = mine_live & (mine_owner == east_index)
    from_self = mine_live & (mine_owner == me_index)
    local_part = blocks[jnp.where(from_self, mine_inside, 0)]
    west_owner = lax.dynamic_slice_in_dim(owner_all, west_index, 1, 0)[0]
    west_inside = lax.dynamic_slice_in_dim(inside_all, west_index, 1, 0)[0]
    west_live = lax.dynamic_slice_in_dim(live_all, west_index, 1, 0)[0]
    wanted = (west_live & (west_owner == me_index)).astype(jnp.int32)
    wanted_rank = jnp.cumsum(wanted) - 1
    slot_ids = jnp.arange(slots, dtype=jnp.int32)
    picker = wanted[None, :] * (wanted_rank[None, :] == slot_ids[:, None]).astype(jnp.int32)
    send_index = jnp.sum(picker * west_inside[None, :], axis=1)
    send_valid = jnp.sum(picker, axis=1).astype(jnp.bfloat16)
    outgoing = blocks[send_index] * send_valid[:, None, None]
    incoming = shifted(outgoing, "gx", -1)
    east_int = from_east.astype(jnp.int32)
    east_rank = jnp.cumsum(east_int) - 1
    remote_part = incoming[jnp.where(from_east, east_rank, 0)]
    gathered = jnp.where(
        from_self[:, None, None],
        local_part,
        jnp.where(from_east[:, None, None], remote_part, jnp.zeros_like(local_part)),
    )
    gathered = gathered.reshape(ocean_blocks, lists, comps, width)
    ocean_rows, ocean_cols = land_mask.shape
    remapped = jnp.einsum(
        "bkij,bkcj->cbi", remap_weight, gathered, preferred_element_type=jnp.float32
    )
    ocean_flux = remapped.reshape(comps, ocean_rows, ocean_cols)
    coded = jnp.where(land_mask != 0, ocean_term, -1.0)
    coded_all = whole_grid(coded)
    maskf = (coded_all >= 0.0).astype(jnp.float32)
    rhs_tile = land_mask.astype(jnp.float32) * (ocean_flux[0] + ocean_flux[1])
    rhs = whole_grid(rhs_tile)
    height = jnp.zeros_like(rhs)
    residual = rhs
    direction = rhs
    norm_now = jnp.sum(residual * residual)
    for step in range(ITERS):
        image = grid_operator(direction, maskf, coded_all)
        alpha = norm_now / jnp.sum(direction * image)
        height = height + alpha * direction
        residual = residual - alpha * image
        norm_next = jnp.sum(residual * residual)
        direction = residual + norm_next / norm_now * direction
        norm_now = norm_next
    height = lax.dynamic_slice(height, (gy_index * ocean_rows, gx_index * ocean_cols), (ocean_rows, ocean_cols))
    residual = lax.dynamic_slice(residual, (gy_index * ocean_rows, gx_index * ocean_cols), (ocean_rows, ocean_cols))
    return (field, ocean_flux, height, residual)


def solution(mesh):
    return jax.shard_map(
        body,
        mesh=mesh,
        in_specs=(
            P(None, "gy", "gx"),
            P(),
            P(),
            P(),
            P(),
            P(("gx", "gy"), None, None, None),
            P("gy", "gx"),
            P("gy", "gx"),
        ),
        out_specs=(P(None, "gy", "gx"), P(None, "gy", "gx"), P("gy", "gx"), P("gy", "gx")),
        check_vma=False,
    )
```

```python
import jax
import jax.numpy as jnp
from jax import lax
from jax.sharding import PartitionSpec as P

STEPS = 4
ITERS = 3


def with_halo(x, sides, width):
    for axis, dim in sides:
        size, length = (lax.axis_size(axis), x.shape[dim])
        up = [(i, (i + 1) % size) for i in range(size - 1)]
        down = [(j, i) for i, j in up]
        last = lax.slice_in_dim(x, length - width, length, axis=dim)
        first = lax.slice_in_dim(x, 0, width, axis=dim)
        before = lax.ppermute(last, axis, up)
        after = lax.ppermute(first, axis, down)
        x = jnp.concatenate([before, x, after], axis=dim)
    return x


def shifted(x, axis, by):
    size = lax.axis_size(axis)
    return lax.ppermute(x, axis, [(i, (i + by) % size) for i in range(size)])


def ocean_operator(vector, maskf, ocean_term):
    padded = with_halo(maskf * vector, (("gx", 1), ("gy", 0)), 1)
    beside = padded[2:, 1:-1] + padded[:-2, 1:-1] + padded[1:-1, 2:] + padded[1:-1, :-2]
    return maskf * ((4.0 + ocean_term) * vector - beside) + (1.0 - maskf) * vector


def square_total(residual):
    return lax.psum(jnp.sum(residual * residual), ("gx", "gy"))


def doubling_gather(x, axis, dim):
    size = lax.axis_size(axis)
    index = lax.axis_index(axis)
    distance = 1
    while distance < size:
        other = lax.ppermute(x, axis, [(j, j ^ distance) for j in range(size)])
        low = jnp.concatenate([x, other], axis=dim)
        high = jnp.concatenate([other, x], axis=dim)
        x = jnp.where((index & distance) == 0, low, high)
        distance *= 2
    return x


def whole_grid(tile):
    return doubling_gather(doubling_gather(tile, "gx", 1), "gy", 0)


def grid_operator(vector, maskf, ocean_term):
    padded = jnp.pad(maskf * vector, 1)
    beside = padded[2:, 1:-1] + padded[:-2, 1:-1] + padded[1:-1, 2:] + padded[1:-1, :-2]
    return maskf * ((4.0 + ocean_term) * vector - beside) + (1.0 - maskf) * vector


def body(
    atm_state, atm_kappa, vert_weight, remap_src, remap_count, remap_weight, land_mask, ocean_term
):
    levels, tile_lat, tile_lon = atm_state.shape
    kappa = atm_kappa[:, None, None]
    count_gx = lax.axis_size("gx")
    count_gy = lax.axis_size("gy")
    coded_all = whole_grid(jnp.where(land_mask != 0, ocean_term, -1.0))
    maskf = (coded_all >= 0.0).astype(jnp.float32)
    field = atm_state
    for step in range(STEPS):
        padded = with_halo(field, (("gx", 2), ("gy", 1)), 1)
        lap = (
            padded[:, 2:, 1:-1]
            + padded[:, :-2, 1:-1]
            + padded[:, 1:-1, 2:]
            + padded[:, 1:-1, :-2]
            - 4.0 * field
        )
        field = field + kappa * lap
    flux = jnp.dot(
        vert_weight,
        field.reshape(levels, tile_lat * tile_lon),
        precision=lax.Precision.HIGHEST,
        preferred_element_type=jnp.float32,
    )
    ocean_blocks, lists, width, _ = remap_weight.shape
    comps = vert_weight.shape[0]
    own_blocks = tile_lat * tile_lon // width
    blocks = flux.astype(jnp.bfloat16).reshape(comps, own_blocks, width).transpose(1, 0, 2)
    devices = count_gx * count_gy
    gx_index = lax.axis_index("gx")
    gy_index = lax.axis_index("gy")
    me_index = gx_index * count_gy + gy_index
    east_index = (gx_index + 1) % count_gx * count_gy + gy_index
    west_index = (gx_index + count_gx - 1) % count_gx * count_gy + gy_index
    entries = ocean_blocks * lists
    slots = 2 * land_mask.shape[0]
    src_all = remap_src.reshape(devices, entries)
    live_all = (
        jnp.arange(lists, dtype=jnp.int32)[None, None, :]
        < remap_count.reshape(devices, ocean_blocks)[:, :, None]
    ).reshape(devices, entries)
    owner_all = src_all // own_blocks
    inside_all = src_all % own_blocks
    mine_owner = lax.dynamic_slice_in_dim(owner_all, me_index, 1, 0)[0]
    mine_inside = lax.dynamic_slice_in_dim(inside_all, me_index, 1, 0)[0]
    mine_live = lax.dynamic_slice_in_dim(live_all, me_index, 1, 0)[0]
    from_east = mine_live & (mine_owner == east_index)
    from_self = mine_live & (mine_owner == me_index)
    local_part = blocks[jnp.where(from_self, mine_inside, 0)]
    west_owner = lax.dynamic_slice_in_dim(owner_all, west_index, 1, 0)[0]
    west_inside = lax.dynamic_slice_in_dim(inside_all, west_index, 1, 0)[0]
    west_live = lax.dynamic_slice_in_dim(live_all, west_index, 1, 0)[0]
    wanted = (west_live & (west_owner == me_index)).astype(jnp.int32)
    wanted_rank = jnp.cumsum(wanted) - 1
    slot_ids = jnp.arange(slots, dtype=jnp.int32)
    picker = wanted[None, :] * (wanted_rank[None, :] == slot_ids[:, None]).astype(jnp.int32)
    send_index = jnp.sum(picker * west_inside[None, :], axis=1)
    send_valid = jnp.sum(picker, axis=1).astype(jnp.bfloat16)
    outgoing = blocks[send_index] * send_valid[:, None, None]
    incoming = shifted(outgoing, "gx", -1)
    east_int = from_east.astype(jnp.int32)
    east_rank = jnp.cumsum(east_int) - 1
    remote_part = incoming[jnp.where(from_east, east_rank, 0)]
    gathered = jnp.where(
        from_self[:, None, None],
        local_part,
        jnp.where(from_east[:, None, None], remote_part, jnp.zeros_like(local_part)),
    )
    gathered = gathered.reshape(ocean_blocks, lists, comps, width)
    ocean_rows, ocean_cols = land_mask.shape
    remapped = jnp.einsum(
        "bkij,bkcj->cbi", remap_weight, gathered, preferred_element_type=jnp.float32
    )
    ocean_flux = remapped.reshape(comps, ocean_rows, ocean_cols)
    rhs_tile = land_mask.astype(jnp.float32) * (ocean_flux[0] + ocean_flux[1])
    rhs = whole_grid(rhs_tile)
    height = jnp.zeros_like(rhs)
    residual = rhs
    direction = rhs
    norm_now = jnp.sum(residual * residual)
    for step in range(ITERS):
        image = grid_operator(direction, maskf, coded_all)
        alpha = norm_now / jnp.sum(direction * image)
        height = height + alpha * direction
        residual = residual - alpha * image
        norm_next = jnp.sum(residual * residual)
        direction = residual + norm_next / norm_now * direction
        norm_now = norm_next
    height = lax.dynamic_slice(height, (gy_index * ocean_rows, gx_index * ocean_cols), (ocean_rows, ocean_cols))
    residual = lax.dynamic_slice(residual, (gy_index * ocean_rows, gx_index * ocean_cols), (ocean_rows, ocean_cols))
    return (field, ocean_flux, height, residual)


def solution(mesh):
    return jax.shard_map(
        body,
        mesh=mesh,
        in_specs=(
            P(None, "gy", "gx"),
            P(),
            P(),
            P(),
            P(),
            P(("gx", "gy"), None, None, None),
            P("gy", "gx"),
            P("gy", "gx"),
        ),
        out_specs=(P(None, "gy", "gx"), P(None, "gy", "gx"), P("gy", "gx"), P("gy", "gx")),
        check_vma=False,
    )
```

```python
import jax
import jax.numpy as jnp
from jax import lax
from jax.sharding import PartitionSpec as P
from jax.experimental import pallas as pl
from jax.experimental.pallas import tpu as pltpu

STEPS = 4
ITERS = 3


def with_halo(x, sides, width):
    for axis, dim in sides:
        size, length = (lax.axis_size(axis), x.shape[dim])
        up = [(i, (i + 1) % size) for i in range(size - 1)]
        down = [(j, i) for i, j in up]
        last = lax.slice_in_dim(x, length - width, length, axis=dim)
        first = lax.slice_in_dim(x, 0, width, axis=dim)
        before = lax.ppermute(last, axis, up)
        after = lax.ppermute(first, axis, down)
        x = jnp.concatenate([before, x, after], axis=dim)
    return x


def shifted(x, axis, by):
    size = lax.axis_size(axis)
    return lax.ppermute(x, axis, [(i, (i + by) % size) for i in range(size)])


def ocean_operator(vector, maskf, ocean_term):
    padded = with_halo(maskf * vector, (("gx", 1), ("gy", 0)), 1)
    beside = padded[2:, 1:-1] + padded[:-2, 1:-1] + padded[1:-1, 2:] + padded[1:-1, :-2]
    return maskf * ((4.0 + ocean_term) * vector - beside) + (1.0 - maskf) * vector


def square_total(residual):
    return lax.psum(jnp.sum(residual * residual), ("gx", "gy"))


def doubling_gather(x, axis, dim):
    size = lax.axis_size(axis)
    index = lax.axis_index(axis)
    distance = 1
    while distance < size:
        other = lax.ppermute(x, axis, [(j, j ^ distance) for j in range(size)])
        low = jnp.concatenate([x, other], axis=dim)
        high = jnp.concatenate([other, x], axis=dim)
        x = jnp.where((index & distance) == 0, low, high)
        distance *= 2
    return x


def whole_grid(tile):
    return doubling_gather(doubling_gather(tile, "gx", 1), "gy", 0)


def grid_operator(vector, maskf, ocean_term):
    padded = jnp.pad(maskf * vector, 1)
    beside = padded[2:, 1:-1] + padded[:-2, 1:-1] + padded[1:-1, 2:] + padded[1:-1, :-2]
    return maskf * ((4.0 + ocean_term) * vector - beside) + (1.0 - maskf) * vector


HALO = 4
LEVEL_BLOCK = 8


def diffusion_kernel(kappa_ref, weight_ref, core_ref, lanes_ref, rows_ref, mask_ref, out_ref, flux_ref):
    block = pl.program_id(0)
    levels, rows, cols = core_ref.shape

    @pl.when(block == 0)
    def _():
        flux_ref[...] = jnp.zeros_like(flux_ref)

    mask = mask_ref[...]

    def level(l, carry):
        lev = block * levels + l
        kappa = kappa_ref[lev]
        top = jnp.concatenate([core_ref[l], lanes_ref[l]], axis=1)
        f = jnp.concatenate([top, rows_ref[l]], axis=0)
        height, width = f.shape
        for step in range(STEPS):
            beside = (
                pltpu.roll(f, height - 1, 0)
                + pltpu.roll(f, 1, 0)
                + pltpu.roll(f, width - 1, 1)
                + pltpu.roll(f, 1, 1)
            )
            f = (f + kappa * (beside - 4.0 * f)) * mask
        core = f[:rows, :cols]
        out_ref[l] = core
        for c in range(flux_ref.shape[0]):
            flux_ref[c] += weight_ref[c, lev] * core
        return carry

    lax.fori_loop(0, levels, level, 0)


def diffuse(field, atm_kappa, vert_weight):
    levels, rows, cols = field.shape
    comps = vert_weight.shape[0]
    count_gx = lax.axis_size("gx")
    count_gy = lax.axis_size("gy")
    gx_index = lax.axis_index("gx")
    gy_index = lax.axis_index("gy")
    up_gx = [(i, i + 1) for i in range(count_gx - 1)]
    down_gx = [(i + 1, i) for i in range(count_gx - 1)]
    up_gy = [(i, i + 1) for i in range(count_gy - 1)]
    down_gy = [(i + 1, i) for i in range(count_gy - 1)]
    east = lax.ppermute(field[:, :, :HALO], "gx", down_gx)
    west = lax.ppermute(field[:, :, cols - HALO :], "gx", up_gx)
    gap = jnp.zeros((levels, rows, 128 - 2 * HALO), field.dtype)
    lanes = jnp.concatenate([east, gap, west], axis=2)
    first = jnp.concatenate([field[:, :HALO, :], lanes[:, :HALO, :]], axis=2)
    last = jnp.concatenate([field[:, rows - HALO :, :], lanes[:, rows - HALO :, :]], axis=2)
    south = lax.ppermute(first, "gy", down_gy)
    north = lax.ppermute(last, "gy", up_gy)
    halo_rows = jnp.concatenate([south, north], axis=1)
    height = rows + 2 * HALO
    width = cols + 128
    r = jnp.arange(height, dtype=jnp.int32)
    c = jnp.arange(width, dtype=jnp.int32)
    global_r = gy_index * rows + jnp.where(r < rows + HALO, r, r - height)
    global_c = gx_index * cols + jnp.where(c < cols + HALO, c, c - width)
    inside_r = (global_r >= 0) & (global_r < count_gy * rows)
    inside_c = (global_c >= 0) & (global_c < count_gx * cols) & ((c < cols + HALO) | (c >= width - HALO))
    mask = (inside_r[:, None] & inside_c[None, :]).astype(jnp.float32)
    blocks = levels // LEVEL_BLOCK
    smem = pl.BlockSpec(memory_space=pltpu.SMEM)
    out, flux = pl.pallas_call(
        diffusion_kernel,
        grid=(blocks,),
        in_specs=[
            smem,
            smem,
            pl.BlockSpec((LEVEL_BLOCK, rows, cols), lambda b: (b, 0, 0)),
            pl.BlockSpec((LEVEL_BLOCK, rows, 128), lambda b: (b, 0, 0)),
            pl.BlockSpec((LEVEL_BLOCK, 2 * HALO, width), lambda b: (b, 0, 0)),
            pl.BlockSpec((height, width), lambda b: (0, 0)),
        ],
        out_specs=[
            pl.BlockSpec((LEVEL_BLOCK, rows, cols), lambda b: (b, 0, 0)),
            pl.BlockSpec((comps, rows, cols), lambda b: (0, 0, 0)),
        ],
        out_shape=[
            jax.ShapeDtypeStruct(field.shape, field.dtype),
            jax.ShapeDtypeStruct((comps, rows, cols), jnp.float32),
        ],
        compiler_params=pltpu.CompilerParams(dimension_semantics=("arbitrary",)),
    )(atm_kappa, vert_weight, field, lanes, halo_rows, mask)
    return out, flux


def body(
    atm_state, atm_kappa, vert_weight, remap_src, remap_count, remap_weight, land_mask, ocean_term
):
    levels, tile_lat, tile_lon = atm_state.shape
    kappa = atm_kappa[:, None, None]
    count_gx = lax.axis_size("gx")
    count_gy = lax.axis_size("gy")
    coded_all = whole_grid(jnp.where(land_mask != 0, ocean_term, -1.0))
    maskf = (coded_all >= 0.0).astype(jnp.float32)
    field, flux = diffuse(atm_state, atm_kappa, vert_weight)
    flux = flux.reshape(flux.shape[0], tile_lat * tile_lon)
    ocean_blocks, lists, width, _ = remap_weight.shape
    comps = vert_weight.shape[0]
    own_blocks = tile_lat * tile_lon // width
    blocks = flux.astype(jnp.bfloat16).reshape(comps, own_blocks, width).transpose(1, 0, 2)
    devices = count_gx * count_gy
    gx_index = lax.axis_index("gx")
    gy_index = lax.axis_index("gy")
    me_index = gx_index * count_gy + gy_index
    east_index = (gx_index + 1) % count_gx * count_gy + gy_index
    west_index = (gx_index + count_gx - 1) % count_gx * count_gy + gy_index
    entries = ocean_blocks * lists
    slots = 2 * land_mask.shape[0]
    src_all = remap_src.reshape(devices, entries)
    live_all = (
        jnp.arange(lists, dtype=jnp.int32)[None, None, :]
        < remap_count.reshape(devices, ocean_blocks)[:, :, None]
    ).reshape(devices, entries)
    owner_all = src_all // own_blocks
    inside_all = src_all % own_blocks
    mine_owner = lax.dynamic_slice_in_dim(owner_all, me_index, 1, 0)[0]
    mine_inside = lax.dynamic_slice_in_dim(inside_all, me_index, 1, 0)[0]
    mine_live = lax.dynamic_slice_in_dim(live_all, me_index, 1, 0)[0]
    from_east = mine_live & (mine_owner == east_index)
    from_self = mine_live & (mine_owner == me_index)
    local_part = blocks[jnp.where(from_self, mine_inside, 0)]
    west_owner = lax.dynamic_slice_in_dim(owner_all, west_index, 1, 0)[0]
    west_inside = lax.dynamic_slice_in_dim(inside_all, west_index, 1, 0)[0]
    west_live = lax.dynamic_slice_in_dim(live_all, west_index, 1, 0)[0]
    wanted = (west_live & (west_owner == me_index)).astype(jnp.int32)
    wanted_rank = jnp.cumsum(wanted) - 1
    slot_ids = jnp.arange(slots, dtype=jnp.int32)
    picker = wanted[None, :] * (wanted_rank[None, :] == slot_ids[:, None]).astype(jnp.int32)
    send_index = jnp.sum(picker * west_inside[None, :], axis=1)
    send_valid = jnp.sum(picker, axis=1).astype(jnp.bfloat16)
    outgoing = blocks[send_index] * send_valid[:, None, None]
    incoming = shifted(outgoing, "gx", -1)
    east_int = from_east.astype(jnp.int32)
    east_rank = jnp.cumsum(east_int) - 1
    remote_part = incoming[jnp.where(from_east, east_rank, 0)]
    gathered = jnp.where(
        from_self[:, None, None],
        local_part,
        jnp.where(from_east[:, None, None], remote_part, jnp.zeros_like(local_part)),
    )
    gathered = gathered.reshape(ocean_blocks, lists, comps, width)
    ocean_rows, ocean_cols = land_mask.shape
    remapped = jnp.einsum(
        "bkij,bkcj->cbi", remap_weight, gathered, preferred_element_type=jnp.float32
    )
    ocean_flux = remapped.reshape(comps, ocean_rows, ocean_cols)
    rhs_tile = land_mask.astype(jnp.float32) * (ocean_flux[0] + ocean_flux[1])
    rhs = whole_grid(rhs_tile)
    height = jnp.zeros_like(rhs)
    residual = rhs
    direction = rhs
    norm_now = jnp.sum(residual * residual)
    for step in range(ITERS):
        image = grid_operator(direction, maskf, coded_all)
        alpha = norm_now / jnp.sum(direction * image)
        height = height + alpha * direction
        residual = residual - alpha * image
        norm_next = jnp.sum(residual * residual)
        direction = residual + norm_next / norm_now * direction
        norm_now = norm_next
    height = lax.dynamic_slice(height, (gy_index * ocean_rows, gx_index * ocean_cols), (ocean_rows, ocean_cols))
    residual = lax.dynamic_slice(residual, (gy_index * ocean_rows, gx_index * ocean_cols), (ocean_rows, ocean_cols))
    return (field, ocean_flux, height, residual)


def solution(mesh):
    return jax.shard_map(
        body,
        mesh=mesh,
        in_specs=(
            P(None, "gy", "gx"),
            P(),
            P(),
            P(),
            P(),
            P(("gx", "gy"), None, None, None),
            P("gy", "gx"),
            P("gy", "gx"),
        ),
        out_specs=(P(None, "gy", "gx"), P(None, "gy", "gx"), P("gy", "gx"), P("gy", "gx")),
        check_vma=False,
    )
```

```python
import jax
import jax.numpy as jnp
from jax import lax
from jax.sharding import PartitionSpec as P
from jax.experimental import pallas as pl
from jax.experimental.pallas import tpu as pltpu

STEPS = 4
ITERS = 3


def with_halo(x, sides, width):
    for axis, dim in sides:
        size, length = (lax.axis_size(axis), x.shape[dim])
        up = [(i, (i + 1) % size) for i in range(size - 1)]
        down = [(j, i) for i, j in up]
        last = lax.slice_in_dim(x, length - width, length, axis=dim)
        first = lax.slice_in_dim(x, 0, width, axis=dim)
        before = lax.ppermute(last, axis, up)
        after = lax.ppermute(first, axis, down)
        x = jnp.concatenate([before, x, after], axis=dim)
    return x


def shifted(x, axis, by):
    size = lax.axis_size(axis)
    return lax.ppermute(x, axis, [(i, (i + by) % size) for i in range(size)])


def ocean_operator(vector, maskf, ocean_term):
    padded = with_halo(maskf * vector, (("gx", 1), ("gy", 0)), 1)
    beside = padded[2:, 1:-1] + padded[:-2, 1:-1] + padded[1:-1, 2:] + padded[1:-1, :-2]
    return maskf * ((4.0 + ocean_term) * vector - beside) + (1.0 - maskf) * vector


def square_total(residual):
    return lax.psum(jnp.sum(residual * residual), ("gx", "gy"))


def gather_rounds():
    rounds = []
    for axis, bits in (("gy", lax.axis_size("gy")), ("gx", lax.axis_size("gx"))):
        distances = []
        d = 1
        while d < bits:
            distances.append(d)
            d *= 2
        rounds.append([(axis, d) for d in distances])
    gy_rounds, gx_rounds = rounds
    far = gy_rounds[1::2] + gx_rounds[2:]
    near = gy_rounds[0::2] + gx_rounds[1:2] + gx_rounds[:1]
    return far + near


def whole_grid(tile):
    rows, cols = tile.shape
    rounds = gather_rounds()
    x = tile[None]
    for axis, distance in rounds:
        size = lax.axis_size(axis)
        index = lax.axis_index(axis)
        other = lax.ppermute(x, axis, [(j, j ^ distance) for j in range(size)])
        low = jnp.concatenate([x, other], axis=0)
        high = jnp.concatenate([other, x], axis=0)
        x = jnp.where((index & distance) == 0, low, high)
    count = len(rounds)
    x = x.reshape((2,) * count + (rows, cols))
    order = []
    for axis in ("gy", "gx"):
        d = lax.axis_size(axis) // 2
        while d >= 1:
            order.append(count - 1 - rounds.index((axis, d)))
            d //= 2
    x = x.transpose(order + [count, count + 1])
    count_gy = lax.axis_size("gy")
    count_gx = lax.axis_size("gx")
    x = x.reshape(count_gy, count_gx, rows, cols).transpose(0, 2, 1, 3)
    return x.reshape(count_gy * rows, count_gx * cols)


def grid_operator(vector, maskf, ocean_term):
    padded = jnp.pad(maskf * vector, 1)
    beside = padded[2:, 1:-1] + padded[:-2, 1:-1] + padded[1:-1, 2:] + padded[1:-1, :-2]
    return maskf * ((4.0 + ocean_term) * vector - beside) + (1.0 - maskf) * vector


HALO = 4
LEVEL_BLOCK = 8


def diffusion_kernel(kappa_ref, weight_ref, core_ref, lanes_ref, rows_ref, mask_ref, out_ref, flux_ref):
    block = pl.program_id(0)
    levels, rows, cols = core_ref.shape

    @pl.when(block == 0)
    def _():
        flux_ref[...] = jnp.zeros_like(flux_ref)

    mask = mask_ref[...]

    def level(l, carry):
        lev = block * levels + l
        kappa = kappa_ref[lev]
        top = jnp.concatenate([core_ref[l], lanes_ref[l]], axis=1)
        f = jnp.concatenate([top, rows_ref[l]], axis=0)
        height, width = f.shape
        for step in range(STEPS):
            beside = (
                pltpu.roll(f, height - 1, 0)
                + pltpu.roll(f, 1, 0)
                + pltpu.roll(f, width - 1, 1)
                + pltpu.roll(f, 1, 1)
            )
            f = (f + kappa * (beside - 4.0 * f)) * mask
        core = f[:rows, :cols]
        out_ref[l] = core
        for c in range(flux_ref.shape[0]):
            flux_ref[c] += weight_ref[c, lev] * core
        return carry

    lax.fori_loop(0, levels, level, 0)


def diffuse(field, atm_kappa, vert_weight):
    levels, rows, cols = field.shape
    comps = vert_weight.shape[0]
    count_gx = lax.axis_size("gx")
    count_gy = lax.axis_size("gy")
    gx_index = lax.axis_index("gx")
    gy_index = lax.axis_index("gy")
    up_gx = [(i, i + 1) for i in range(count_gx - 1)]
    down_gx = [(i + 1, i) for i in range(count_gx - 1)]
    up_gy = [(i, i + 1) for i in range(count_gy - 1)]
    down_gy = [(i + 1, i) for i in range(count_gy - 1)]
    east = lax.ppermute(field[:, :, :HALO], "gx", down_gx)
    west = lax.ppermute(field[:, :, cols - HALO :], "gx", up_gx)
    gap = jnp.zeros((levels, rows, 128 - 2 * HALO), field.dtype)
    lanes = jnp.concatenate([east, gap, west], axis=2)
    first = jnp.concatenate([field[:, :HALO, :], lanes[:, :HALO, :]], axis=2)
    last = jnp.concatenate([field[:, rows - HALO :, :], lanes[:, rows - HALO :, :]], axis=2)
    south = lax.ppermute(first, "gy", down_gy)
    north = lax.ppermute(last, "gy", up_gy)
    halo_rows = jnp.concatenate([south, north], axis=1)
    height = rows + 2 * HALO
    width = cols + 128
    r = jnp.arange(height, dtype=jnp.int32)
    c = jnp.arange(width, dtype=jnp.int32)
    global_r = gy_index * rows + jnp.where(r < rows + HALO, r, r - height)
    global_c = gx_index * cols + jnp.where(c < cols + HALO, c, c - width)
    inside_r = (global_r >= 0) & (global_r < count_gy * rows)
    inside_c = (global_c >= 0) & (global_c < count_gx * cols) & ((c < cols + HALO) | (c >= width - HALO))
    mask = (inside_r[:, None] & inside_c[None, :]).astype(jnp.float32)
    blocks = levels // LEVEL_BLOCK
    smem = pl.BlockSpec(memory_space=pltpu.SMEM)
    out, flux = pl.pallas_call(
        diffusion_kernel,
        grid=(blocks,),
        in_specs=[
            smem,
            smem,
            pl.BlockSpec((LEVEL_BLOCK, rows, cols), lambda b: (b, 0, 0)),
            pl.BlockSpec((LEVEL_BLOCK, rows, 128), lambda b: (b, 0, 0)),
            pl.BlockSpec((LEVEL_BLOCK, 2 * HALO, width), lambda b: (b, 0, 0)),
            pl.BlockSpec((height, width), lambda b: (0, 0)),
        ],
        out_specs=[
            pl.BlockSpec((LEVEL_BLOCK, rows, cols), lambda b: (b, 0, 0)),
            pl.BlockSpec((comps, rows, cols), lambda b: (0, 0, 0)),
        ],
        out_shape=[
            jax.ShapeDtypeStruct(field.shape, field.dtype),
            jax.ShapeDtypeStruct((comps, rows, cols), jnp.float32),
        ],
        compiler_params=pltpu.CompilerParams(dimension_semantics=("arbitrary",)),
        cost_estimate=pl.CostEstimate(
            flops=levels * height * width * STEPS * 10,
            transcendentals=0,
            bytes_accessed=2 * field.size * 4,
        ),
    )(atm_kappa, vert_weight, field, lanes, halo_rows, mask)
    return out, flux


def body(
    atm_state, atm_kappa, vert_weight, remap_src, remap_count, remap_weight, land_mask, ocean_term
):
    levels, tile_lat, tile_lon = atm_state.shape
    kappa = atm_kappa[:, None, None]
    count_gx = lax.axis_size("gx")
    count_gy = lax.axis_size("gy")
    coded_all = whole_grid(jnp.where(land_mask != 0, ocean_term, -1.0))
    maskf = (coded_all >= 0.0).astype(jnp.float32)
    field, flux = diffuse(atm_state, atm_kappa, vert_weight)
    flux = flux.reshape(flux.shape[0], tile_lat * tile_lon)
    ocean_blocks, lists, width, _ = remap_weight.shape
    comps = vert_weight.shape[0]
    own_blocks = tile_lat * tile_lon // width
    blocks = flux.astype(jnp.bfloat16).reshape(comps, own_blocks, width).transpose(1, 0, 2)
    devices = count_gx * count_gy
    gx_index = lax.axis_index("gx")
    gy_index = lax.axis_index("gy")
    me_index = gx_index * count_gy + gy_index
    east_index = (gx_index + 1) % count_gx * count_gy + gy_index
    west_index = (gx_index + count_gx - 1) % count_gx * count_gy + gy_index
    entries = ocean_blocks * lists
    slots = 2 * land_mask.shape[0]
    src_all = remap_src.reshape(devices, entries)
    live_all = (
        jnp.arange(lists, dtype=jnp.int32)[None, None, :]
        < remap_count.reshape(devices, ocean_blocks)[:, :, None]
    ).reshape(devices, entries)
    owner_all = src_all // own_blocks
    inside_all = src_all % own_blocks
    mine_owner = lax.dynamic_slice_in_dim(owner_all, me_index, 1, 0)[0]
    mine_inside = lax.dynamic_slice_in_dim(inside_all, me_index, 1, 0)[0]
    mine_live = lax.dynamic_slice_in_dim(live_all, me_index, 1, 0)[0]
    from_east = mine_live & (mine_owner == east_index)
    from_self = mine_live & (mine_owner == me_index)
    local_part = blocks[jnp.where(from_self, mine_inside, 0)]
    west_owner = lax.dynamic_slice_in_dim(owner_all, west_index, 1, 0)[0]
    west_inside = lax.dynamic_slice_in_dim(inside_all, west_index, 1, 0)[0]
    west_live = lax.dynamic_slice_in_dim(live_all, west_index, 1, 0)[0]
    wanted = (west_live & (west_owner == me_index)).astype(jnp.int32)
    wanted_rank = jnp.cumsum(wanted) - 1
    slot_ids = jnp.arange(slots, dtype=jnp.int32)
    picker = wanted[None, :] * (wanted_rank[None, :] == slot_ids[:, None]).astype(jnp.int32)
    send_index = jnp.sum(picker * west_inside[None, :], axis=1)
    send_valid = jnp.sum(picker, axis=1).astype(jnp.bfloat16)
    outgoing = blocks[send_index] * send_valid[:, None, None]
    incoming = shifted(outgoing, "gx", -1)
    east_int = from_east.astype(jnp.int32)
    east_rank = jnp.cumsum(east_int) - 1
    remote_part = incoming[jnp.where(from_east, east_rank, 0)]
    gathered = jnp.where(
        from_self[:, None, None],
        local_part,
        jnp.where(from_east[:, None, None], remote_part, jnp.zeros_like(local_part)),
    )
    gathered = gathered.reshape(ocean_blocks, lists, comps, width)
    ocean_rows, ocean_cols = land_mask.shape
    remapped = jnp.einsum(
        "bkij,bkcj->cbi", remap_weight, gathered, preferred_element_type=jnp.float32
    )
    ocean_flux = remapped.reshape(comps, ocean_rows, ocean_cols)
    rhs_tile = land_mask.astype(jnp.float32) * (ocean_flux[0] + ocean_flux[1])
    rhs = whole_grid(rhs_tile)
    height = jnp.zeros_like(rhs)
    residual = rhs
    direction = rhs
    norm_now = jnp.sum(residual * residual)
    for step in range(ITERS):
        image = grid_operator(direction, maskf, coded_all)
        alpha = norm_now / jnp.sum(direction * image)
        height = height + alpha * direction
        residual = residual - alpha * image
        norm_next = jnp.sum(residual * residual)
        direction = residual + norm_next / norm_now * direction
        norm_now = norm_next
    height = lax.dynamic_slice(height, (gy_index * ocean_rows, gx_index * ocean_cols), (ocean_rows, ocean_cols))
    residual = lax.dynamic_slice(residual, (gy_index * ocean_rows, gx_index * ocean_cols), (ocean_rows, ocean_cols))
    return (field, ocean_flux, height, residual)


def solution(mesh):
    return jax.shard_map(
        body,
        mesh=mesh,
        in_specs=(
            P(None, "gy", "gx"),
            P(),
            P(),
            P(),
            P(),
            P(("gx", "gy"), None, None, None),
            P("gy", "gx"),
            P("gy", "gx"),
        ),
        out_specs=(P(None, "gy", "gx"), P(None, "gy", "gx"), P("gy", "gx"), P("gy", "gx")),
        check_vma=False,
    )
```

```python
import jax
import jax.numpy as jnp
from jax import lax
from jax.sharding import PartitionSpec as P
from jax.experimental import pallas as pl
from jax.experimental.pallas import tpu as pltpu

STEPS = 4
ITERS = 3


def with_halo(x, sides, width):
    for axis, dim in sides:
        size, length = (lax.axis_size(axis), x.shape[dim])
        up = [(i, (i + 1) % size) for i in range(size - 1)]
        down = [(j, i) for i, j in up]
        last = lax.slice_in_dim(x, length - width, length, axis=dim)
        first = lax.slice_in_dim(x, 0, width, axis=dim)
        before = lax.ppermute(last, axis, up)
        after = lax.ppermute(first, axis, down)
        x = jnp.concatenate([before, x, after], axis=dim)
    return x


def shifted(x, axis, by):
    size = lax.axis_size(axis)
    return lax.ppermute(x, axis, [(i, (i + by) % size) for i in range(size)])


def ocean_operator(vector, maskf, ocean_term):
    padded = with_halo(maskf * vector, (("gx", 1), ("gy", 0)), 1)
    beside = padded[2:, 1:-1] + padded[:-2, 1:-1] + padded[1:-1, 2:] + padded[1:-1, :-2]
    return maskf * ((4.0 + ocean_term) * vector - beside) + (1.0 - maskf) * vector


def square_total(residual):
    return lax.psum(jnp.sum(residual * residual), ("gx", "gy"))


def gather_rounds():
    rounds = []
    for axis, bits in (("gy", lax.axis_size("gy")), ("gx", lax.axis_size("gx"))):
        distances = []
        d = 1
        while d < bits:
            distances.append(d)
            d *= 2
        rounds.append([(axis, d) for d in distances])
    gy_rounds, gx_rounds = rounds
    far = gy_rounds[1::2] + gx_rounds[2:]
    near = gy_rounds[0::2] + gx_rounds[1:2] + gx_rounds[:1]
    return far + near


def whole_grid(tile):
    rows, cols = tile.shape
    rounds = gather_rounds()
    x = tile[None]
    for axis, distance in rounds:
        size = lax.axis_size(axis)
        index = lax.axis_index(axis)
        other = lax.ppermute(x, axis, [(j, j ^ distance) for j in range(size)])
        low = jnp.concatenate([x, other], axis=0)
        high = jnp.concatenate([other, x], axis=0)
        x = jnp.where((index & distance) == 0, low, high)
    count = len(rounds)
    x = x.reshape((2,) * count + (rows, cols))
    order = []
    for axis in ("gy", "gx"):
        d = lax.axis_size(axis) // 2
        while d >= 1:
            order.append(count - 1 - rounds.index((axis, d)))
            d //= 2
    x = x.transpose(order + [count, count + 1])
    count_gy = lax.axis_size("gy")
    count_gx = lax.axis_size("gx")
    x = x.reshape(count_gy, count_gx, rows, cols).transpose(0, 2, 1, 3)
    return x.reshape(count_gy * rows, count_gx * cols)


def grid_operator(vector, maskf, ocean_term):
    padded = jnp.pad(maskf * vector, 1)
    beside = padded[2:, 1:-1] + padded[:-2, 1:-1] + padded[1:-1, 2:] + padded[1:-1, :-2]
    return maskf * ((4.0 + ocean_term) * vector - beside) + (1.0 - maskf) * vector


HALO = 4
LEVEL_BLOCK = 8


def diffusion_kernel(kappa_ref, weight_ref, core_ref, lanes_ref, rows_ref, mask_ref, out_ref, flux_ref):
    block = pl.program_id(0)
    levels, rows, cols = core_ref.shape

    @pl.when(block == 0)
    def _():
        flux_ref[...] = jnp.zeros_like(flux_ref)

    mask = mask_ref[...]

    def level(l, carry):
        lev = block * levels + l
        kappa = kappa_ref[lev]
        top = jnp.concatenate([core_ref[l], lanes_ref[l]], axis=1)
        f = jnp.concatenate([top, rows_ref[l]], axis=0)
        height, width = f.shape
        for step in range(STEPS):
            beside = (
                pltpu.roll(f, height - 1, 0)
                + pltpu.roll(f, 1, 0)
                + pltpu.roll(f, width - 1, 1)
                + pltpu.roll(f, 1, 1)
            )
            f = (f + kappa * (beside - 4.0 * f)) * mask
        core = f[:rows, :cols]
        out_ref[l] = core
        for c in range(flux_ref.shape[0]):
            flux_ref[c] += weight_ref[c, lev] * core
        return carry

    lax.fori_loop(0, levels, level, 0)


def diffuse(field, atm_kappa, vert_weight):
    levels, rows, cols = field.shape
    comps = vert_weight.shape[0]
    count_gx = lax.axis_size("gx")
    count_gy = lax.axis_size("gy")
    gx_index = lax.axis_index("gx")
    gy_index = lax.axis_index("gy")
    up_gx = [(i, i + 1) for i in range(count_gx - 1)]
    down_gx = [(i + 1, i) for i in range(count_gx - 1)]
    up_gy = [(i, i + 1) for i in range(count_gy - 1)]
    down_gy = [(i + 1, i) for i in range(count_gy - 1)]
    pairs = lambda di, dj: [
        ((i + di) * count_gy + j + dj, i * count_gy + j)
        for i in range(count_gx)
        for j in range(count_gy)
        if 0 <= i + di < count_gx and 0 <= j + dj < count_gy
    ]
    both = ("gx", "gy")
    south = lax.ppermute(field[:, :HALO, :], "gy", down_gy)
    north = lax.ppermute(field[:, rows - HALO :, :], "gy", up_gy)
    east = lax.ppermute(field[:, :, :HALO], "gx", down_gx)
    west = lax.ppermute(field[:, :, cols - HALO :], "gx", up_gx)
    south_east = lax.ppermute(field[:, :HALO, :HALO], both, pairs(1, 1))
    south_west = lax.ppermute(field[:, :HALO, cols - HALO :], both, pairs(-1, 1))
    north_east = lax.ppermute(field[:, rows - HALO :, :HALO], both, pairs(1, -1))
    north_west = lax.ppermute(field[:, rows - HALO :, cols - HALO :], both, pairs(-1, -1))
    gap = jnp.zeros((levels, rows, 128 - 2 * HALO), field.dtype)
    lanes = jnp.concatenate([east, gap, west], axis=2)
    corner_gap = jnp.zeros((levels, HALO, 128 - 2 * HALO), field.dtype)
    halo_rows = jnp.concatenate(
        [
            jnp.concatenate([south, south_east, corner_gap, south_west], axis=2),
            jnp.concatenate([north, north_east, corner_gap, north_west], axis=2),
        ],
        axis=1,
    )
    height = rows + 2 * HALO
    width = cols + 128
    r = jnp.arange(height, dtype=jnp.int32)
    c = jnp.arange(width, dtype=jnp.int32)
    global_r = gy_index * rows + jnp.where(r < rows + HALO, r, r - height)
    global_c = gx_index * cols + jnp.where(c < cols + HALO, c, c - width)
    inside_r = (global_r >= 0) & (global_r < count_gy * rows)
    inside_c = (global_c >= 0) & (global_c < count_gx * cols) & ((c < cols + HALO) | (c >= width - HALO))
    mask = (inside_r[:, None] & inside_c[None, :]).astype(jnp.float32)
    blocks = levels // LEVEL_BLOCK
    smem = pl.BlockSpec(memory_space=pltpu.SMEM)
    out, flux = pl.pallas_call(
        diffusion_kernel,
        grid=(blocks,),
        in_specs=[
            smem,
            smem,
            pl.BlockSpec((LEVEL_BLOCK, rows, cols), lambda b: (b, 0, 0)),
            pl.BlockSpec((LEVEL_BLOCK, rows, 128), lambda b: (b, 0, 0)),
            pl.BlockSpec((LEVEL_BLOCK, 2 * HALO, width), lambda b: (b, 0, 0)),
            pl.BlockSpec((height, width), lambda b: (0, 0)),
        ],
        out_specs=[
            pl.BlockSpec((LEVEL_BLOCK, rows, cols), lambda b: (b, 0, 0)),
            pl.BlockSpec((comps, rows, cols), lambda b: (0, 0, 0)),
        ],
        out_shape=[
            jax.ShapeDtypeStruct(field.shape, field.dtype),
            jax.ShapeDtypeStruct((comps, rows, cols), jnp.float32),
        ],
        compiler_params=pltpu.CompilerParams(dimension_semantics=("arbitrary",)),
        cost_estimate=pl.CostEstimate(
            flops=levels * height * width * STEPS * 10,
            transcendentals=0,
            bytes_accessed=2 * field.size * 4,
        ),
    )(atm_kappa, vert_weight, field, lanes, halo_rows, mask)
    return out, flux


def body(
    atm_state, atm_kappa, vert_weight, remap_src, remap_count, remap_weight, land_mask, ocean_term
):
    levels, tile_lat, tile_lon = atm_state.shape
    kappa = atm_kappa[:, None, None]
    count_gx = lax.axis_size("gx")
    count_gy = lax.axis_size("gy")
    coded_all = whole_grid(jnp.where(land_mask != 0, ocean_term, -1.0))
    maskf = (coded_all >= 0.0).astype(jnp.float32)
    field, flux = diffuse(atm_state, atm_kappa, vert_weight)
    flux = flux.reshape(flux.shape[0], tile_lat * tile_lon)
    ocean_blocks, lists, width, _ = remap_weight.shape
    comps = vert_weight.shape[0]
    own_blocks = tile_lat * tile_lon // width
    blocks = flux.astype(jnp.bfloat16).reshape(comps, own_blocks, width).transpose(1, 0, 2)
    devices = count_gx * count_gy
    gx_index = lax.axis_index("gx")
    gy_index = lax.axis_index("gy")
    me_index = gx_index * count_gy + gy_index
    east_index = (gx_index + 1) % count_gx * count_gy + gy_index
    west_index = (gx_index + count_gx - 1) % count_gx * count_gy + gy_index
    entries = ocean_blocks * lists
    slots = 2 * land_mask.shape[0]
    src_all = remap_src.reshape(devices, entries)
    live_all = (
        jnp.arange(lists, dtype=jnp.int32)[None, None, :]
        < remap_count.reshape(devices, ocean_blocks)[:, :, None]
    ).reshape(devices, entries)
    owner_all = src_all // own_blocks
    inside_all = src_all % own_blocks
    mine_owner = lax.dynamic_slice_in_dim(owner_all, me_index, 1, 0)[0]
    mine_inside = lax.dynamic_slice_in_dim(inside_all, me_index, 1, 0)[0]
    mine_live = lax.dynamic_slice_in_dim(live_all, me_index, 1, 0)[0]
    from_east = mine_live & (mine_owner == east_index)
    from_self = mine_live & (mine_owner == me_index)
    local_part = blocks[jnp.where(from_self, mine_inside, 0)]
    west_owner = lax.dynamic_slice_in_dim(owner_all, west_index, 1, 0)[0]
    west_inside = lax.dynamic_slice_in_dim(inside_all, west_index, 1, 0)[0]
    west_live = lax.dynamic_slice_in_dim(live_all, west_index, 1, 0)[0]
    wanted = (west_live & (west_owner == me_index)).astype(jnp.int32)
    wanted_rank = jnp.cumsum(wanted) - 1
    slot_ids = jnp.arange(slots, dtype=jnp.int32)
    picker = wanted[None, :] * (wanted_rank[None, :] == slot_ids[:, None]).astype(jnp.int32)
    send_index = jnp.sum(picker * west_inside[None, :], axis=1)
    send_valid = jnp.sum(picker, axis=1).astype(jnp.bfloat16)
    outgoing = blocks[send_index] * send_valid[:, None, None]
    incoming = shifted(outgoing, "gx", -1)
    east_int = from_east.astype(jnp.int32)
    east_rank = jnp.cumsum(east_int) - 1
    remote_part = incoming[jnp.where(from_east, east_rank, 0)]
    gathered = jnp.where(
        from_self[:, None, None],
        local_part,
        jnp.where(from_east[:, None, None], remote_part, jnp.zeros_like(local_part)),
    )
    gathered = gathered.reshape(ocean_blocks, lists, comps, width)
    ocean_rows, ocean_cols = land_mask.shape
    remapped = jnp.einsum(
        "bkij,bkcj->cbi", remap_weight, gathered, preferred_element_type=jnp.float32
    )
    ocean_flux = remapped.reshape(comps, ocean_rows, ocean_cols)
    rhs_tile = land_mask.astype(jnp.float32) * (ocean_flux[0] + ocean_flux[1])
    rhs = whole_grid(rhs_tile)
    height = jnp.zeros_like(rhs)
    residual = rhs
    direction = rhs
    norm_now = jnp.sum(residual * residual)
    for step in range(ITERS):
        image = grid_operator(direction, maskf, coded_all)
        alpha = norm_now / jnp.sum(direction * image)
        height = height + alpha * direction
        residual = residual - alpha * image
        norm_next = jnp.sum(residual * residual)
        direction = residual + norm_next / norm_now * direction
        norm_now = norm_next
    height = lax.dynamic_slice(height, (gy_index * ocean_rows, gx_index * ocean_cols), (ocean_rows, ocean_cols))
    residual = lax.dynamic_slice(residual, (gy_index * ocean_rows, gx_index * ocean_cols), (ocean_rows, ocean_cols))
    return (field, ocean_flux, height, residual)


def solution(mesh):
    return jax.shard_map(
        body,
        mesh=mesh,
        in_specs=(
            P(None, "gy", "gx"),
            P(),
            P(),
            P(),
            P(),
            P(("gx", "gy"), None, None, None),
            P("gy", "gx"),
            P("gy", "gx"),
        ),
        out_specs=(P(None, "gy", "gx"), P(None, "gy", "gx"), P("gy", "gx"), P("gy", "gx")),
        check_vma=False,
    )
```

```python
import jax
import jax.numpy as jnp
from jax import lax
from jax.sharding import PartitionSpec as P
from jax.experimental import pallas as pl
from jax.experimental.pallas import tpu as pltpu

STEPS = 4
ITERS = 3


def with_halo(x, sides, width):
    for axis, dim in sides:
        size, length = (lax.axis_size(axis), x.shape[dim])
        up = [(i, (i + 1) % size) for i in range(size - 1)]
        down = [(j, i) for i, j in up]
        last = lax.slice_in_dim(x, length - width, length, axis=dim)
        first = lax.slice_in_dim(x, 0, width, axis=dim)
        before = lax.ppermute(last, axis, up)
        after = lax.ppermute(first, axis, down)
        x = jnp.concatenate([before, x, after], axis=dim)
    return x


def shifted(x, axis, by):
    size = lax.axis_size(axis)
    return lax.ppermute(x, axis, [(i, (i + by) % size) for i in range(size)])


def ocean_operator(vector, maskf, ocean_term):
    padded = with_halo(maskf * vector, (("gx", 1), ("gy", 0)), 1)
    beside = padded[2:, 1:-1] + padded[:-2, 1:-1] + padded[1:-1, 2:] + padded[1:-1, :-2]
    return maskf * ((4.0 + ocean_term) * vector - beside) + (1.0 - maskf) * vector


def square_total(residual):
    return lax.psum(jnp.sum(residual * residual), ("gx", "gy"))


def gather_rounds():
    rounds = []
    for axis, bits in (("gy", lax.axis_size("gy")), ("gx", lax.axis_size("gx"))):
        distances = []
        d = 1
        while d < bits:
            distances.append(d)
            d *= 2
        rounds.append([(axis, d) for d in distances])
    gy_rounds, gx_rounds = rounds
    far = gy_rounds[1::2] + gx_rounds[2:]
    near = gy_rounds[0::2] + gx_rounds[1:2] + gx_rounds[:1]
    return far + near


def whole_grid(tile):
    rows, cols = tile.shape
    rounds = gather_rounds()
    x = tile[None]
    for axis, distance in rounds:
        size = lax.axis_size(axis)
        index = lax.axis_index(axis)
        other = lax.ppermute(x, axis, [(j, j ^ distance) for j in range(size)])
        low = jnp.concatenate([x, other], axis=0)
        high = jnp.concatenate([other, x], axis=0)
        x = jnp.where((index & distance) == 0, low, high)
    count = len(rounds)
    x = x.reshape((2,) * count + (rows, cols))
    order = []
    for axis in ("gy", "gx"):
        d = lax.axis_size(axis) // 2
        while d >= 1:
            order.append(count - 1 - rounds.index((axis, d)))
            d //= 2
    x = x.transpose(order + [count, count + 1])
    count_gy = lax.axis_size("gy")
    count_gx = lax.axis_size("gx")
    x = x.reshape(count_gy, count_gx, rows, cols).transpose(0, 2, 1, 3)
    return x.reshape(count_gy * rows, count_gx * cols)


def grid_operator(vector, maskf, ocean_term):
    padded = jnp.pad(maskf * vector, 1)
    beside = padded[2:, 1:-1] + padded[:-2, 1:-1] + padded[1:-1, 2:] + padded[1:-1, :-2]
    return maskf * ((4.0 + ocean_term) * vector - beside) + (1.0 - maskf) * vector


HALO = 4
LEVEL_BLOCK = 8


def diffusion_kernel(kappa_ref, weight_ref, core_ref, lanes_ref, rows_ref, mask_ref, out_ref, flux_ref):
    block = pl.program_id(0)
    levels, rows, cols = core_ref.shape

    @pl.when(block == 0)
    def _():
        flux_ref[...] = jnp.zeros_like(flux_ref)

    mask = mask_ref[...]

    def level(l, carry):
        lev = block * levels + l
        kappa = kappa_ref[lev]
        top = jnp.concatenate([core_ref[l], lanes_ref[l]], axis=1)
        f = jnp.concatenate([top, rows_ref[l]], axis=0)
        height, width = f.shape
        for step in range(STEPS):
            beside = (
                pltpu.roll(f, height - 1, 0)
                + pltpu.roll(f, 1, 0)
                + pltpu.roll(f, width - 1, 1)
                + pltpu.roll(f, 1, 1)
            )
            f = (f + kappa * (beside - 4.0 * f)) * mask
        core = f[:rows, :cols]
        out_ref[l] = core
        for c in range(flux_ref.shape[0]):
            flux_ref[c] += weight_ref[c, lev] * core
        return carry

    lax.fori_loop(0, levels, level, 0, unroll=2)


def diffuse(field, atm_kappa, vert_weight):
    levels, rows, cols = field.shape
    comps = vert_weight.shape[0]
    count_gx = lax.axis_size("gx")
    count_gy = lax.axis_size("gy")
    gx_index = lax.axis_index("gx")
    gy_index = lax.axis_index("gy")
    up_gx = [(i, i + 1) for i in range(count_gx - 1)]
    down_gx = [(i + 1, i) for i in range(count_gx - 1)]
    up_gy = [(i, i + 1) for i in range(count_gy - 1)]
    down_gy = [(i + 1, i) for i in range(count_gy - 1)]
    pairs = lambda di, dj: [
        ((i + di) * count_gy + j + dj, i * count_gy + j)
        for i in range(count_gx)
        for j in range(count_gy)
        if 0 <= i + di < count_gx and 0 <= j + dj < count_gy
    ]
    both = ("gx", "gy")
    south = lax.ppermute(field[:, :HALO, :], "gy", down_gy)
    north = lax.ppermute(field[:, rows - HALO :, :], "gy", up_gy)
    east = lax.ppermute(field[:, :, :HALO], "gx", down_gx)
    west = lax.ppermute(field[:, :, cols - HALO :], "gx", up_gx)
    south_east = lax.ppermute(field[:, :HALO, :HALO], both, pairs(1, 1))
    south_west = lax.ppermute(field[:, :HALO, cols - HALO :], both, pairs(-1, 1))
    north_east = lax.ppermute(field[:, rows - HALO :, :HALO], both, pairs(1, -1))
    north_west = lax.ppermute(field[:, rows - HALO :, cols - HALO :], both, pairs(-1, -1))
    gap = jnp.zeros((levels, rows, 128 - 2 * HALO), field.dtype)
    lanes = jnp.concatenate([east, gap, west], axis=2)
    corner_gap = jnp.zeros((levels, HALO, 128 - 2 * HALO), field.dtype)
    halo_rows = jnp.concatenate(
        [
            jnp.concatenate([south, south_east, corner_gap, south_west], axis=2),
            jnp.concatenate([north, north_east, corner_gap, north_west], axis=2),
        ],
        axis=1,
    )
    height = rows + 2 * HALO
    width = cols + 128
    r = jnp.arange(height, dtype=jnp.int32)
    c = jnp.arange(width, dtype=jnp.int32)
    global_r = gy_index * rows + jnp.where(r < rows + HALO, r, r - height)
    global_c = gx_index * cols + jnp.where(c < cols + HALO, c, c - width)
    inside_r = (global_r >= 0) & (global_r < count_gy * rows)
    inside_c = (global_c >= 0) & (global_c < count_gx * cols) & ((c < cols + HALO) | (c >= width - HALO))
    mask = (inside_r[:, None] & inside_c[None, :]).astype(jnp.float32)
    blocks = levels // LEVEL_BLOCK
    smem = pl.BlockSpec(memory_space=pltpu.SMEM)
    out, flux = pl.pallas_call(
        diffusion_kernel,
        grid=(blocks,),
        in_specs=[
            smem,
            smem,
            pl.BlockSpec((LEVEL_BLOCK, rows, cols), lambda b: (b, 0, 0)),
            pl.BlockSpec((LEVEL_BLOCK, rows, 128), lambda b: (b, 0, 0)),
            pl.BlockSpec((LEVEL_BLOCK, 2 * HALO, width), lambda b: (b, 0, 0)),
            pl.BlockSpec((height, width), lambda b: (0, 0)),
        ],
        out_specs=[
            pl.BlockSpec((LEVEL_BLOCK, rows, cols), lambda b: (b, 0, 0)),
            pl.BlockSpec((comps, rows, cols), lambda b: (0, 0, 0)),
        ],
        out_shape=[
            jax.ShapeDtypeStruct(field.shape, field.dtype),
            jax.ShapeDtypeStruct((comps, rows, cols), jnp.float32),
        ],
        compiler_params=pltpu.CompilerParams(dimension_semantics=("arbitrary",)),
        cost_estimate=pl.CostEstimate(
            flops=levels * height * width * STEPS * 10,
            transcendentals=0,
            bytes_accessed=2 * field.size * 4,
        ),
    )(atm_kappa, vert_weight, field, lanes, halo_rows, mask)
    return out, flux


def strip_sum(acc):
    return acc.sum(axis=0, keepdims=True).sum(axis=1, keepdims=True)


def cg_kernel(rhs_ref, coded_ref, height_ref, residual_ref, pad_ref, dir_ref, img_ref):
    rows, cols = rhs_ref.shape
    strips = rows // 8
    zeros = jnp.zeros((8, cols), jnp.float32)
    pad_ref[0:8, :] = zeros
    pad_ref[rows + 8 : rows + 16, :] = zeros
    row = lax.broadcasted_iota(jnp.int32, (8, cols), 0)
    col = lax.broadcasted_iota(jnp.int32, (8, cols), 1)

    def at(k, offset=0):
        return pl.ds(pl.multiple_of(k * 8 + offset, 8), 8)

    def init(k, acc):
        v = rhs_ref[at(k), :]
        m = (coded_ref[at(k), :] >= 0.0).astype(jnp.float32)
        residual_ref[at(k), :] = v
        dir_ref[at(k), :] = v
        height_ref[at(k), :] = jnp.zeros_like(v)
        pad_ref[at(k, 8), :] = m * v
        return acc + v * v

    def image(k, acc):
        prev = pad_ref[at(k), :]
        cur = pad_ref[at(k, 8), :]
        nxt = pad_ref[at(k, 16), :]
        south = jnp.where(row == 7, pltpu.roll(nxt, 7, 0), pltpu.roll(cur, 7, 0))
        north = jnp.where(row == 0, pltpu.roll(prev, 1, 0), pltpu.roll(cur, 1, 0))
        east = jnp.where(col == cols - 1, 0.0, pltpu.roll(cur, cols - 1, 1))
        west = jnp.where(col == 0, 0.0, pltpu.roll(cur, 1, 1))
        beside = south + north + east + west
        ot = coded_ref[at(k), :]
        m = (ot >= 0.0).astype(jnp.float32)
        v = dir_ref[at(k), :]
        w = m * ((4.0 + ot) * v - beside) + (1.0 - m) * v
        img_ref[at(k), :] = w
        return acc + v * w

    norm_now = strip_sum(lax.fori_loop(0, strips, init, zeros))
    for step in range(ITERS):
        alpha = norm_now / strip_sum(lax.fori_loop(0, strips, image, zeros))

        def update(k, acc):
            v = dir_ref[at(k), :]
            height_ref[at(k), :] = height_ref[at(k), :] + alpha * v
            r = residual_ref[at(k), :] - alpha * img_ref[at(k), :]
            residual_ref[at(k), :] = r
            return acc + r * r

        norm_next = strip_sum(lax.fori_loop(0, strips, update, zeros))
        beta = norm_next / norm_now

        def direct(k, carry):
            d = residual_ref[at(k), :] + beta * dir_ref[at(k), :]
            dir_ref[at(k), :] = d
            m = (coded_ref[at(k), :] >= 0.0).astype(jnp.float32)
            pad_ref[at(k, 8), :] = m * d
            return carry

        if step < ITERS - 1:
            lax.fori_loop(0, strips, direct, 0)
        norm_now = norm_next


def solve_grid(rhs, coded):
    rows, cols = rhs.shape
    whole = pl.BlockSpec(memory_space=pltpu.VMEM)
    return pl.pallas_call(
        cg_kernel,
        in_specs=[whole, whole],
        out_specs=[whole, whole],
        out_shape=[jax.ShapeDtypeStruct(rhs.shape, jnp.float32)] * 2,
        scratch_shapes=[
            pltpu.VMEM((rows + 16, cols), jnp.float32),
            pltpu.VMEM((rows, cols), jnp.float32),
            pltpu.VMEM((rows, cols), jnp.float32),
        ],
    )(rhs, coded)


def body(
    atm_state, atm_kappa, vert_weight, remap_src, remap_count, remap_weight, land_mask, ocean_term
):
    levels, tile_lat, tile_lon = atm_state.shape
    kappa = atm_kappa[:, None, None]
    count_gx = lax.axis_size("gx")
    count_gy = lax.axis_size("gy")
    coded_all = whole_grid(jnp.where(land_mask != 0, ocean_term, -1.0))
    field, flux = diffuse(atm_state, atm_kappa, vert_weight)
    flux = flux.reshape(flux.shape[0], tile_lat * tile_lon)
    ocean_blocks, lists, width, _ = remap_weight.shape
    comps = vert_weight.shape[0]
    own_blocks = tile_lat * tile_lon // width
    blocks = flux.astype(jnp.bfloat16).reshape(comps, own_blocks, width).transpose(1, 0, 2)
    devices = count_gx * count_gy
    gx_index = lax.axis_index("gx")
    gy_index = lax.axis_index("gy")
    me_index = gx_index * count_gy + gy_index
    east_index = (gx_index + 1) % count_gx * count_gy + gy_index
    west_index = (gx_index + count_gx - 1) % count_gx * count_gy + gy_index
    entries = ocean_blocks * lists
    slots = 2 * land_mask.shape[0]
    src_all = remap_src.reshape(devices, entries)
    live_all = (
        jnp.arange(lists, dtype=jnp.int32)[None, None, :]
        < remap_count.reshape(devices, ocean_blocks)[:, :, None]
    ).reshape(devices, entries)
    owner_all = src_all // own_blocks
    inside_all = src_all % own_blocks
    mine_owner = lax.dynamic_slice_in_dim(owner_all, me_index, 1, 0)[0]
    mine_inside = lax.dynamic_slice_in_dim(inside_all, me_index, 1, 0)[0]
    mine_live = lax.dynamic_slice_in_dim(live_all, me_index, 1, 0)[0]
    from_east = mine_live & (mine_owner == east_index)
    from_self = mine_live & (mine_owner == me_index)
    local_part = blocks[jnp.where(from_self, mine_inside, 0)]
    west_owner = lax.dynamic_slice_in_dim(owner_all, west_index, 1, 0)[0]
    west_inside = lax.dynamic_slice_in_dim(inside_all, west_index, 1, 0)[0]
    west_live = lax.dynamic_slice_in_dim(live_all, west_index, 1, 0)[0]
    wanted = (west_live & (west_owner == me_index)).astype(jnp.int32)
    wanted_rank = jnp.cumsum(wanted) - 1
    slot_ids = jnp.arange(slots, dtype=jnp.int32)
    picker = wanted[None, :] * (wanted_rank[None, :] == slot_ids[:, None]).astype(jnp.int32)
    send_index = jnp.sum(picker * west_inside[None, :], axis=1)
    send_valid = jnp.sum(picker, axis=1).astype(jnp.bfloat16)
    outgoing = blocks[send_index] * send_valid[:, None, None]
    incoming = shifted(outgoing, "gx", -1)
    east_int = from_east.astype(jnp.int32)
    east_rank = jnp.cumsum(east_int) - 1
    remote_part = incoming[jnp.where(from_east, east_rank, 0)]
    gathered = jnp.where(
        from_self[:, None, None],
        local_part,
        jnp.where(from_east[:, None, None], remote_part, jnp.zeros_like(local_part)),
    )
    gathered = gathered.reshape(ocean_blocks, lists, comps, width)
    ocean_rows, ocean_cols = land_mask.shape
    remapped = jnp.einsum(
        "bkij,bkcj->cbi", remap_weight, gathered, preferred_element_type=jnp.float32
    )
    ocean_flux = remapped.reshape(comps, ocean_rows, ocean_cols)
    rhs_tile = land_mask.astype(jnp.float32) * (ocean_flux[0] + ocean_flux[1])
    rhs = whole_grid(rhs_tile)
    height, residual = solve_grid(rhs, coded_all)
    height = lax.dynamic_slice(height, (gy_index * ocean_rows, gx_index * ocean_cols), (ocean_rows, ocean_cols))
    residual = lax.dynamic_slice(residual, (gy_index * ocean_rows, gx_index * ocean_cols), (ocean_rows, ocean_cols))
    return (field, ocean_flux, height, residual)


def solution(mesh):
    return jax.shard_map(
        body,
        mesh=mesh,
        in_specs=(
            P(None, "gy", "gx"),
            P(),
            P(),
            P(),
            P(),
            P(("gx", "gy"), None, None, None),
            P("gy", "gx"),
            P("gy", "gx"),
        ),
        out_specs=(P(None, "gy", "gx"), P(None, "gy", "gx"), P("gy", "gx"), P("gy", "gx")),
        check_vma=False,
    )
```

```python
import functools

import jax
import jax.numpy as jnp
from jax import lax
from jax.sharding import PartitionSpec as P
from jax.experimental import pallas as pl
from jax.experimental.pallas import tpu as pltpu

STEPS = 4
ITERS = 3


def with_halo(x, sides, width):
    for axis, dim in sides:
        size, length = (lax.axis_size(axis), x.shape[dim])
        up = [(i, (i + 1) % size) for i in range(size - 1)]
        down = [(j, i) for i, j in up]
        last = lax.slice_in_dim(x, length - width, length, axis=dim)
        first = lax.slice_in_dim(x, 0, width, axis=dim)
        before = lax.ppermute(last, axis, up)
        after = lax.ppermute(first, axis, down)
        x = jnp.concatenate([before, x, after], axis=dim)
    return x


def shifted(x, axis, by):
    size = lax.axis_size(axis)
    return lax.ppermute(x, axis, [(i, (i + by) % size) for i in range(size)])


def ocean_operator(vector, maskf, ocean_term):
    padded = with_halo(maskf * vector, (("gx", 1), ("gy", 0)), 1)
    beside = padded[2:, 1:-1] + padded[:-2, 1:-1] + padded[1:-1, 2:] + padded[1:-1, :-2]
    return maskf * ((4.0 + ocean_term) * vector - beside) + (1.0 - maskf) * vector


def square_total(residual):
    return lax.psum(jnp.sum(residual * residual), ("gx", "gy"))


def gather_rounds():
    rounds = []
    for axis, bits in (("gy", lax.axis_size("gy")), ("gx", lax.axis_size("gx"))):
        distances = []
        d = 1
        while d < bits:
            distances.append(d)
            d *= 2
        rounds.append([(axis, d) for d in distances])
    gy_rounds, gx_rounds = rounds
    far = gy_rounds[1::2] + gx_rounds[2:]
    near = gy_rounds[0::2] + gx_rounds[1:2] + gx_rounds[:1]
    return far + near


def stack_gather(tile, rounds):
    x = tile[None]
    for axis, distance in rounds:
        size = lax.axis_size(axis)
        other = lax.ppermute(x, axis, [(j, j ^ distance) for j in range(size)])
        x = jnp.concatenate([x, other], axis=0)
    return x


def grid_operator(vector, maskf, ocean_term):
    padded = jnp.pad(maskf * vector, 1)
    beside = padded[2:, 1:-1] + padded[:-2, 1:-1] + padded[1:-1, 2:] + padded[1:-1, :-2]
    return maskf * ((4.0 + ocean_term) * vector - beside) + (1.0 - maskf) * vector


HALO = 4
LEVEL_BLOCK = 8


def diffusion_kernel(kappa_ref, weight_ref, core_ref, lanes_ref, rows_ref, mask_ref, out_ref, flux_ref):
    block = pl.program_id(0)
    levels, rows, cols = core_ref.shape

    @pl.when(block == 0)
    def _():
        flux_ref[...] = jnp.zeros_like(flux_ref)

    mask = mask_ref[...]

    def level(l, carry):
        lev = block * levels + l
        kappa = kappa_ref[lev]
        top = jnp.concatenate([core_ref[l], lanes_ref[l]], axis=1)
        f = jnp.concatenate([top, rows_ref[l]], axis=0)
        height, width = f.shape
        for step in range(STEPS):
            beside = (
                pltpu.roll(f, height - 1, 0)
                + pltpu.roll(f, 1, 0)
                + pltpu.roll(f, width - 1, 1)
                + pltpu.roll(f, 1, 1)
            )
            f = (f + kappa * (beside - 4.0 * f)) * mask
        core = f[:rows, :cols]
        out_ref[l] = core
        for c in range(flux_ref.shape[0]):
            flux_ref[c] += weight_ref[c, lev] * core
        return carry

    lax.fori_loop(0, levels, level, 0, unroll=2)


def diffuse(field, atm_kappa, vert_weight):
    levels, rows, cols = field.shape
    comps = vert_weight.shape[0]
    count_gx = lax.axis_size("gx")
    count_gy = lax.axis_size("gy")
    gx_index = lax.axis_index("gx")
    gy_index = lax.axis_index("gy")
    up_gx = [(i, i + 1) for i in range(count_gx - 1)]
    down_gx = [(i + 1, i) for i in range(count_gx - 1)]
    up_gy = [(i, i + 1) for i in range(count_gy - 1)]
    down_gy = [(i + 1, i) for i in range(count_gy - 1)]
    pairs = lambda di, dj: [
        ((i + di) * count_gy + j + dj, i * count_gy + j)
        for i in range(count_gx)
        for j in range(count_gy)
        if 0 <= i + di < count_gx and 0 <= j + dj < count_gy
    ]
    both = ("gx", "gy")
    south = lax.ppermute(field[:, :HALO, :], "gy", down_gy)
    north = lax.ppermute(field[:, rows - HALO :, :], "gy", up_gy)
    east = lax.ppermute(field[:, :, :HALO], "gx", down_gx)
    west = lax.ppermute(field[:, :, cols - HALO :], "gx", up_gx)
    south_east = lax.ppermute(field[:, :HALO, :HALO], both, pairs(1, 1))
    south_west = lax.ppermute(field[:, :HALO, cols - HALO :], both, pairs(-1, 1))
    north_east = lax.ppermute(field[:, rows - HALO :, :HALO], both, pairs(1, -1))
    north_west = lax.ppermute(field[:, rows - HALO :, cols - HALO :], both, pairs(-1, -1))
    gap = jnp.zeros((levels, rows, 128 - 2 * HALO), field.dtype)
    lanes = jnp.concatenate([east, gap, west], axis=2)
    corner_gap = jnp.zeros((levels, HALO, 128 - 2 * HALO), field.dtype)
    halo_rows = jnp.concatenate(
        [
            jnp.concatenate([south, south_east, corner_gap, south_west], axis=2),
            jnp.concatenate([north, north_east, corner_gap, north_west], axis=2),
        ],
        axis=1,
    )
    height = rows + 2 * HALO
    width = cols + 128
    r = jnp.arange(height, dtype=jnp.int32)
    c = jnp.arange(width, dtype=jnp.int32)
    global_r = gy_index * rows + jnp.where(r < rows + HALO, r, r - height)
    global_c = gx_index * cols + jnp.where(c < cols + HALO, c, c - width)
    inside_r = (global_r >= 0) & (global_r < count_gy * rows)
    inside_c = (global_c >= 0) & (global_c < count_gx * cols) & ((c < cols + HALO) | (c >= width - HALO))
    mask = (inside_r[:, None] & inside_c[None, :]).astype(jnp.float32)
    blocks = levels // LEVEL_BLOCK
    smem = pl.BlockSpec(memory_space=pltpu.SMEM)
    out, flux = pl.pallas_call(
        diffusion_kernel,
        grid=(blocks,),
        in_specs=[
            smem,
            smem,
            pl.BlockSpec((LEVEL_BLOCK, rows, cols), lambda b: (b, 0, 0)),
            pl.BlockSpec((LEVEL_BLOCK, rows, 128), lambda b: (b, 0, 0)),
            pl.BlockSpec((LEVEL_BLOCK, 2 * HALO, width), lambda b: (b, 0, 0)),
            pl.BlockSpec((height, width), lambda b: (0, 0)),
        ],
        out_specs=[
            pl.BlockSpec((LEVEL_BLOCK, rows, cols), lambda b: (b, 0, 0)),
            pl.BlockSpec((comps, rows, cols), lambda b: (0, 0, 0)),
        ],
        out_shape=[
            jax.ShapeDtypeStruct(field.shape, field.dtype),
            jax.ShapeDtypeStruct((comps, rows, cols), jnp.float32),
        ],
        compiler_params=pltpu.CompilerParams(dimension_semantics=("arbitrary",)),
        cost_estimate=pl.CostEstimate(
            flops=levels * height * width * STEPS * 10,
            transcendentals=0,
            bytes_accessed=2 * field.size * 4,
        ),
    )(atm_kappa, vert_weight, field, lanes, halo_rows, mask)
    return out, flux


def strip_sum(acc):
    return acc.sum(axis=0, keepdims=True).sum(axis=1, keepdims=True)


def cg_kernel(
    rounds, index_ref, rhs_stack, coded_stack, height_out, residual_out,
    rhs_ref, coded_ref, height_ref, residual_ref, pad_ref, dir_ref, img_ref,
):
    rows, cols = rhs_ref.shape
    tile_rows, tile_cols = height_out.shape
    gy = index_ref[0]
    gx = index_ref[1]

    def place(k, carry):
        gy_off = 0
        gx_off = 0
        for bit, (axis, distance) in enumerate(rounds):
            flag = lax.shift_right_logical(k, bit) & 1
            if axis == "gy":
                gy_off = gy_off + flag * distance
            else:
                gx_off = gx_off + flag * distance
        r0 = pl.multiple_of(lax.bitwise_xor(gy, gy_off) * tile_rows, tile_rows)
        c0 = pl.multiple_of(lax.bitwise_xor(gx, gx_off) * tile_cols, tile_cols)
        rhs_ref[pl.ds(r0, tile_rows), pl.ds(c0, tile_cols)] = rhs_stack[k]
        coded_ref[pl.ds(r0, tile_rows), pl.ds(c0, tile_cols)] = coded_stack[k]
        return carry

    lax.fori_loop(0, rhs_stack.shape[0], place, 0)
    strips = rows // 8
    zeros = jnp.zeros((8, cols), jnp.float32)
    pad_ref[0:8, :] = zeros
    pad_ref[rows + 8 : rows + 16, :] = zeros
    row = lax.broadcasted_iota(jnp.int32, (8, cols), 0)
    col = lax.broadcasted_iota(jnp.int32, (8, cols), 1)

    def at(k, offset=0):
        return pl.ds(pl.multiple_of(k * 8 + offset, 8), 8)

    def init(k, acc):
        v = rhs_ref[at(k), :]
        m = (coded_ref[at(k), :] >= 0.0).astype(jnp.float32)
        residual_ref[at(k), :] = v
        dir_ref[at(k), :] = v
        height_ref[at(k), :] = jnp.zeros_like(v)
        pad_ref[at(k, 8), :] = m * v
        return acc + v * v

    def image(k, acc):
        prev = pad_ref[at(k), :]
        cur = pad_ref[at(k, 8), :]
        nxt = pad_ref[at(k, 16), :]
        south = jnp.where(row == 7, pltpu.roll(nxt, 7, 0), pltpu.roll(cur, 7, 0))
        north = jnp.where(row == 0, pltpu.roll(prev, 1, 0), pltpu.roll(cur, 1, 0))
        east = jnp.where(col == cols - 1, 0.0, pltpu.roll(cur, cols - 1, 1))
        west = jnp.where(col == 0, 0.0, pltpu.roll(cur, 1, 1))
        beside = south + north + east + west
        ot = coded_ref[at(k), :]
        m = (ot >= 0.0).astype(jnp.float32)
        v = dir_ref[at(k), :]
        w = m * ((4.0 + ot) * v - beside) + (1.0 - m) * v
        img_ref[at(k), :] = w
        return acc + v * w

    norm_now = strip_sum(lax.fori_loop(0, strips, init, zeros))
    for step in range(ITERS):
        alpha = norm_now / strip_sum(lax.fori_loop(0, strips, image, zeros))

        def update(k, acc):
            v = dir_ref[at(k), :]
            height_ref[at(k), :] = height_ref[at(k), :] + alpha * v
            r = residual_ref[at(k), :] - alpha * img_ref[at(k), :]
            residual_ref[at(k), :] = r
            return acc + r * r

        norm_next = strip_sum(lax.fori_loop(0, strips, update, zeros))
        beta = norm_next / norm_now

        def direct(k, carry):
            d = residual_ref[at(k), :] + beta * dir_ref[at(k), :]
            dir_ref[at(k), :] = d
            m = (coded_ref[at(k), :] >= 0.0).astype(jnp.float32)
            pad_ref[at(k, 8), :] = m * d
            return carry

        if step < ITERS - 1:
            lax.fori_loop(0, strips, direct, 0)
        norm_now = norm_next
    r0 = pl.multiple_of(gy * tile_rows, tile_rows)
    c0 = pl.multiple_of(gx * tile_cols, tile_cols)
    height_out[...] = height_ref[pl.ds(r0, tile_rows), pl.ds(c0, tile_cols)]
    residual_out[...] = residual_ref[pl.ds(r0, tile_rows), pl.ds(c0, tile_cols)]


def solve_grid(rhs_stack, coded_stack, rounds):
    parts, tile_rows, tile_cols = rhs_stack.shape
    rows = lax.axis_size("gy") * tile_rows
    cols = lax.axis_size("gx") * tile_cols
    index = jnp.stack([lax.axis_index("gy"), lax.axis_index("gx")]).astype(jnp.int32)
    whole = pl.BlockSpec(memory_space=pltpu.VMEM)
    grid = pltpu.VMEM((rows, cols), jnp.float32)
    return pl.pallas_call(
        functools.partial(cg_kernel, rounds),
        in_specs=[pl.BlockSpec(memory_space=pltpu.SMEM), whole, whole],
        out_specs=[whole, whole],
        out_shape=[jax.ShapeDtypeStruct((tile_rows, tile_cols), jnp.float32)] * 2,
        scratch_shapes=[grid, grid, grid, grid, pltpu.VMEM((rows + 16, cols), jnp.float32), grid, grid],
    )(index, rhs_stack, coded_stack)


def body(
    atm_state, atm_kappa, vert_weight, remap_src, remap_count, remap_weight, land_mask, ocean_term
):
    levels, tile_lat, tile_lon = atm_state.shape
    kappa = atm_kappa[:, None, None]
    count_gx = lax.axis_size("gx")
    count_gy = lax.axis_size("gy")
    rounds = gather_rounds()
    coded_all = stack_gather(jnp.where(land_mask != 0, ocean_term, -1.0), rounds)
    field, flux = diffuse(atm_state, atm_kappa, vert_weight)
    flux = flux.reshape(flux.shape[0], tile_lat * tile_lon)
    ocean_blocks, lists, width, _ = remap_weight.shape
    comps = vert_weight.shape[0]
    own_blocks = tile_lat * tile_lon // width
    blocks = flux.astype(jnp.bfloat16).reshape(comps, own_blocks, width).transpose(1, 0, 2)
    devices = count_gx * count_gy
    gx_index = lax.axis_index("gx")
    gy_index = lax.axis_index("gy")
    me_index = gx_index * count_gy + gy_index
    east_index = (gx_index + 1) % count_gx * count_gy + gy_index
    west_index = (gx_index + count_gx - 1) % count_gx * count_gy + gy_index
    entries = ocean_blocks * lists
    slots = 2 * land_mask.shape[0]
    src_all = remap_src.reshape(devices, entries)
    live_all = (
        jnp.arange(lists, dtype=jnp.int32)[None, None, :]
        < remap_count.reshape(devices, ocean_blocks)[:, :, None]
    ).reshape(devices, entries)
    owner_all = src_all // own_blocks
    inside_all = src_all % own_blocks
    mine_owner = lax.dynamic_slice_in_dim(owner_all, me_index, 1, 0)[0]
    mine_inside = lax.dynamic_slice_in_dim(inside_all, me_index, 1, 0)[0]
    mine_live = lax.dynamic_slice_in_dim(live_all, me_index, 1, 0)[0]
    from_east = mine_live & (mine_owner == east_index)
    from_self = mine_live & (mine_owner == me_index)
    local_part = blocks[jnp.where(from_self, mine_inside, 0)]
    west_owner = lax.dynamic_slice_in_dim(owner_all, west_index, 1, 0)[0]
    west_inside = lax.dynamic_slice_in_dim(inside_all, west_index, 1, 0)[0]
    west_live = lax.dynamic_slice_in_dim(live_all, west_index, 1, 0)[0]
    wanted = (west_live & (west_owner == me_index)).astype(jnp.int32)
    wanted_rank = jnp.cumsum(wanted) - 1
    slot_ids = jnp.arange(slots, dtype=jnp.int32)
    picker = wanted[None, :] * (wanted_rank[None, :] == slot_ids[:, None]).astype(jnp.int32)
    send_index = jnp.sum(picker * west_inside[None, :], axis=1)
    send_valid = jnp.sum(picker, axis=1).astype(jnp.bfloat16)
    outgoing = blocks[send_index] * send_valid[:, None, None]
    incoming = shifted(outgoing, "gx", -1)
    east_int = from_east.astype(jnp.int32)
    east_rank = jnp.cumsum(east_int) - 1
    remote_part = incoming[jnp.where(from_east, east_rank, 0)]
    gathered = jnp.where(
        from_self[:, None, None],
        local_part,
        jnp.where(from_east[:, None, None], remote_part, jnp.zeros_like(local_part)),
    )
    gathered = gathered.reshape(ocean_blocks, lists, comps, width)
    ocean_rows, ocean_cols = land_mask.shape
    remapped = jnp.einsum(
        "bkij,bkcj->cbi", remap_weight, gathered, preferred_element_type=jnp.float32
    )
    ocean_flux = remapped.reshape(comps, ocean_rows, ocean_cols)
    rhs_tile = land_mask.astype(jnp.float32) * (ocean_flux[0] + ocean_flux[1])
    rhs = stack_gather(rhs_tile, rounds)
    height, residual = solve_grid(rhs, coded_all, rounds)
    return (field, ocean_flux, height, residual)


def solution(mesh):
    return jax.shard_map(
        body,
        mesh=mesh,
        in_specs=(
            P(None, "gy", "gx"),
            P(),
            P(),
            P(),
            P(),
            P(("gx", "gy"), None, None, None),
            P("gy", "gx"),
            P("gy", "gx"),
        ),
        out_specs=(P(None, "gy", "gx"), P(None, "gy", "gx"), P("gy", "gx"), P("gy", "gx")),
        check_vma=False,
    )
```

```python
import functools

import jax
import jax.numpy as jnp
from jax import lax
from jax.sharding import PartitionSpec as P
from jax.experimental import pallas as pl
from jax.experimental.pallas import tpu as pltpu

STEPS = 4
ITERS = 3


def with_halo(x, sides, width):
    for axis, dim in sides:
        size, length = (lax.axis_size(axis), x.shape[dim])
        up = [(i, (i + 1) % size) for i in range(size - 1)]
        down = [(j, i) for i, j in up]
        last = lax.slice_in_dim(x, length - width, length, axis=dim)
        first = lax.slice_in_dim(x, 0, width, axis=dim)
        before = lax.ppermute(last, axis, up)
        after = lax.ppermute(first, axis, down)
        x = jnp.concatenate([before, x, after], axis=dim)
    return x


def shifted(x, axis, by):
    size = lax.axis_size(axis)
    return lax.ppermute(x, axis, [(i, (i + by) % size) for i in range(size)])


def ocean_operator(vector, maskf, ocean_term):
    padded = with_halo(maskf * vector, (("gx", 1), ("gy", 0)), 1)
    beside = padded[2:, 1:-1] + padded[:-2, 1:-1] + padded[1:-1, 2:] + padded[1:-1, :-2]
    return maskf * ((4.0 + ocean_term) * vector - beside) + (1.0 - maskf) * vector


def square_total(residual):
    return lax.psum(jnp.sum(residual * residual), ("gx", "gy"))


def gather_rounds():
    rounds = []
    for axis, bits in (("gy", lax.axis_size("gy")), ("gx", lax.axis_size("gx"))):
        distances = []
        d = 1
        while d < bits:
            distances.append(d)
            d *= 2
        rounds.append([(axis, d) for d in distances])
    gy_rounds, gx_rounds = rounds
    far = gy_rounds[1::2] + gx_rounds[2:]
    near = gy_rounds[0::2] + gx_rounds[1:2] + gx_rounds[:1]
    return far + near


def stack_gather(tile, rounds):
    x = tile[None]
    for axis, distance in rounds:
        size = lax.axis_size(axis)
        other = lax.ppermute(x, axis, [(j, j ^ distance) for j in range(size)])
        x = jnp.concatenate([x, other], axis=0)
    return x


def grid_operator(vector, maskf, ocean_term):
    padded = jnp.pad(maskf * vector, 1)
    beside = padded[2:, 1:-1] + padded[:-2, 1:-1] + padded[1:-1, 2:] + padded[1:-1, :-2]
    return maskf * ((4.0 + ocean_term) * vector - beside) + (1.0 - maskf) * vector


HALO = 4
LEVEL_BLOCK = 8


def diffusion_kernel(kappa_ref, weight_ref, core_ref, lanes_ref, rows_ref, mask_ref, out_ref, flux_ref):
    block = pl.program_id(0)
    levels, rows, cols = core_ref.shape

    @pl.when(block == 0)
    def _():
        flux_ref[...] = jnp.zeros_like(flux_ref)

    mask = mask_ref[...]

    def level(l, carry):
        lev = block * levels + l
        kappa = kappa_ref[lev]
        top = jnp.concatenate([core_ref[l], lanes_ref[l]], axis=1)
        f = jnp.concatenate([top, rows_ref[l]], axis=0)
        height, width = f.shape
        for step in range(STEPS):
            beside = (
                pltpu.roll(f, height - 1, 0)
                + pltpu.roll(f, 1, 0)
                + pltpu.roll(f, width - 1, 1)
                + pltpu.roll(f, 1, 1)
            )
            f = (f + kappa * (beside - 4.0 * f)) * mask
        core = f[:rows, :cols]
        out_ref[l] = core
        for c in range(flux_ref.shape[0]):
            flux_ref[c] += weight_ref[c, lev] * core
        return carry

    lax.fori_loop(0, levels, level, 0, unroll=2)


def diffuse(field, atm_kappa, vert_weight):
    levels, rows, cols = field.shape
    comps = vert_weight.shape[0]
    count_gx = lax.axis_size("gx")
    count_gy = lax.axis_size("gy")
    gx_index = lax.axis_index("gx")
    gy_index = lax.axis_index("gy")
    up_gx = [(i, i + 1) for i in range(count_gx - 1)]
    down_gx = [(i + 1, i) for i in range(count_gx - 1)]
    up_gy = [(i, i + 1) for i in range(count_gy - 1)]
    down_gy = [(i + 1, i) for i in range(count_gy - 1)]
    pairs = lambda di, dj: [
        ((i + di) * count_gy + j + dj, i * count_gy + j)
        for i in range(count_gx)
        for j in range(count_gy)
        if 0 <= i + di < count_gx and 0 <= j + dj < count_gy
    ]
    both = ("gx", "gy")
    south = lax.ppermute(field[:, :HALO, :], "gy", down_gy)
    north = lax.ppermute(field[:, rows - HALO :, :], "gy", up_gy)
    east = lax.ppermute(field[:, :, :HALO], "gx", down_gx)
    west = lax.ppermute(field[:, :, cols - HALO :], "gx", up_gx)
    south_east = lax.ppermute(field[:, :HALO, :HALO], both, pairs(1, 1))
    south_west = lax.ppermute(field[:, :HALO, cols - HALO :], both, pairs(-1, 1))
    north_east = lax.ppermute(field[:, rows - HALO :, :HALO], both, pairs(1, -1))
    north_west = lax.ppermute(field[:, rows - HALO :, cols - HALO :], both, pairs(-1, -1))
    gap = jnp.zeros((levels, rows, 128 - 2 * HALO), field.dtype)
    lanes = jnp.concatenate([east, gap, west], axis=2)
    corner_gap = jnp.zeros((levels, HALO, 128 - 2 * HALO), field.dtype)
    halo_rows = jnp.concatenate(
        [
            jnp.concatenate([south, south_east, corner_gap, south_west], axis=2),
            jnp.concatenate([north, north_east, corner_gap, north_west], axis=2),
        ],
        axis=1,
    )
    height = rows + 2 * HALO
    width = cols + 128
    r = jnp.arange(height, dtype=jnp.int32)
    c = jnp.arange(width, dtype=jnp.int32)
    global_r = gy_index * rows + jnp.where(r < rows + HALO, r, r - height)
    global_c = gx_index * cols + jnp.where(c < cols + HALO, c, c - width)
    inside_r = (global_r >= 0) & (global_r < count_gy * rows)
    inside_c = (global_c >= 0) & (global_c < count_gx * cols) & ((c < cols + HALO) | (c >= width - HALO))
    mask = (inside_r[:, None] & inside_c[None, :]).astype(jnp.float32)
    blocks = levels // LEVEL_BLOCK
    smem = pl.BlockSpec(memory_space=pltpu.SMEM)
    out, flux = pl.pallas_call(
        diffusion_kernel,
        grid=(blocks,),
        in_specs=[
            smem,
            smem,
            pl.BlockSpec((LEVEL_BLOCK, rows, cols), lambda b: (b, 0, 0)),
            pl.BlockSpec((LEVEL_BLOCK, rows, 128), lambda b: (b, 0, 0)),
            pl.BlockSpec((LEVEL_BLOCK, 2 * HALO, width), lambda b: (b, 0, 0)),
            pl.BlockSpec((height, width), lambda b: (0, 0)),
        ],
        out_specs=[
            pl.BlockSpec((LEVEL_BLOCK, rows, cols), lambda b: (b, 0, 0)),
            pl.BlockSpec((comps, rows, cols), lambda b: (0, 0, 0)),
        ],
        out_shape=[
            jax.ShapeDtypeStruct(field.shape, field.dtype),
            jax.ShapeDtypeStruct((comps, rows, cols), jnp.float32),
        ],
        compiler_params=pltpu.CompilerParams(dimension_semantics=("arbitrary",)),
        cost_estimate=pl.CostEstimate(
            flops=levels * height * width * STEPS * 10,
            transcendentals=0,
            bytes_accessed=2 * field.size * 4,
        ),
    )(atm_kappa, vert_weight, field, lanes, halo_rows, mask)
    return out, flux


def strip_sum(acc):
    return acc.sum(axis=0, keepdims=True).sum(axis=1, keepdims=True)


def cg_kernel(
    rounds, index_ref, both_stack, height_out, residual_out,
    rhs_ref, coded_ref, height_ref, residual_ref, pad_ref, dir_ref, img_ref,
):
    rows, cols = rhs_ref.shape
    tile_rows, tile_cols = height_out.shape
    gy = index_ref[0]
    gx = index_ref[1]

    def place(k, carry):
        gy_off = 0
        gx_off = 0
        for bit, (axis, distance) in enumerate(rounds):
            flag = lax.shift_right_logical(k, bit) & 1
            if axis == "gy":
                gy_off = gy_off + flag * distance
            else:
                gx_off = gx_off + flag * distance
        r0 = pl.multiple_of(lax.bitwise_xor(gy, gy_off) * tile_rows, tile_rows)
        c0 = pl.multiple_of(lax.bitwise_xor(gx, gx_off) * tile_cols, tile_cols)
        rhs_ref[pl.ds(r0, tile_rows), pl.ds(c0, tile_cols)] = both_stack[k, 1]
        coded_ref[pl.ds(r0, tile_rows), pl.ds(c0, tile_cols)] = both_stack[k, 0]
        return carry

    lax.fori_loop(0, both_stack.shape[0], place, 0)
    strips = rows // 8
    zeros = jnp.zeros((8, cols), jnp.float32)
    pad_ref[0:8, :] = zeros
    pad_ref[rows + 8 : rows + 16, :] = zeros
    row = lax.broadcasted_iota(jnp.int32, (8, cols), 0)
    col = lax.broadcasted_iota(jnp.int32, (8, cols), 1)

    def at(k, offset=0):
        return pl.ds(pl.multiple_of(k * 8 + offset, 8), 8)

    def init(k, acc):
        v = rhs_ref[at(k), :]
        m = (coded_ref[at(k), :] >= 0.0).astype(jnp.float32)
        residual_ref[at(k), :] = v
        dir_ref[at(k), :] = v
        height_ref[at(k), :] = jnp.zeros_like(v)
        pad_ref[at(k, 8), :] = m * v
        return acc + v * v

    def image(k, acc):
        prev = pad_ref[at(k), :]
        cur = pad_ref[at(k, 8), :]
        nxt = pad_ref[at(k, 16), :]
        south = jnp.where(row == 7, pltpu.roll(nxt, 7, 0), pltpu.roll(cur, 7, 0))
        north = jnp.where(row == 0, pltpu.roll(prev, 1, 0), pltpu.roll(cur, 1, 0))
        east = jnp.where(col == cols - 1, 0.0, pltpu.roll(cur, cols - 1, 1))
        west = jnp.where(col == 0, 0.0, pltpu.roll(cur, 1, 1))
        beside = south + north + east + west
        ot = coded_ref[at(k), :]
        m = (ot >= 0.0).astype(jnp.float32)
        v = dir_ref[at(k), :]
        w = m * ((4.0 + ot) * v - beside) + (1.0 - m) * v
        img_ref[at(k), :] = w
        return acc + v * w

    norm_now = strip_sum(lax.fori_loop(0, strips, init, zeros))
    for step in range(ITERS):
        alpha = norm_now / strip_sum(lax.fori_loop(0, strips, image, zeros))

        def update(k, acc):
            v = dir_ref[at(k), :]
            height_ref[at(k), :] = height_ref[at(k), :] + alpha * v
            r = residual_ref[at(k), :] - alpha * img_ref[at(k), :]
            residual_ref[at(k), :] = r
            return acc + r * r

        norm_next = strip_sum(lax.fori_loop(0, strips, update, zeros))
        beta = norm_next / norm_now

        def direct(k, carry):
            d = residual_ref[at(k), :] + beta * dir_ref[at(k), :]
            dir_ref[at(k), :] = d
            m = (coded_ref[at(k), :] >= 0.0).astype(jnp.float32)
            pad_ref[at(k, 8), :] = m * d
            return carry

        if step < ITERS - 1:
            lax.fori_loop(0, strips, direct, 0)
        norm_now = norm_next
    r0 = pl.multiple_of(gy * tile_rows, tile_rows)
    c0 = pl.multiple_of(gx * tile_cols, tile_cols)
    height_out[...] = height_ref[pl.ds(r0, tile_rows), pl.ds(c0, tile_cols)]
    residual_out[...] = residual_ref[pl.ds(r0, tile_rows), pl.ds(c0, tile_cols)]


def solve_grid(both_stack, rounds):
    parts, _, tile_rows, tile_cols = both_stack.shape
    rows = lax.axis_size("gy") * tile_rows
    cols = lax.axis_size("gx") * tile_cols
    index = jnp.stack([lax.axis_index("gy"), lax.axis_index("gx")]).astype(jnp.int32)
    whole = pl.BlockSpec(memory_space=pltpu.VMEM)
    grid = pltpu.VMEM((rows, cols), jnp.float32)
    return pl.pallas_call(
        functools.partial(cg_kernel, rounds),
        in_specs=[pl.BlockSpec(memory_space=pltpu.SMEM), whole],
        out_specs=[whole, whole],
        out_shape=[jax.ShapeDtypeStruct((tile_rows, tile_cols), jnp.float32)] * 2,
        scratch_shapes=[grid, grid, grid, grid, pltpu.VMEM((rows + 16, cols), jnp.float32), grid, grid],
    )(index, both_stack)


def body(
    atm_state, atm_kappa, vert_weight, remap_src, remap_count, remap_weight, land_mask, ocean_term
):
    levels, tile_lat, tile_lon = atm_state.shape
    kappa = atm_kappa[:, None, None]
    count_gx = lax.axis_size("gx")
    count_gy = lax.axis_size("gy")
    rounds = gather_rounds()
    coded = jnp.where(land_mask != 0, ocean_term, -1.0)
    field, flux = diffuse(atm_state, atm_kappa, vert_weight)
    flux = flux.reshape(flux.shape[0], tile_lat * tile_lon)
    ocean_blocks, lists, width, _ = remap_weight.shape
    comps = vert_weight.shape[0]
    own_blocks = tile_lat * tile_lon // width
    blocks = flux.astype(jnp.bfloat16).reshape(comps, own_blocks, width).transpose(1, 0, 2)
    devices = count_gx * count_gy
    gx_index = lax.axis_index("gx")
    gy_index = lax.axis_index("gy")
    me_index = gx_index * count_gy + gy_index
    east_index = (gx_index + 1) % count_gx * count_gy + gy_index
    west_index = (gx_index + count_gx - 1) % count_gx * count_gy + gy_index
    entries = ocean_blocks * lists
    slots = 2 * land_mask.shape[0]
    src_all = remap_src.reshape(devices, entries)
    live_all = (
        jnp.arange(lists, dtype=jnp.int32)[None, None, :]
        < remap_count.reshape(devices, ocean_blocks)[:, :, None]
    ).reshape(devices, entries)
    owner_all = src_all // own_blocks
    inside_all = src_all % own_blocks
    mine_owner = lax.dynamic_slice_in_dim(owner_all, me_index, 1, 0)[0]
    mine_inside = lax.dynamic_slice_in_dim(inside_all, me_index, 1, 0)[0]
    mine_live = lax.dynamic_slice_in_dim(live_all, me_index, 1, 0)[0]
    from_east = mine_live & (mine_owner == east_index)
    from_self = mine_live & (mine_owner == me_index)
    local_part = blocks[jnp.where(from_self, mine_inside, 0)]
    west_owner = lax.dynamic_slice_in_dim(owner_all, west_index, 1, 0)[0]
    west_inside = lax.dynamic_slice_in_dim(inside_all, west_index, 1, 0)[0]
    west_live = lax.dynamic_slice_in_dim(live_all, west_index, 1, 0)[0]
    wanted = (west_live & (west_owner == me_index)).astype(jnp.int32)
    wanted_rank = jnp.cumsum(wanted) - 1
    slot_ids = jnp.arange(slots, dtype=jnp.int32)
    picker = wanted[None, :] * (wanted_rank[None, :] == slot_ids[:, None]).astype(jnp.int32)
    send_index = jnp.sum(picker * west_inside[None, :], axis=1)
    send_valid = jnp.sum(picker, axis=1).astype(jnp.bfloat16)
    outgoing = blocks[send_index] * send_valid[:, None, None]
    incoming = shifted(outgoing, "gx", -1)
    east_int = from_east.astype(jnp.int32)
    east_rank = jnp.cumsum(east_int) - 1
    remote_part = incoming[jnp.where(from_east, east_rank, 0)]
    gathered = jnp.where(
        from_self[:, None, None],
        local_part,
        jnp.where(from_east[:, None, None], remote_part, jnp.zeros_like(local_part)),
    )
    gathered = gathered.reshape(ocean_blocks, lists, comps, width)
    ocean_rows, ocean_cols = land_mask.shape
    remapped = jnp.einsum(
        "bkij,bkcj->cbi", remap_weight, gathered, preferred_element_type=jnp.float32
    )
    ocean_flux = remapped.reshape(comps, ocean_rows, ocean_cols)
    rhs_tile = land_mask.astype(jnp.float32) * (ocean_flux[0] + ocean_flux[1])
    both = stack_gather(jnp.stack([coded, rhs_tile]), rounds)
    height, residual = solve_grid(both, rounds)
    return (field, ocean_flux, height, residual)


def solution(mesh):
    return jax.shard_map(
        body,
        mesh=mesh,
        in_specs=(
            P(None, "gy", "gx"),
            P(),
            P(),
            P(),
            P(),
            P(("gx", "gy"), None, None, None),
            P("gy", "gx"),
            P("gy", "gx"),
        ),
        out_specs=(P(None, "gy", "gx"), P(None, "gy", "gx"), P("gy", "gx"), P("gy", "gx")),
        check_vma=False,
    )
```

```python
import functools

import jax
import jax.numpy as jnp
from jax import lax
from jax.sharding import PartitionSpec as P
from jax.experimental import pallas as pl
from jax.experimental.pallas import tpu as pltpu

STEPS = 4
ITERS = 3


def with_halo(x, sides, width):
    for axis, dim in sides:
        size, length = (lax.axis_size(axis), x.shape[dim])
        up = [(i, (i + 1) % size) for i in range(size - 1)]
        down = [(j, i) for i, j in up]
        last = lax.slice_in_dim(x, length - width, length, axis=dim)
        first = lax.slice_in_dim(x, 0, width, axis=dim)
        before = lax.ppermute(last, axis, up)
        after = lax.ppermute(first, axis, down)
        x = jnp.concatenate([before, x, after], axis=dim)
    return x


def shifted(x, axis, by):
    size = lax.axis_size(axis)
    return lax.ppermute(x, axis, [(i, (i + by) % size) for i in range(size)])


def ocean_operator(vector, maskf, ocean_term):
    padded = with_halo(maskf * vector, (("gx", 1), ("gy", 0)), 1)
    beside = padded[2:, 1:-1] + padded[:-2, 1:-1] + padded[1:-1, 2:] + padded[1:-1, :-2]
    return maskf * ((4.0 + ocean_term) * vector - beside) + (1.0 - maskf) * vector


def square_total(residual):
    return lax.psum(jnp.sum(residual * residual), ("gx", "gy"))


def gather_rounds():
    rounds = []
    for axis, bits in (("gy", lax.axis_size("gy")), ("gx", lax.axis_size("gx"))):
        distances = []
        d = 1
        while d < bits:
            distances.append(d)
            d *= 2
        rounds.append([(axis, d) for d in distances])
    gy_rounds, gx_rounds = rounds
    far = gy_rounds[1::2] + gx_rounds[2:]
    near = gy_rounds[0::2] + gx_rounds[1:2] + gx_rounds[:1]
    return far + near


def stack_gather(tile, rounds):
    x = tile[None]
    for axis, distance in rounds:
        size = lax.axis_size(axis)
        other = lax.ppermute(x, axis, [(j, j ^ distance) for j in range(size)])
        x = jnp.concatenate([x, other], axis=0)
    return x


def grid_operator(vector, maskf, ocean_term):
    padded = jnp.pad(maskf * vector, 1)
    beside = padded[2:, 1:-1] + padded[:-2, 1:-1] + padded[1:-1, 2:] + padded[1:-1, :-2]
    return maskf * ((4.0 + ocean_term) * vector - beside) + (1.0 - maskf) * vector


HALO = 4
LEVEL_BLOCK = 8


def diffusion_kernel(kappa_ref, weight_ref, core_ref, lanes_ref, rows_ref, mask_ref, out_ref, flux_ref, buf_a, buf_b):
    block = pl.program_id(0)
    height, levels, width = buf_a.shape
    rows = height - 2 * HALO
    cols = flux_ref.shape[2]

    @pl.when(block == 0)
    def _():
        flux_ref[...] = jnp.zeros_like(flux_ref)

    kappa = kappa_ref[...]
    weight = weight_ref[0]

    chunks = cols // 128
    wide = width // 128

    def load_core(q, carry):
        r = q - HALO
        pieces = [core_ref[pl.ds(r * chunks + k, levels, stride=rows * chunks), :] for k in range(chunks)]
        pieces.append(lanes_ref[pl.ds(r, levels, stride=rows), :])
        buf_a[q] = jnp.concatenate(pieces, axis=1)
        return carry

    lax.fori_loop(HALO, HALO + rows, load_core, 0)
    for h in range(2 * HALO):
        q = rows + HALO + h if h < HALO else h - HALO
        buf_a[q] = jnp.concatenate(
            [rows_ref[pl.ds(h * wide + k, levels, stride=2 * HALO * wide), :] for k in range(wide)], axis=1
        )

    def advance(src, q):
        cur = src[q]
        beside = (
            src[q + 1]
            + src[q - 1]
            + pltpu.roll(cur, width - 1, 1)
            + pltpu.roll(cur, 1, 1)
        )
        return (cur + kappa * (beside - 4.0 * cur)) * mask_ref[q]

    for step in range(1, STEPS):
        src, dst = (buf_a, buf_b) if step % 2 == 1 else (buf_b, buf_a)

        def one(q, carry, src=src, dst=dst):
            dst[q] = advance(src, q)
            return carry

        lax.fori_loop(step, height - step, one, 0, unroll=2)

    last = buf_b if STEPS % 2 == 0 else buf_a

    def final(q, carry):
        f = advance(last, q)[:, :cols]
        r = q - HALO
        for k in range(chunks):
            out_ref[pl.ds(r * chunks + k, levels, stride=rows * chunks), :] = f[:, k * 128 : (k + 1) * 128]
        flux_ref[r] += jnp.dot(weight, f, precision=lax.Precision.HIGHEST, preferred_element_type=jnp.float32)
        return carry

    lax.fori_loop(HALO, HALO + rows, final, 0, unroll=2)


def diffuse(field, atm_kappa, vert_weight):
    levels, rows, cols = field.shape
    comps = vert_weight.shape[0]
    count_gx = lax.axis_size("gx")
    count_gy = lax.axis_size("gy")
    gx_index = lax.axis_index("gx")
    gy_index = lax.axis_index("gy")
    up_gx = [(i, i + 1) for i in range(count_gx - 1)]
    down_gx = [(i + 1, i) for i in range(count_gx - 1)]
    up_gy = [(i, i + 1) for i in range(count_gy - 1)]
    down_gy = [(i + 1, i) for i in range(count_gy - 1)]
    pairs = lambda di, dj: [
        ((i + di) * count_gy + j + dj, i * count_gy + j)
        for i in range(count_gx)
        for j in range(count_gy)
        if 0 <= i + di < count_gx and 0 <= j + dj < count_gy
    ]
    both = ("gx", "gy")
    south = lax.ppermute(field[:, :HALO, :], "gy", down_gy)
    north = lax.ppermute(field[:, rows - HALO :, :], "gy", up_gy)
    east = lax.ppermute(field[:, :, :HALO], "gx", down_gx)
    west = lax.ppermute(field[:, :, cols - HALO :], "gx", up_gx)
    south_east = lax.ppermute(field[:, :HALO, :HALO], both, pairs(1, 1))
    south_west = lax.ppermute(field[:, :HALO, cols - HALO :], both, pairs(-1, 1))
    north_east = lax.ppermute(field[:, rows - HALO :, :HALO], both, pairs(1, -1))
    north_west = lax.ppermute(field[:, rows - HALO :, cols - HALO :], both, pairs(-1, -1))
    gap = jnp.zeros((levels, rows, 128 - 2 * HALO), field.dtype)
    lanes = jnp.concatenate([east, gap, west], axis=2)
    corner_gap = jnp.zeros((levels, HALO, 128 - 2 * HALO), field.dtype)
    halo_rows = jnp.concatenate(
        [
            jnp.concatenate([south, south_east, corner_gap, south_west], axis=2),
            jnp.concatenate([north, north_east, corner_gap, north_west], axis=2),
        ],
        axis=1,
    )
    height = rows + 2 * HALO
    width = cols + 128
    r = jnp.arange(height, dtype=jnp.int32)
    c = jnp.arange(width, dtype=jnp.int32)
    global_r = gy_index * rows + r - HALO
    global_c = gx_index * cols + jnp.where(c < cols + HALO, c, c - width)
    inside_r = (global_r >= 0) & (global_r < count_gy * rows)
    inside_c = (global_c >= 0) & (global_c < count_gx * cols) & ((c < cols + HALO) | (c >= width - HALO))
    mask = (inside_r[:, None] & inside_c[None, :]).astype(jnp.float32)
    mask = jnp.broadcast_to(mask[:, None, :], (height, LEVEL_BLOCK, width))
    blocks = levels // LEVEL_BLOCK
    kappa = jnp.broadcast_to(atm_kappa[:, None], (levels, width))
    weight = vert_weight.reshape(comps, blocks, LEVEL_BLOCK).transpose(1, 0, 2)
    out, flux = pl.pallas_call(
        diffusion_kernel,
        grid=(blocks,),
        in_specs=[
            pl.BlockSpec((LEVEL_BLOCK, width), lambda b: (b, 0)),
            pl.BlockSpec((1, comps, LEVEL_BLOCK), lambda b: (b, 0, 0)),
            pl.BlockSpec((LEVEL_BLOCK * rows * cols // 128, 128), lambda b: (b, 0)),
            pl.BlockSpec((LEVEL_BLOCK * rows, 128), lambda b: (b, 0)),
            pl.BlockSpec((LEVEL_BLOCK * 2 * HALO * width // 128, 128), lambda b: (b, 0)),
            pl.BlockSpec((height, LEVEL_BLOCK, width), lambda b: (0, 0, 0)),
        ],
        out_specs=[
            pl.BlockSpec((LEVEL_BLOCK * rows * cols // 128, 128), lambda b: (b, 0)),
            pl.BlockSpec((rows, comps, cols), lambda b: (0, 0, 0)),
        ],
        out_shape=[
            jax.ShapeDtypeStruct((levels * rows * cols // 128, 128), field.dtype),
            jax.ShapeDtypeStruct((rows, comps, cols), jnp.float32),
        ],
        scratch_shapes=[pltpu.VMEM((height, LEVEL_BLOCK, width), jnp.float32)] * 2,
        compiler_params=pltpu.CompilerParams(dimension_semantics=("arbitrary",)),
        cost_estimate=pl.CostEstimate(
            flops=levels * height * width * STEPS * 10,
            transcendentals=0,
            bytes_accessed=2 * field.size * 4,
        ),
    )(
        kappa,
        weight,
        field.reshape(levels * rows * cols // 128, 128),
        lanes.reshape(levels * rows, 128),
        halo_rows.reshape(levels * 2 * HALO * width // 128, 128),
        mask,
    )
    out = out.reshape(levels, rows, cols)
    flux = flux.transpose(1, 0, 2)
    return out, flux


def strip_sum(acc):
    return acc.sum(axis=0, keepdims=True).sum(axis=1, keepdims=True)


def cg_kernel(
    rounds, index_ref, rhs_stack, coded_stack, height_out, residual_out,
    rhs_ref, coded_ref, height_ref, residual_ref, pad_ref, dir_ref, img_ref,
):
    rows, cols = rhs_ref.shape
    tile_rows, tile_cols = height_out.shape
    gy = index_ref[0]
    gx = index_ref[1]

    def place(k, carry):
        gy_off = 0
        gx_off = 0
        for bit, (axis, distance) in enumerate(rounds):
            flag = lax.shift_right_logical(k, bit) & 1
            if axis == "gy":
                gy_off = gy_off + flag * distance
            else:
                gx_off = gx_off + flag * distance
        r0 = pl.multiple_of(lax.bitwise_xor(gy, gy_off) * tile_rows, tile_rows)
        c0 = pl.multiple_of(lax.bitwise_xor(gx, gx_off) * tile_cols, tile_cols)
        rhs_ref[pl.ds(r0, tile_rows), pl.ds(c0, tile_cols)] = rhs_stack[k]
        coded_ref[pl.ds(r0, tile_rows), pl.ds(c0, tile_cols)] = coded_stack[k]
        return carry

    lax.fori_loop(0, rhs_stack.shape[0], place, 0)
    strips = rows // 8
    zeros = jnp.zeros((8, cols), jnp.float32)
    pad_ref[0:8, :] = zeros
    pad_ref[rows + 8 : rows + 16, :] = zeros
    row = lax.broadcasted_iota(jnp.int32, (8, cols), 0)
    col = lax.broadcasted_iota(jnp.int32, (8, cols), 1)

    def at(k, offset=0):
        return pl.ds(pl.multiple_of(k * 8 + offset, 8), 8)

    def init(k, acc):
        v = rhs_ref[at(k), :]
        m = (coded_ref[at(k), :] >= 0.0).astype(jnp.float32)
        residual_ref[at(k), :] = v
        dir_ref[at(k), :] = v
        height_ref[at(k), :] = jnp.zeros_like(v)
        pad_ref[at(k, 8), :] = m * v
        return acc + v * v

    def image(k, acc):
        prev = pad_ref[at(k), :]
        cur = pad_ref[at(k, 8), :]
        nxt = pad_ref[at(k, 16), :]
        south = jnp.where(row == 7, pltpu.roll(nxt, 7, 0), pltpu.roll(cur, 7, 0))
        north = jnp.where(row == 0, pltpu.roll(prev, 1, 0), pltpu.roll(cur, 1, 0))
        east = jnp.where(col == cols - 1, 0.0, pltpu.roll(cur, cols - 1, 1))
        west = jnp.where(col == 0, 0.0, pltpu.roll(cur, 1, 1))
        beside = south + north + east + west
        ot = coded_ref[at(k), :]
        m = (ot >= 0.0).astype(jnp.float32)
        v = dir_ref[at(k), :]
        w = m * ((4.0 + ot) * v - beside) + (1.0 - m) * v
        img_ref[at(k), :] = w
        return acc + v * w

    norm_now = strip_sum(lax.fori_loop(0, strips, init, zeros))
    for step in range(ITERS):
        alpha = norm_now / strip_sum(lax.fori_loop(0, strips, image, zeros))

        def update(k, acc):
            v = dir_ref[at(k), :]
            height_ref[at(k), :] = height_ref[at(k), :] + alpha * v
            r = residual_ref[at(k), :] - alpha * img_ref[at(k), :]
            residual_ref[at(k), :] = r
            return acc + r * r

        norm_next = strip_sum(lax.fori_loop(0, strips, update, zeros))
        beta = norm_next / norm_now

        def direct(k, carry):
            d = residual_ref[at(k), :] + beta * dir_ref[at(k), :]
            dir_ref[at(k), :] = d
            m = (coded_ref[at(k), :] >= 0.0).astype(jnp.float32)
            pad_ref[at(k, 8), :] = m * d
            return carry

        if step < ITERS - 1:
            lax.fori_loop(0, strips, direct, 0)
        norm_now = norm_next
    r0 = pl.multiple_of(gy * tile_rows, tile_rows)
    c0 = pl.multiple_of(gx * tile_cols, tile_cols)
    height_out[...] = height_ref[pl.ds(r0, tile_rows), pl.ds(c0, tile_cols)]
    residual_out[...] = residual_ref[pl.ds(r0, tile_rows), pl.ds(c0, tile_cols)]


def solve_grid(rhs_stack, coded_stack, rounds):
    parts, tile_rows, tile_cols = rhs_stack.shape
    rows = lax.axis_size("gy") * tile_rows
    cols = lax.axis_size("gx") * tile_cols
    index = jnp.stack([lax.axis_index("gy"), lax.axis_index("gx")]).astype(jnp.int32)
    whole = pl.BlockSpec(memory_space=pltpu.VMEM)
    grid = pltpu.VMEM((rows, cols), jnp.float32)
    return pl.pallas_call(
        functools.partial(cg_kernel, rounds),
        in_specs=[pl.BlockSpec(memory_space=pltpu.SMEM), whole, whole],
        out_specs=[whole, whole],
        out_shape=[jax.ShapeDtypeStruct((tile_rows, tile_cols), jnp.float32)] * 2,
        scratch_shapes=[grid, grid, grid, grid, pltpu.VMEM((rows + 16, cols), jnp.float32), grid, grid],
    )(index, rhs_stack, coded_stack)


def body(
    atm_state, atm_kappa, vert_weight, remap_src, remap_count, remap_weight, land_mask, ocean_term
):
    levels, tile_lat, tile_lon = atm_state.shape
    kappa = atm_kappa[:, None, None]
    count_gx = lax.axis_size("gx")
    count_gy = lax.axis_size("gy")
    rounds = gather_rounds()
    coded_all = stack_gather(jnp.where(land_mask != 0, ocean_term, -1.0), rounds)
    field, flux = diffuse(atm_state, atm_kappa, vert_weight)
    flux = flux.reshape(flux.shape[0], tile_lat * tile_lon)
    ocean_blocks, lists, width, _ = remap_weight.shape
    comps = vert_weight.shape[0]
    own_blocks = tile_lat * tile_lon // width
    blocks = flux.astype(jnp.bfloat16).reshape(comps, own_blocks, width).transpose(1, 0, 2)
    devices = count_gx * count_gy
    gx_index = lax.axis_index("gx")
    gy_index = lax.axis_index("gy")
    me_index = gx_index * count_gy + gy_index
    east_index = (gx_index + 1) % count_gx * count_gy + gy_index
    west_index = (gx_index + count_gx - 1) % count_gx * count_gy + gy_index
    entries = ocean_blocks * lists
    slots = 2 * land_mask.shape[0]
    src_all = remap_src.reshape(devices, entries)
    live_all = (
        jnp.arange(lists, dtype=jnp.int32)[None, None, :]
        < remap_count.reshape(devices, ocean_blocks)[:, :, None]
    ).reshape(devices, entries)
    owner_all = src_all // own_blocks
    inside_all = src_all % own_blocks
    mine_owner = lax.dynamic_slice_in_dim(owner_all, me_index, 1, 0)[0]
    mine_inside = lax.dynamic_slice_in_dim(inside_all, me_index, 1, 0)[0]
    mine_live = lax.dynamic_slice_in_dim(live_all, me_index, 1, 0)[0]
    from_east = mine_live & (mine_owner == east_index)
    from_self = mine_live & (mine_owner == me_index)
    local_part = blocks[jnp.where(from_self, mine_inside, 0)]
    west_owner = lax.dynamic_slice_in_dim(owner_all, west_index, 1, 0)[0]
    west_inside = lax.dynamic_slice_in_dim(inside_all, west_index, 1, 0)[0]
    west_live = lax.dynamic_slice_in_dim(live_all, west_index, 1, 0)[0]
    wanted = (west_live & (west_owner == me_index)).astype(jnp.int32)
    wanted_rank = jnp.cumsum(wanted) - 1
    slot_ids = jnp.arange(slots, dtype=jnp.int32)
    picker = wanted[None, :] * (wanted_rank[None, :] == slot_ids[:, None]).astype(jnp.int32)
    send_index = jnp.sum(picker * west_inside[None, :], axis=1)
    send_valid = jnp.sum(picker, axis=1).astype(jnp.bfloat16)
    outgoing = blocks[send_index] * send_valid[:, None, None]
    incoming = shifted(outgoing, "gx", -1)
    east_int = from_east.astype(jnp.int32)
    east_rank = jnp.cumsum(east_int) - 1
    remote_part = incoming[jnp.where(from_east, east_rank, 0)]
    gathered = jnp.where(
        from_self[:, None, None],
        local_part,
        jnp.where(from_east[:, None, None], remote_part, jnp.zeros_like(local_part)),
    )
    gathered = gathered.reshape(ocean_blocks, lists, comps, width)
    ocean_rows, ocean_cols = land_mask.shape
    remapped = jnp.einsum(
        "bkij,bkcj->cbi", remap_weight, gathered, preferred_element_type=jnp.float32
    )
    ocean_flux = remapped.reshape(comps, ocean_rows, ocean_cols)
    rhs_tile = land_mask.astype(jnp.float32) * (ocean_flux[0] + ocean_flux[1])
    rhs = stack_gather(rhs_tile, rounds)
    height, residual = solve_grid(rhs, coded_all, rounds)
    return (field, ocean_flux, height, residual)


def solution(mesh):
    return jax.shard_map(
        body,
        mesh=mesh,
        in_specs=(
            P(None, "gy", "gx"),
            P(),
            P(),
            P(),
            P(),
            P(("gx", "gy"), None, None, None),
            P("gy", "gx"),
            P("gy", "gx"),
        ),
        out_specs=(P(None, "gy", "gx"), P(None, "gy", "gx"), P("gy", "gx"), P("gy", "gx")),
        check_vma=False,
    )
```

```python
import functools

import jax
import jax.numpy as jnp
from jax import lax
from jax.sharding import PartitionSpec as P
from jax.experimental import pallas as pl
from jax.experimental.pallas import tpu as pltpu

STEPS = 4
ITERS = 3


def with_halo(x, sides, width):
    for axis, dim in sides:
        size, length = (lax.axis_size(axis), x.shape[dim])
        up = [(i, (i + 1) % size) for i in range(size - 1)]
        down = [(j, i) for i, j in up]
        last = lax.slice_in_dim(x, length - width, length, axis=dim)
        first = lax.slice_in_dim(x, 0, width, axis=dim)
        before = lax.ppermute(last, axis, up)
        after = lax.ppermute(first, axis, down)
        x = jnp.concatenate([before, x, after], axis=dim)
    return x


def shifted(x, axis, by):
    size = lax.axis_size(axis)
    return lax.ppermute(x, axis, [(i, (i + by) % size) for i in range(size)])


def ocean_operator(vector, maskf, ocean_term):
    padded = with_halo(maskf * vector, (("gx", 1), ("gy", 0)), 1)
    beside = padded[2:, 1:-1] + padded[:-2, 1:-1] + padded[1:-1, 2:] + padded[1:-1, :-2]
    return maskf * ((4.0 + ocean_term) * vector - beside) + (1.0 - maskf) * vector


def square_total(residual):
    return lax.psum(jnp.sum(residual * residual), ("gx", "gy"))


def gather_rounds():
    rounds = []
    for axis, bits in (("gy", lax.axis_size("gy")), ("gx", lax.axis_size("gx"))):
        distances = []
        d = 1
        while d < bits:
            distances.append(d)
            d *= 2
        rounds.append([(axis, d) for d in distances])
    gy_rounds, gx_rounds = rounds
    far = gy_rounds[1::2] + gx_rounds[2:]
    near = gy_rounds[0::2] + gx_rounds[1:2] + gx_rounds[:1]
    return far + near


def stack_gather(tile, rounds):
    x = tile[None]
    for axis, distance in rounds:
        size = lax.axis_size(axis)
        other = lax.ppermute(x, axis, [(j, j ^ distance) for j in range(size)])
        x = jnp.concatenate([x, other], axis=0)
    return x


def grid_operator(vector, maskf, ocean_term):
    padded = jnp.pad(maskf * vector, 1)
    beside = padded[2:, 1:-1] + padded[:-2, 1:-1] + padded[1:-1, 2:] + padded[1:-1, :-2]
    return maskf * ((4.0 + ocean_term) * vector - beside) + (1.0 - maskf) * vector


HALO = 4
LEVEL_BLOCK = 16


def diffusion_kernel(kappa_ref, weight_ref, core_ref, lanes_ref, rows_ref, mask_ref, out_ref, flux_ref):
    block = pl.program_id(0)
    levels, rows, cols = core_ref.shape

    @pl.when(block == 0)
    def _():
        flux_ref[...] = jnp.zeros_like(flux_ref)

    mask = mask_ref[...]
    mask_side = mask[:rows, cols:]
    mask_low = mask[rows:, :]

    def level(l, carry):
        lev = block * levels + l
        kappa = kappa_ref[lev]
        top = jnp.concatenate([core_ref[l], lanes_ref[l]], axis=1)
        f = jnp.concatenate([top, rows_ref[l]], axis=0)
        height, width = f.shape
        for step in range(STEPS):
            beside = (
                pltpu.roll(f, height - 1, 0)
                + pltpu.roll(f, 1, 0)
                + pltpu.roll(f, width - 1, 1)
                + pltpu.roll(f, 1, 1)
            )
            f = f + kappa * (beside - 4.0 * f)
            top = jnp.concatenate([f[:rows, :cols], f[:rows, cols:] * mask_side], axis=1)
            f = jnp.concatenate([top, f[rows:, :] * mask_low], axis=0)
        core = f[:rows, :cols]
        out_ref[l] = core
        for c in range(flux_ref.shape[0]):
            flux_ref[c] += weight_ref[c, lev] * core
        return carry

    lax.fori_loop(0, levels, level, 0, unroll=2)


def diffuse(field, atm_kappa, vert_weight):
    levels, rows, cols = field.shape
    comps = vert_weight.shape[0]
    count_gx = lax.axis_size("gx")
    count_gy = lax.axis_size("gy")
    gx_index = lax.axis_index("gx")
    gy_index = lax.axis_index("gy")
    up_gx = [(i, i + 1) for i in range(count_gx - 1)]
    down_gx = [(i + 1, i) for i in range(count_gx - 1)]
    up_gy = [(i, i + 1) for i in range(count_gy - 1)]
    down_gy = [(i + 1, i) for i in range(count_gy - 1)]
    pairs = lambda di, dj: [
        ((i + di) * count_gy + j + dj, i * count_gy + j)
        for i in range(count_gx)
        for j in range(count_gy)
        if 0 <= i + di < count_gx and 0 <= j + dj < count_gy
    ]
    both = ("gx", "gy")
    south = lax.ppermute(field[:, :HALO, :], "gy", down_gy)
    north = lax.ppermute(field[:, rows - HALO :, :], "gy", up_gy)
    east = lax.ppermute(field[:, :, :HALO], "gx", down_gx)
    west = lax.ppermute(field[:, :, cols - HALO :], "gx", up_gx)
    south_east = lax.ppermute(field[:, :HALO, :HALO], both, pairs(1, 1))
    south_west = lax.ppermute(field[:, :HALO, cols - HALO :], both, pairs(-1, 1))
    north_east = lax.ppermute(field[:, rows - HALO :, :HALO], both, pairs(1, -1))
    north_west = lax.ppermute(field[:, rows - HALO :, cols - HALO :], both, pairs(-1, -1))
    gap = jnp.zeros((levels, rows, 128 - 2 * HALO), field.dtype)
    lanes = jnp.concatenate([east, gap, west], axis=2)
    corner_gap = jnp.zeros((levels, HALO, 128 - 2 * HALO), field.dtype)
    halo_rows = jnp.concatenate(
        [
            jnp.concatenate([south, south_east, corner_gap, south_west], axis=2),
            jnp.concatenate([north, north_east, corner_gap, north_west], axis=2),
        ],
        axis=1,
    )
    height = rows + 2 * HALO
    width = cols + 128
    r = jnp.arange(height, dtype=jnp.int32)
    c = jnp.arange(width, dtype=jnp.int32)
    global_r = gy_index * rows + jnp.where(r < rows + HALO, r, r - height)
    global_c = gx_index * cols + jnp.where(c < cols + HALO, c, c - width)
    inside_r = (global_r >= 0) & (global_r < count_gy * rows)
    inside_c = (global_c >= 0) & (global_c < count_gx * cols) & ((c < cols + HALO) | (c >= width - HALO))
    mask = (inside_r[:, None] & inside_c[None, :]).astype(jnp.float32)
    blocks = levels // LEVEL_BLOCK
    smem = pl.BlockSpec(memory_space=pltpu.SMEM)
    out, flux = pl.pallas_call(
        diffusion_kernel,
        grid=(blocks,),
        in_specs=[
            smem,
            smem,
            pl.BlockSpec((LEVEL_BLOCK, rows, cols), lambda b: (b, 0, 0)),
            pl.BlockSpec((LEVEL_BLOCK, rows, 128), lambda b: (b, 0, 0)),
            pl.BlockSpec((LEVEL_BLOCK, 2 * HALO, width), lambda b: (b, 0, 0)),
            pl.BlockSpec((height, width), lambda b: (0, 0)),
        ],
        out_specs=[
            pl.BlockSpec((LEVEL_BLOCK, rows, cols), lambda b: (b, 0, 0)),
            pl.BlockSpec((comps, rows, cols), lambda b: (0, 0, 0)),
        ],
        out_shape=[
            jax.ShapeDtypeStruct(field.shape, field.dtype),
            jax.ShapeDtypeStruct((comps, rows, cols), jnp.float32),
        ],
        compiler_params=pltpu.CompilerParams(dimension_semantics=("arbitrary",)),
        cost_estimate=pl.CostEstimate(
            flops=levels * height * width * STEPS * 10,
            transcendentals=0,
            bytes_accessed=2 * field.size * 4,
        ),
    )(atm_kappa, vert_weight, field, lanes, halo_rows, mask)
    return out, flux


def strip_sum(acc):
    return acc.sum(axis=0, keepdims=True).sum(axis=1, keepdims=True)


def cg_kernel(
    rounds, index_ref, rhs_stack, coded_stack, height_out, residual_out,
    rhs_ref, coded_ref, height_ref, residual_ref, pad_ref, dir_ref, img_ref,
):
    rows, cols = rhs_ref.shape
    tile_rows, tile_cols = height_out.shape
    gy = index_ref[0]
    gx = index_ref[1]

    def place(k, carry):
        gy_off = 0
        gx_off = 0
        for bit, (axis, distance) in enumerate(rounds):
            flag = lax.shift_right_logical(k, bit) & 1
            if axis == "gy":
                gy_off = gy_off + flag * distance
            else:
                gx_off = gx_off + flag * distance
        r0 = pl.multiple_of(lax.bitwise_xor(gy, gy_off) * tile_rows, tile_rows)
        c0 = pl.multiple_of(lax.bitwise_xor(gx, gx_off) * tile_cols, tile_cols)
        rhs_ref[pl.ds(r0, tile_rows), pl.ds(c0, tile_cols)] = rhs_stack[k]
        coded_ref[pl.ds(r0, tile_rows), pl.ds(c0, tile_cols)] = coded_stack[k]
        return carry

    lax.fori_loop(0, rhs_stack.shape[0], place, 0)
    strips = rows // 8
    zeros = jnp.zeros((8, cols), jnp.float32)
    pad_ref[0:8, :] = zeros
    pad_ref[rows + 8 : rows + 16, :] = zeros
    row = lax.broadcasted_iota(jnp.int32, (8, cols), 0)
    col = lax.broadcasted_iota(jnp.int32, (8, cols), 1)

    def at(k, offset=0):
        return pl.ds(pl.multiple_of(k * 8 + offset, 8), 8)

    def init(k, acc):
        v = rhs_ref[at(k), :]
        m = (coded_ref[at(k), :] >= 0.0).astype(jnp.float32)
        residual_ref[at(k), :] = v
        dir_ref[at(k), :] = v
        height_ref[at(k), :] = jnp.zeros_like(v)
        pad_ref[at(k, 8), :] = m * v
        return acc + v * v

    def image(k, acc):
        prev = pad_ref[at(k), :]
        cur = pad_ref[at(k, 8), :]
        nxt = pad_ref[at(k, 16), :]
        south = jnp.where(row == 7, pltpu.roll(nxt, 7, 0), pltpu.roll(cur, 7, 0))
        north = jnp.where(row == 0, pltpu.roll(prev, 1, 0), pltpu.roll(cur, 1, 0))
        east = jnp.where(col == cols - 1, 0.0, pltpu.roll(cur, cols - 1, 1))
        west = jnp.where(col == 0, 0.0, pltpu.roll(cur, 1, 1))
        beside = south + north + east + west
        ot = coded_ref[at(k), :]
        m = (ot >= 0.0).astype(jnp.float32)
        v = dir_ref[at(k), :]
        w = m * ((4.0 + ot) * v - beside) + (1.0 - m) * v
        img_ref[at(k), :] = w
        return acc + v * w

    norm_now = strip_sum(lax.fori_loop(0, strips, init, zeros))
    for step in range(ITERS):
        alpha = norm_now / strip_sum(lax.fori_loop(0, strips, image, zeros))

        def update(k, acc):
            v = dir_ref[at(k), :]
            height_ref[at(k), :] = height_ref[at(k), :] + alpha * v
            r = residual_ref[at(k), :] - alpha * img_ref[at(k), :]
            residual_ref[at(k), :] = r
            return acc + r * r

        norm_next = strip_sum(lax.fori_loop(0, strips, update, zeros))
        beta = norm_next / norm_now

        def direct(k, carry):
            d = residual_ref[at(k), :] + beta * dir_ref[at(k), :]
            dir_ref[at(k), :] = d
            m = (coded_ref[at(k), :] >= 0.0).astype(jnp.float32)
            pad_ref[at(k, 8), :] = m * d
            return carry

        if step < ITERS - 1:
            lax.fori_loop(0, strips, direct, 0)
        norm_now = norm_next
    r0 = pl.multiple_of(gy * tile_rows, tile_rows)
    c0 = pl.multiple_of(gx * tile_cols, tile_cols)
    height_out[...] = height_ref[pl.ds(r0, tile_rows), pl.ds(c0, tile_cols)]
    residual_out[...] = residual_ref[pl.ds(r0, tile_rows), pl.ds(c0, tile_cols)]


def solve_grid(rhs_stack, coded_stack, rounds):
    parts, tile_rows, tile_cols = rhs_stack.shape
    rows = lax.axis_size("gy") * tile_rows
    cols = lax.axis_size("gx") * tile_cols
    index = jnp.stack([lax.axis_index("gy"), lax.axis_index("gx")]).astype(jnp.int32)
    whole = pl.BlockSpec(memory_space=pltpu.VMEM)
    grid = pltpu.VMEM((rows, cols), jnp.float32)
    return pl.pallas_call(
        functools.partial(cg_kernel, rounds),
        in_specs=[pl.BlockSpec(memory_space=pltpu.SMEM), whole, whole],
        out_specs=[whole, whole],
        out_shape=[jax.ShapeDtypeStruct((tile_rows, tile_cols), jnp.float32)] * 2,
        scratch_shapes=[grid, grid, grid, grid, pltpu.VMEM((rows + 16, cols), jnp.float32), grid, grid],
    )(index, rhs_stack, coded_stack)


def body(
    atm_state, atm_kappa, vert_weight, remap_src, remap_count, remap_weight, land_mask, ocean_term
):
    levels, tile_lat, tile_lon = atm_state.shape
    kappa = atm_kappa[:, None, None]
    count_gx = lax.axis_size("gx")
    count_gy = lax.axis_size("gy")
    rounds = gather_rounds()
    coded_all = stack_gather(jnp.where(land_mask != 0, ocean_term, -1.0), rounds)
    field, flux = diffuse(atm_state, atm_kappa, vert_weight)
    flux = flux.reshape(flux.shape[0], tile_lat * tile_lon)
    ocean_blocks, lists, width, _ = remap_weight.shape
    comps = vert_weight.shape[0]
    own_blocks = tile_lat * tile_lon // width
    blocks = flux.astype(jnp.bfloat16).reshape(comps, own_blocks, width).transpose(1, 0, 2)
    devices = count_gx * count_gy
    gx_index = lax.axis_index("gx")
    gy_index = lax.axis_index("gy")
    me_index = gx_index * count_gy + gy_index
    east_index = (gx_index + 1) % count_gx * count_gy + gy_index
    west_index = (gx_index + count_gx - 1) % count_gx * count_gy + gy_index
    entries = ocean_blocks * lists
    slots = 2 * land_mask.shape[0]
    src_all = remap_src.reshape(devices, entries)
    live_all = (
        jnp.arange(lists, dtype=jnp.int32)[None, None, :]
        < remap_count.reshape(devices, ocean_blocks)[:, :, None]
    ).reshape(devices, entries)
    owner_all = src_all // own_blocks
    inside_all = src_all % own_blocks
    mine_owner = lax.dynamic_slice_in_dim(owner_all, me_index, 1, 0)[0]
    mine_inside = lax.dynamic_slice_in_dim(inside_all, me_index, 1, 0)[0]
    mine_live = lax.dynamic_slice_in_dim(live_all, me_index, 1, 0)[0]
    from_east = mine_live & (mine_owner == east_index)
    from_self = mine_live & (mine_owner == me_index)
    local_part = blocks[jnp.where(from_self, mine_inside, 0)]
    west_owner = lax.dynamic_slice_in_dim(owner_all, west_index, 1, 0)[0]
    west_inside = lax.dynamic_slice_in_dim(inside_all, west_index, 1, 0)[0]
    west_live = lax.dynamic_slice_in_dim(live_all, west_index, 1, 0)[0]
    wanted = (west_live & (west_owner == me_index)).astype(jnp.int32)
    wanted_rank = jnp.cumsum(wanted) - 1
    slot_ids = jnp.arange(slots, dtype=jnp.int32)
    picker = wanted[None, :] * (wanted_rank[None, :] == slot_ids[:, None]).astype(jnp.int32)
    send_index = jnp.sum(picker * west_inside[None, :], axis=1)
    send_valid = jnp.sum(picker, axis=1).astype(jnp.bfloat16)
    outgoing = blocks[send_index] * send_valid[:, None, None]
    incoming = shifted(outgoing, "gx", -1)
    east_int = from_east.astype(jnp.int32)
    east_rank = jnp.cumsum(east_int) - 1
    remote_part = incoming[jnp.where(from_east, east_rank, 0)]
    gathered = jnp.where(
        from_self[:, None, None],
        local_part,
        jnp.where(from_east[:, None, None], remote_part, jnp.zeros_like(local_part)),
    )
    gathered = gathered.reshape(ocean_blocks, lists, comps, width)
    ocean_rows, ocean_cols = land_mask.shape
    remapped = jnp.einsum(
        "bkij,bkcj->cbi", remap_weight, gathered, preferred_element_type=jnp.float32
    )
    ocean_flux = remapped.reshape(comps, ocean_rows, ocean_cols)
    rhs_tile = land_mask.astype(jnp.float32) * (ocean_flux[0] + ocean_flux[1])
    rhs = stack_gather(rhs_tile, rounds)
    height, residual = solve_grid(rhs, coded_all, rounds)
    return (field, ocean_flux, height, residual)


def solution(mesh):
    return jax.shard_map(
        body,
        mesh=mesh,
        in_specs=(
            P(None, "gy", "gx"),
            P(),
            P(),
            P(),
            P(),
            P(("gx", "gy"), None, None, None),
            P("gy", "gx"),
            P("gy", "gx"),
        ),
        out_specs=(P(None, "gy", "gx"), P(None, "gy", "gx"), P("gy", "gx"), P("gy", "gx")),
        check_vma=False,
    )
```

```python
import functools

import jax
import jax.numpy as jnp
from jax import lax
from jax.sharding import PartitionSpec as P
from jax.experimental import pallas as pl
from jax.experimental.pallas import tpu as pltpu

STEPS = 4
ITERS = 3


def with_halo(x, sides, width):
    for axis, dim in sides:
        size, length = (lax.axis_size(axis), x.shape[dim])
        up = [(i, (i + 1) % size) for i in range(size - 1)]
        down = [(j, i) for i, j in up]
        last = lax.slice_in_dim(x, length - width, length, axis=dim)
        first = lax.slice_in_dim(x, 0, width, axis=dim)
        before = lax.ppermute(last, axis, up)
        after = lax.ppermute(first, axis, down)
        x = jnp.concatenate([before, x, after], axis=dim)
    return x


def shifted(x, axis, by):
    size = lax.axis_size(axis)
    return lax.ppermute(x, axis, [(i, (i + by) % size) for i in range(size)])


def ocean_operator(vector, maskf, ocean_term):
    padded = with_halo(maskf * vector, (("gx", 1), ("gy", 0)), 1)
    beside = padded[2:, 1:-1] + padded[:-2, 1:-1] + padded[1:-1, 2:] + padded[1:-1, :-2]
    return maskf * ((4.0 + ocean_term) * vector - beside) + (1.0 - maskf) * vector


def square_total(residual):
    return lax.psum(jnp.sum(residual * residual), ("gx", "gy"))


def gather_rounds():
    rounds = []
    for axis, bits in (("gy", lax.axis_size("gy")), ("gx", lax.axis_size("gx"))):
        distances = []
        d = 1
        while d < bits:
            distances.append(d)
            d *= 2
        rounds.append([(axis, d) for d in distances])
    gy_rounds, gx_rounds = rounds
    far = gy_rounds[1::2] + gx_rounds[2:]
    near = gy_rounds[0::2] + gx_rounds[1:2] + gx_rounds[:1]
    return far + near


def stack_gather(tile, rounds):
    x = tile[None]
    for axis, distance in rounds:
        size = lax.axis_size(axis)
        other = lax.ppermute(x, axis, [(j, j ^ distance) for j in range(size)])
        x = jnp.concatenate([x, other], axis=0)
    return x


def grid_operator(vector, maskf, ocean_term):
    padded = jnp.pad(maskf * vector, 1)
    beside = padded[2:, 1:-1] + padded[:-2, 1:-1] + padded[1:-1, 2:] + padded[1:-1, :-2]
    return maskf * ((4.0 + ocean_term) * vector - beside) + (1.0 - maskf) * vector


HALO = 4
LEVEL_BLOCK = 16


def diffusion_kernel(kappa_ref, weight_ref, core_ref, lanes_ref, rows_ref, mask_ref, out_ref, flux_ref):
    block = pl.program_id(0)
    levels, rows, cols = core_ref.shape

    @pl.when(block == 0)
    def _():
        flux_ref[...] = jnp.zeros_like(flux_ref)

    mask = mask_ref[...]
    mask_side = mask[:rows, cols:]
    mask_low = mask[rows:, :]

    def level(l, carry):
        lev = block * levels + l
        kappa = kappa_ref[lev]
        top = jnp.concatenate([core_ref[l], lanes_ref[l]], axis=1)
        f = jnp.concatenate([top, rows_ref[l]], axis=0)
        height, width = f.shape
        for step in range(STEPS):
            beside = (
                pltpu.roll(f, height - 1, 0)
                + pltpu.roll(f, 1, 0)
                + pltpu.roll(f, width - 1, 1)
                + pltpu.roll(f, 1, 1)
            )
            f = f + kappa * (beside - 4.0 * f)
            top = jnp.concatenate([f[:rows, :cols], f[:rows, cols:] * mask_side], axis=1)
            f = jnp.concatenate([top, f[rows:, :] * mask_low], axis=0)
        core = f[:rows, :cols]
        out_ref[l] = core
        for c in range(flux_ref.shape[0]):
            flux_ref[c] += weight_ref[c, lev] * core
        return carry

    lax.fori_loop(0, levels, level, 0, unroll=2)


def diffuse(field, core, atm_kappa, vert_weight):
    levels, rows, cols = field.shape
    comps = vert_weight.shape[0]
    count_gx = lax.axis_size("gx")
    count_gy = lax.axis_size("gy")
    gx_index = lax.axis_index("gx")
    gy_index = lax.axis_index("gy")
    up_gx = [(i, i + 1) for i in range(count_gx - 1)]
    down_gx = [(i + 1, i) for i in range(count_gx - 1)]
    up_gy = [(i, i + 1) for i in range(count_gy - 1)]
    down_gy = [(i + 1, i) for i in range(count_gy - 1)]
    pairs = lambda di, dj: [
        ((i + di) * count_gy + j + dj, i * count_gy + j)
        for i in range(count_gx)
        for j in range(count_gy)
        if 0 <= i + di < count_gx and 0 <= j + dj < count_gy
    ]
    both = ("gx", "gy")
    south = lax.ppermute(field[:, :HALO, :], "gy", down_gy)
    north = lax.ppermute(field[:, rows - HALO :, :], "gy", up_gy)
    east = lax.ppermute(field[:, :, :HALO], "gx", down_gx)
    west = lax.ppermute(field[:, :, cols - HALO :], "gx", up_gx)
    south_east = lax.ppermute(field[:, :HALO, :HALO], both, pairs(1, 1))
    south_west = lax.ppermute(field[:, :HALO, cols - HALO :], both, pairs(-1, 1))
    north_east = lax.ppermute(field[:, rows - HALO :, :HALO], both, pairs(1, -1))
    north_west = lax.ppermute(field[:, rows - HALO :, cols - HALO :], both, pairs(-1, -1))
    gap = jnp.zeros((levels, rows, 128 - 2 * HALO), field.dtype)
    lanes = jnp.concatenate([east, gap, west], axis=2)
    corner_gap = jnp.zeros((levels, HALO, 128 - 2 * HALO), field.dtype)
    halo_rows = jnp.concatenate(
        [
            jnp.concatenate([south, south_east, corner_gap, south_west], axis=2),
            jnp.concatenate([north, north_east, corner_gap, north_west], axis=2),
        ],
        axis=1,
    )
    height = rows + 2 * HALO
    width = cols + 128
    r = jnp.arange(height, dtype=jnp.int32)
    c = jnp.arange(width, dtype=jnp.int32)
    global_r = gy_index * rows + jnp.where(r < rows + HALO, r, r - height)
    global_c = gx_index * cols + jnp.where(c < cols + HALO, c, c - width)
    inside_r = (global_r >= 0) & (global_r < count_gy * rows)
    inside_c = (global_c >= 0) & (global_c < count_gx * cols) & ((c < cols + HALO) | (c >= width - HALO))
    mask = (inside_r[:, None] & inside_c[None, :]).astype(jnp.float32)
    blocks = levels // LEVEL_BLOCK
    smem = pl.BlockSpec(memory_space=pltpu.SMEM)
    out, flux = pl.pallas_call(
        diffusion_kernel,
        grid=(blocks,),
        in_specs=[
            smem,
            smem,
            pl.BlockSpec((LEVEL_BLOCK, rows, cols), lambda b: (b, 0, 0)),
            pl.BlockSpec((LEVEL_BLOCK, rows, 128), lambda b: (b, 0, 0)),
            pl.BlockSpec((LEVEL_BLOCK, 2 * HALO, width), lambda b: (b, 0, 0)),
            pl.BlockSpec((height, width), lambda b: (0, 0)),
        ],
        out_specs=[
            pl.BlockSpec((LEVEL_BLOCK, rows, cols), lambda b: (b, 0, 0)),
            pl.BlockSpec((comps, rows, cols), lambda b: (0, 0, 0)),
        ],
        out_shape=[
            jax.ShapeDtypeStruct(field.shape, field.dtype),
            jax.ShapeDtypeStruct((comps, rows, cols), jnp.float32),
        ],
        compiler_params=pltpu.CompilerParams(dimension_semantics=("arbitrary",)),
        cost_estimate=pl.CostEstimate(
            flops=levels * height * width * STEPS * 10,
            transcendentals=0,
            bytes_accessed=2 * field.size * 4,
        ),
    )(atm_kappa, vert_weight, core, lanes, halo_rows, mask)
    return out, flux


def strip_sum(acc):
    return acc.sum(axis=0, keepdims=True).sum(axis=1, keepdims=True)


def cg_kernel(
    rounds, index_ref, rhs_stack, coded_stack, height_out, residual_out,
    rhs_ref, coded_ref, height_ref, residual_ref, pad_ref, dir_ref, img_ref,
):
    rows, cols = rhs_ref.shape
    tile_rows, tile_cols = height_out.shape
    gy = index_ref[0]
    gx = index_ref[1]

    def place(k, carry):
        gy_off = 0
        gx_off = 0
        for bit, (axis, distance) in enumerate(rounds):
            flag = lax.shift_right_logical(k, bit) & 1
            if axis == "gy":
                gy_off = gy_off + flag * distance
            else:
                gx_off = gx_off + flag * distance
        r0 = pl.multiple_of(lax.bitwise_xor(gy, gy_off) * tile_rows, tile_rows)
        c0 = pl.multiple_of(lax.bitwise_xor(gx, gx_off) * tile_cols, tile_cols)
        rhs_ref[pl.ds(r0, tile_rows), pl.ds(c0, tile_cols)] = rhs_stack[k]
        coded_ref[pl.ds(r0, tile_rows), pl.ds(c0, tile_cols)] = coded_stack[k]
        return carry

    lax.fori_loop(0, rhs_stack.shape[0], place, 0)
    strips = rows // 8
    zeros = jnp.zeros((8, cols), jnp.float32)
    pad_ref[0:8, :] = zeros
    pad_ref[rows + 8 : rows + 16, :] = zeros
    row = lax.broadcasted_iota(jnp.int32, (8, cols), 0)
    col = lax.broadcasted_iota(jnp.int32, (8, cols), 1)

    def at(k, offset=0):
        return pl.ds(pl.multiple_of(k * 8 + offset, 8), 8)

    def init(k, acc):
        v = rhs_ref[at(k), :]
        m = (coded_ref[at(k), :] >= 0.0).astype(jnp.float32)
        residual_ref[at(k), :] = v
        dir_ref[at(k), :] = v
        height_ref[at(k), :] = jnp.zeros_like(v)
        pad_ref[at(k, 8), :] = m * v
        return acc + v * v

    def image(k, acc):
        prev = pad_ref[at(k), :]
        cur = pad_ref[at(k, 8), :]
        nxt = pad_ref[at(k, 16), :]
        south = jnp.where(row == 7, pltpu.roll(nxt, 7, 0), pltpu.roll(cur, 7, 0))
        north = jnp.where(row == 0, pltpu.roll(prev, 1, 0), pltpu.roll(cur, 1, 0))
        east = jnp.where(col == cols - 1, 0.0, pltpu.roll(cur, cols - 1, 1))
        west = jnp.where(col == 0, 0.0, pltpu.roll(cur, 1, 1))
        beside = south + north + east + west
        ot = coded_ref[at(k), :]
        m = (ot >= 0.0).astype(jnp.float32)
        v = dir_ref[at(k), :]
        w = m * ((4.0 + ot) * v - beside) + (1.0 - m) * v
        img_ref[at(k), :] = w
        return acc + v * w

    norm_now = strip_sum(lax.fori_loop(0, strips, init, zeros))
    for step in range(ITERS):
        alpha = norm_now / strip_sum(lax.fori_loop(0, strips, image, zeros))

        def update(k, acc):
            v = dir_ref[at(k), :]
            height_ref[at(k), :] = height_ref[at(k), :] + alpha * v
            r = residual_ref[at(k), :] - alpha * img_ref[at(k), :]
            residual_ref[at(k), :] = r
            return acc + r * r

        norm_next = strip_sum(lax.fori_loop(0, strips, update, zeros))
        beta = norm_next / norm_now

        def direct(k, carry):
            d = residual_ref[at(k), :] + beta * dir_ref[at(k), :]
            dir_ref[at(k), :] = d
            m = (coded_ref[at(k), :] >= 0.0).astype(jnp.float32)
            pad_ref[at(k, 8), :] = m * d
            return carry

        if step < ITERS - 1:
            lax.fori_loop(0, strips, direct, 0)
        norm_now = norm_next
    r0 = pl.multiple_of(gy * tile_rows, tile_rows)
    c0 = pl.multiple_of(gx * tile_cols, tile_cols)
    height_out[...] = height_ref[pl.ds(r0, tile_rows), pl.ds(c0, tile_cols)]
    residual_out[...] = residual_ref[pl.ds(r0, tile_rows), pl.ds(c0, tile_cols)]


def solve_grid(rhs_stack, coded_stack, rounds):
    parts, tile_rows, tile_cols = rhs_stack.shape
    rows = lax.axis_size("gy") * tile_rows
    cols = lax.axis_size("gx") * tile_cols
    index = jnp.stack([lax.axis_index("gy"), lax.axis_index("gx")]).astype(jnp.int32)
    whole = pl.BlockSpec(memory_space=pltpu.VMEM)
    grid = pltpu.VMEM((rows, cols), jnp.float32)
    return pl.pallas_call(
        functools.partial(cg_kernel, rounds),
        in_specs=[pl.BlockSpec(memory_space=pltpu.SMEM), whole, whole],
        out_specs=[whole, whole],
        out_shape=[jax.ShapeDtypeStruct((tile_rows, tile_cols), jnp.float32)] * 2,
        scratch_shapes=[grid, grid, grid, grid, pltpu.VMEM((rows + 16, cols), jnp.float32), grid, grid],
    )(index, rhs_stack, coded_stack)


def body(
    atm_state, atm_kappa, vert_weight, remap_src, remap_count, remap_weight, land_mask, ocean_term
):
    levels, tile_lat, tile_lon = atm_state.shape
    kappa = atm_kappa[:, None, None]
    count_gx = lax.axis_size("gx")
    count_gy = lax.axis_size("gy")
    rounds = gather_rounds()
    coded_all = stack_gather(jnp.where(land_mask != 0, ocean_term, -1.0), rounds)
    core, coded_all = lax.optimization_barrier((atm_state, coded_all))
    field, flux = diffuse(atm_state, core, atm_kappa, vert_weight)
    flux = flux.reshape(flux.shape[0], tile_lat * tile_lon)
    ocean_blocks, lists, width, _ = remap_weight.shape
    comps = vert_weight.shape[0]
    own_blocks = tile_lat * tile_lon // width
    blocks = flux.astype(jnp.bfloat16).reshape(comps, own_blocks, width).transpose(1, 0, 2)
    devices = count_gx * count_gy
    gx_index = lax.axis_index("gx")
    gy_index = lax.axis_index("gy")
    me_index = gx_index * count_gy + gy_index
    east_index = (gx_index + 1) % count_gx * count_gy + gy_index
    west_index = (gx_index + count_gx - 1) % count_gx * count_gy + gy_index
    entries = ocean_blocks * lists
    slots = 2 * land_mask.shape[0]
    src_all = remap_src.reshape(devices, entries)
    live_all = (
        jnp.arange(lists, dtype=jnp.int32)[None, None, :]
        < remap_count.reshape(devices, ocean_blocks)[:, :, None]
    ).reshape(devices, entries)
    owner_all = src_all // own_blocks
    inside_all = src_all % own_blocks
    mine_owner = lax.dynamic_slice_in_dim(owner_all, me_index, 1, 0)[0]
    mine_inside = lax.dynamic_slice_in_dim(inside_all, me_index, 1, 0)[0]
    mine_live = lax.dynamic_slice_in_dim(live_all, me_index, 1, 0)[0]
    from_east = mine_live & (mine_owner == east_index)
    from_self = mine_live & (mine_owner == me_index)
    local_part = blocks[jnp.where(from_self, mine_inside, 0)]
    west_owner = lax.dynamic_slice_in_dim(owner_all, west_index, 1, 0)[0]
    west_inside = lax.dynamic_slice_in_dim(inside_all, west_index, 1, 0)[0]
    west_live = lax.dynamic_slice_in_dim(live_all, west_index, 1, 0)[0]
    wanted = (west_live & (west_owner == me_index)).astype(jnp.int32)
    wanted_rank = jnp.cumsum(wanted) - 1
    slot_ids = jnp.arange(slots, dtype=jnp.int32)
    picker = wanted[None, :] * (wanted_rank[None, :] == slot_ids[:, None]).astype(jnp.int32)
    send_index = jnp.sum(picker * west_inside[None, :], axis=1)
    send_valid = jnp.sum(picker, axis=1).astype(jnp.bfloat16)
    outgoing = blocks[send_index] * send_valid[:, None, None]
    incoming = shifted(outgoing, "gx", -1)
    east_int = from_east.astype(jnp.int32)
    east_rank = jnp.cumsum(east_int) - 1
    remote_part = incoming[jnp.where(from_east, east_rank, 0)]
    gathered = jnp.where(
        from_self[:, None, None],
        local_part,
        jnp.where(from_east[:, None, None], remote_part, jnp.zeros_like(local_part)),
    )
    gathered = gathered.reshape(ocean_blocks, lists, comps, width)
    ocean_rows, ocean_cols = land_mask.shape
    remapped = jnp.einsum(
        "bkij,bkcj->cbi", remap_weight, gathered, preferred_element_type=jnp.float32
    )
    ocean_flux = remapped.reshape(comps, ocean_rows, ocean_cols)
    rhs_tile = land_mask.astype(jnp.float32) * (ocean_flux[0] + ocean_flux[1])
    rhs = stack_gather(rhs_tile, rounds)
    height, residual = solve_grid(rhs, coded_all, rounds)
    return (field, ocean_flux, height, residual)


def solution(mesh):
    return jax.shard_map(
        body,
        mesh=mesh,
        in_specs=(
            P(None, "gy", "gx"),
            P(),
            P(),
            P(),
            P(),
            P(("gx", "gy"), None, None, None),
            P("gy", "gx"),
            P("gy", "gx"),
        ),
        out_specs=(P(None, "gy", "gx"), P(None, "gy", "gx"), P("gy", "gx"), P("gy", "gx")),
        check_vma=False,
    )
```

```python
import functools

import jax
import jax.numpy as jnp
from jax import lax
from jax.sharding import PartitionSpec as P
from jax.experimental import pallas as pl
from jax.experimental.pallas import tpu as pltpu

STEPS = 4
ITERS = 3


def with_halo(x, sides, width):
    for axis, dim in sides:
        size, length = (lax.axis_size(axis), x.shape[dim])
        up = [(i, (i + 1) % size) for i in range(size - 1)]
        down = [(j, i) for i, j in up]
        last = lax.slice_in_dim(x, length - width, length, axis=dim)
        first = lax.slice_in_dim(x, 0, width, axis=dim)
        before = lax.ppermute(last, axis, up)
        after = lax.ppermute(first, axis, down)
        x = jnp.concatenate([before, x, after], axis=dim)
    return x


def shifted(x, axis, by):
    size = lax.axis_size(axis)
    return lax.ppermute(x, axis, [(i, (i + by) % size) for i in range(size)])


def ocean_operator(vector, maskf, ocean_term):
    padded = with_halo(maskf * vector, (("gx", 1), ("gy", 0)), 1)
    beside = padded[2:, 1:-1] + padded[:-2, 1:-1] + padded[1:-1, 2:] + padded[1:-1, :-2]
    return maskf * ((4.0 + ocean_term) * vector - beside) + (1.0 - maskf) * vector


def square_total(residual):
    return lax.psum(jnp.sum(residual * residual), ("gx", "gy"))


def gather_rounds():
    rounds = []
    for axis, bits in (("gy", lax.axis_size("gy")), ("gx", lax.axis_size("gx"))):
        distances = []
        d = 1
        while d < bits:
            distances.append(d)
            d *= 2
        rounds.append([(axis, d) for d in distances])
    gy_rounds, gx_rounds = rounds
    far = gy_rounds[1::2] + gx_rounds[2:]
    near = gy_rounds[0::2] + gx_rounds[1:2] + gx_rounds[:1]
    return far + near


def stack_gather(tile, rounds):
    x = tile[None]
    for axis, distance in rounds:
        size = lax.axis_size(axis)
        other = lax.ppermute(x, axis, [(j, j ^ distance) for j in range(size)])
        x = jnp.concatenate([x, other], axis=0)
    return x


def grid_operator(vector, maskf, ocean_term):
    padded = jnp.pad(maskf * vector, 1)
    beside = padded[2:, 1:-1] + padded[:-2, 1:-1] + padded[1:-1, 2:] + padded[1:-1, :-2]
    return maskf * ((4.0 + ocean_term) * vector - beside) + (1.0 - maskf) * vector


HALO = 4
LEVEL_BLOCK = 16


def diffusion_kernel(kappa_ref, weight_ref, core_ref, lanes_ref, rows_ref, mask_ref, out_ref, flux_ref):
    block = pl.program_id(0)
    levels, rows, cols = core_ref.shape

    @pl.when(block == 0)
    def _():
        flux_ref[...] = jnp.zeros_like(flux_ref)

    mask = mask_ref[...]
    mask_side = mask[:rows, cols:]
    mask_low = mask[rows:, :]

    def level(l, carry):
        lev = block * levels + l
        kappa = kappa_ref[lev]
        top = jnp.concatenate([core_ref[l], lanes_ref[l]], axis=1)
        f = jnp.concatenate([top, rows_ref[l]], axis=0)
        height, width = f.shape
        for step in range(STEPS):
            beside = (
                pltpu.roll(f, height - 1, 0)
                + pltpu.roll(f, 1, 0)
                + pltpu.roll(f, width - 1, 1)
                + pltpu.roll(f, 1, 1)
            )
            f = f + kappa * (beside - 4.0 * f)
            top = jnp.concatenate([f[:rows, :cols], f[:rows, cols:] * mask_side], axis=1)
            f = jnp.concatenate([top, f[rows:, :] * mask_low], axis=0)
        core = f[:rows, :cols]
        out_ref[l] = core
        for c in range(flux_ref.shape[0]):
            flux_ref[c] += weight_ref[c, lev] * core
        return carry

    lax.fori_loop(0, levels, level, 0, unroll=4)


def diffuse(field, atm_kappa, vert_weight):
    levels, rows, cols = field.shape
    comps = vert_weight.shape[0]
    count_gx = lax.axis_size("gx")
    count_gy = lax.axis_size("gy")
    gx_index = lax.axis_index("gx")
    gy_index = lax.axis_index("gy")
    up_gx = [(i, i + 1) for i in range(count_gx - 1)]
    down_gx = [(i + 1, i) for i in range(count_gx - 1)]
    up_gy = [(i, i + 1) for i in range(count_gy - 1)]
    down_gy = [(i + 1, i) for i in range(count_gy - 1)]
    pairs = lambda di, dj: [
        ((i + di) * count_gy + j + dj, i * count_gy + j)
        for i in range(count_gx)
        for j in range(count_gy)
        if 0 <= i + di < count_gx and 0 <= j + dj < count_gy
    ]
    both = ("gx", "gy")
    south = lax.ppermute(field[:, :HALO, :], "gy", down_gy)
    north = lax.ppermute(field[:, rows - HALO :, :], "gy", up_gy)
    east = lax.ppermute(field[:, :, :HALO], "gx", down_gx)
    west = lax.ppermute(field[:, :, cols - HALO :], "gx", up_gx)
    south_east = lax.ppermute(field[:, :HALO, :HALO], both, pairs(1, 1))
    south_west = lax.ppermute(field[:, :HALO, cols - HALO :], both, pairs(-1, 1))
    north_east = lax.ppermute(field[:, rows - HALO :, :HALO], both, pairs(1, -1))
    north_west = lax.ppermute(field[:, rows - HALO :, cols - HALO :], both, pairs(-1, -1))
    gap = jnp.zeros((levels, rows, 128 - 2 * HALO), field.dtype)
    lanes = jnp.concatenate([east, gap, west], axis=2)
    corner_gap = jnp.zeros((levels, HALO, 128 - 2 * HALO), field.dtype)
    halo_rows = jnp.concatenate(
        [
            jnp.concatenate([south, south_east, corner_gap, south_west], axis=2),
            jnp.concatenate([north, north_east, corner_gap, north_west], axis=2),
        ],
        axis=1,
    )
    height = rows + 2 * HALO
    width = cols + 128
    r = jnp.arange(height, dtype=jnp.int32)
    c = jnp.arange(width, dtype=jnp.int32)
    global_r = gy_index * rows + jnp.where(r < rows + HALO, r, r - height)
    global_c = gx_index * cols + jnp.where(c < cols + HALO, c, c - width)
    inside_r = (global_r >= 0) & (global_r < count_gy * rows)
    inside_c = (global_c >= 0) & (global_c < count_gx * cols) & ((c < cols + HALO) | (c >= width - HALO))
    mask = (inside_r[:, None] & inside_c[None, :]).astype(jnp.float32)
    blocks = levels // LEVEL_BLOCK
    smem = pl.BlockSpec(memory_space=pltpu.SMEM)
    out, flux = pl.pallas_call(
        diffusion_kernel,
        grid=(blocks,),
        in_specs=[
            smem,
            smem,
            pl.BlockSpec((LEVEL_BLOCK, rows, cols), lambda b: (b, 0, 0)),
            pl.BlockSpec((LEVEL_BLOCK, rows, 128), lambda b: (b, 0, 0)),
            pl.BlockSpec((LEVEL_BLOCK, 2 * HALO, width), lambda b: (b, 0, 0)),
            pl.BlockSpec((height, width), lambda b: (0, 0)),
        ],
        out_specs=[
            pl.BlockSpec((LEVEL_BLOCK, rows, cols), lambda b: (b, 0, 0)),
            pl.BlockSpec((comps, rows, cols), lambda b: (0, 0, 0)),
        ],
        out_shape=[
            jax.ShapeDtypeStruct(field.shape, field.dtype),
            jax.ShapeDtypeStruct((comps, rows, cols), jnp.float32),
        ],
        compiler_params=pltpu.CompilerParams(dimension_semantics=("arbitrary",)),
        cost_estimate=pl.CostEstimate(
            flops=levels * height * width * STEPS * 10,
            transcendentals=0,
            bytes_accessed=2 * field.size * 4,
        ),
    )(atm_kappa, vert_weight, field, lanes, halo_rows, mask)
    return out, flux


def strip_sum(acc):
    return acc.sum(axis=0, keepdims=True).sum(axis=1, keepdims=True)


def cg_kernel(
    rounds, index_ref, rhs_stack, coded_stack, height_out, residual_out,
    rhs_ref, coded_ref, height_ref, residual_ref, pad_ref, dir_ref, img_ref,
):
    rows, cols = rhs_ref.shape
    tile_rows, tile_cols = height_out.shape
    gy = index_ref[0]
    gx = index_ref[1]

    def place(k, carry):
        gy_off = 0
        gx_off = 0
        for bit, (axis, distance) in enumerate(rounds):
            flag = lax.shift_right_logical(k, bit) & 1
            if axis == "gy":
                gy_off = gy_off + flag * distance
            else:
                gx_off = gx_off + flag * distance
        r0 = pl.multiple_of(lax.bitwise_xor(gy, gy_off) * tile_rows, tile_rows)
        c0 = pl.multiple_of(lax.bitwise_xor(gx, gx_off) * tile_cols, tile_cols)
        rhs_ref[pl.ds(r0, tile_rows), pl.ds(c0, tile_cols)] = rhs_stack[k]
        coded_ref[pl.ds(r0, tile_rows), pl.ds(c0, tile_cols)] = coded_stack[k]
        return carry

    lax.fori_loop(0, rhs_stack.shape[0], place, 0, unroll=4)
    strips = rows // 8
    zeros = jnp.zeros((8, cols), jnp.float32)
    pad_ref[0:8, :] = zeros
    pad_ref[rows + 8 : rows + 16, :] = zeros
    row = lax.broadcasted_iota(jnp.int32, (8, cols), 0)
    col = lax.broadcasted_iota(jnp.int32, (8, cols), 1)

    def at(k, offset=0):
        return pl.ds(pl.multiple_of(k * 8 + offset, 8), 8)

    def init(k, acc):
        v = rhs_ref[at(k), :]
        m = (coded_ref[at(k), :] >= 0.0).astype(jnp.float32)
        residual_ref[at(k), :] = v
        dir_ref[at(k), :] = v
        height_ref[at(k), :] = jnp.zeros_like(v)
        pad_ref[at(k, 8), :] = m * v
        return acc + v * v

    def image(k, acc):
        prev = pad_ref[at(k), :]
        cur = pad_ref[at(k, 8), :]
        nxt = pad_ref[at(k, 16), :]
        south = jnp.where(row == 7, pltpu.roll(nxt, 7, 0), pltpu.roll(cur, 7, 0))
        north = jnp.where(row == 0, pltpu.roll(prev, 1, 0), pltpu.roll(cur, 1, 0))
        east = jnp.where(col == cols - 1, 0.0, pltpu.roll(cur, cols - 1, 1))
        west = jnp.where(col == 0, 0.0, pltpu.roll(cur, 1, 1))
        beside = south + north + east + west
        ot = coded_ref[at(k), :]
        m = (ot >= 0.0).astype(jnp.float32)
        v = dir_ref[at(k), :]
        w = m * ((4.0 + ot) * v - beside) + (1.0 - m) * v
        img_ref[at(k), :] = w
        return acc + v * w

    norm_now = strip_sum(lax.fori_loop(0, strips, init, zeros, unroll=4))
    for step in range(ITERS):
        alpha = norm_now / strip_sum(lax.fori_loop(0, strips, image, zeros, unroll=4))

        def update(k, acc):
            v = dir_ref[at(k), :]
            height_ref[at(k), :] = height_ref[at(k), :] + alpha * v
            r = residual_ref[at(k), :] - alpha * img_ref[at(k), :]
            residual_ref[at(k), :] = r
            return acc + r * r

        norm_next = strip_sum(lax.fori_loop(0, strips, update, zeros, unroll=4))
        beta = norm_next / norm_now

        def direct(k, carry):
            d = residual_ref[at(k), :] + beta * dir_ref[at(k), :]
            dir_ref[at(k), :] = d
            m = (coded_ref[at(k), :] >= 0.0).astype(jnp.float32)
            pad_ref[at(k, 8), :] = m * d
            return carry

        if step < ITERS - 1:
            lax.fori_loop(0, strips, direct, 0, unroll=4)
        norm_now = norm_next
    r0 = pl.multiple_of(gy * tile_rows, tile_rows)
    c0 = pl.multiple_of(gx * tile_cols, tile_cols)
    height_out[...] = height_ref[pl.ds(r0, tile_rows), pl.ds(c0, tile_cols)]
    residual_out[...] = residual_ref[pl.ds(r0, tile_rows), pl.ds(c0, tile_cols)]


def solve_grid(rhs_stack, coded_stack, rounds):
    parts, tile_rows, tile_cols = rhs_stack.shape
    rows = lax.axis_size("gy") * tile_rows
    cols = lax.axis_size("gx") * tile_cols
    index = jnp.stack([lax.axis_index("gy"), lax.axis_index("gx")]).astype(jnp.int32)
    whole = pl.BlockSpec(memory_space=pltpu.VMEM)
    grid = pltpu.VMEM((rows, cols), jnp.float32)
    return pl.pallas_call(
        functools.partial(cg_kernel, rounds),
        in_specs=[pl.BlockSpec(memory_space=pltpu.SMEM), whole, whole],
        out_specs=[whole, whole],
        out_shape=[jax.ShapeDtypeStruct((tile_rows, tile_cols), jnp.float32)] * 2,
        scratch_shapes=[grid, grid, grid, grid, pltpu.VMEM((rows + 16, cols), jnp.float32), grid, grid],
    )(index, rhs_stack, coded_stack)


def body(
    atm_state, atm_kappa, vert_weight, remap_src, remap_count, remap_weight, land_mask, ocean_term
):
    levels, tile_lat, tile_lon = atm_state.shape
    kappa = atm_kappa[:, None, None]
    count_gx = lax.axis_size("gx")
    count_gy = lax.axis_size("gy")
    rounds = gather_rounds()
    coded_all = stack_gather(jnp.where(land_mask != 0, ocean_term, -1.0), rounds)
    field, flux = diffuse(atm_state, atm_kappa, vert_weight)
    flux = flux.reshape(flux.shape[0], tile_lat * tile_lon)
    ocean_blocks, lists, width, _ = remap_weight.shape
    comps = vert_weight.shape[0]
    own_blocks = tile_lat * tile_lon // width
    blocks = flux.astype(jnp.bfloat16).reshape(comps, own_blocks, width).transpose(1, 0, 2)
    devices = count_gx * count_gy
    gx_index = lax.axis_index("gx")
    gy_index = lax.axis_index("gy")
    me_index = gx_index * count_gy + gy_index
    east_index = (gx_index + 1) % count_gx * count_gy + gy_index
    west_index = (gx_index + count_gx - 1) % count_gx * count_gy + gy_index
    entries = ocean_blocks * lists
    slots = 2 * land_mask.shape[0]
    src_all = remap_src.reshape(devices, entries)
    live_all = (
        jnp.arange(lists, dtype=jnp.int32)[None, None, :]
        < remap_count.reshape(devices, ocean_blocks)[:, :, None]
    ).reshape(devices, entries)
    owner_all = src_all // own_blocks
    inside_all = src_all % own_blocks
    mine_owner = lax.dynamic_slice_in_dim(owner_all, me_index, 1, 0)[0]
    mine_inside = lax.dynamic_slice_in_dim(inside_all, me_index, 1, 0)[0]
    mine_live = lax.dynamic_slice_in_dim(live_all, me_index, 1, 0)[0]
    from_east = mine_live & (mine_owner == east_index)
    from_self = mine_live & (mine_owner == me_index)
    local_part = blocks[jnp.where(from_self, mine_inside, 0)]
    west_owner = lax.dynamic_slice_in_dim(owner_all, west_index, 1, 0)[0]
    west_inside = lax.dynamic_slice_in_dim(inside_all, west_index, 1, 0)[0]
    west_live = lax.dynamic_slice_in_dim(live_all, west_index, 1, 0)[0]
    wanted = (west_live & (west_owner == me_index)).astype(jnp.int32)
    wanted_rank = jnp.cumsum(wanted) - 1
    slot_ids = jnp.arange(slots, dtype=jnp.int32)
    picker = wanted[None, :] * (wanted_rank[None, :] == slot_ids[:, None]).astype(jnp.int32)
    send_index = jnp.sum(picker * west_inside[None, :], axis=1)
    send_valid = jnp.sum(picker, axis=1).astype(jnp.bfloat16)
    outgoing = blocks[send_index] * send_valid[:, None, None]
    incoming = shifted(outgoing, "gx", -1)
    east_int = from_east.astype(jnp.int32)
    east_rank = jnp.cumsum(east_int) - 1
    remote_part = incoming[jnp.where(from_east, east_rank, 0)]
    gathered = jnp.where(
        from_self[:, None, None],
        local_part,
        jnp.where(from_east[:, None, None], remote_part, jnp.zeros_like(local_part)),
    )
    gathered = gathered.reshape(ocean_blocks, lists, comps, width)
    ocean_rows, ocean_cols = land_mask.shape
    remapped = jnp.einsum(
        "bkij,bkcj->cbi", remap_weight, gathered, preferred_element_type=jnp.float32
    )
    ocean_flux = remapped.reshape(comps, ocean_rows, ocean_cols)
    rhs_tile = land_mask.astype(jnp.float32) * (ocean_flux[0] + ocean_flux[1])
    rhs = stack_gather(rhs_tile, rounds)
    height, residual = solve_grid(rhs, coded_all, rounds)
    return (field, ocean_flux, height, residual)


def solution(mesh):
    return jax.shard_map(
        body,
        mesh=mesh,
        in_specs=(
            P(None, "gy", "gx"),
            P(),
            P(),
            P(),
            P(),
            P(("gx", "gy"), None, None, None),
            P("gy", "gx"),
            P("gy", "gx"),
        ),
        out_specs=(P(None, "gy", "gx"), P(None, "gy", "gx"), P("gy", "gx"), P("gy", "gx")),
        check_vma=False,
    )
```

```python
import functools

import jax
import jax.numpy as jnp
from jax import lax
from jax.sharding import PartitionSpec as P
from jax.experimental import pallas as pl
from jax.experimental.pallas import tpu as pltpu

STEPS = 4
ITERS = 3


def with_halo(x, sides, width):
    for axis, dim in sides:
        size, length = (lax.axis_size(axis), x.shape[dim])
        up = [(i, (i + 1) % size) for i in range(size - 1)]
        down = [(j, i) for i, j in up]
        last = lax.slice_in_dim(x, length - width, length, axis=dim)
        first = lax.slice_in_dim(x, 0, width, axis=dim)
        before = lax.ppermute(last, axis, up)
        after = lax.ppermute(first, axis, down)
        x = jnp.concatenate([before, x, after], axis=dim)
    return x


def shifted(x, axis, by):
    size = lax.axis_size(axis)
    return lax.ppermute(x, axis, [(i, (i + by) % size) for i in range(size)])


def ocean_operator(vector, maskf, ocean_term):
    padded = with_halo(maskf * vector, (("gx", 1), ("gy", 0)), 1)
    beside = padded[2:, 1:-1] + padded[:-2, 1:-1] + padded[1:-1, 2:] + padded[1:-1, :-2]
    return maskf * ((4.0 + ocean_term) * vector - beside) + (1.0 - maskf) * vector


def square_total(residual):
    return lax.psum(jnp.sum(residual * residual), ("gx", "gy"))


def gather_rounds():
    rounds = []
    for axis, bits in (("gy", lax.axis_size("gy")), ("gx", lax.axis_size("gx"))):
        distances = []
        d = 1
        while d < bits:
            distances.append(d)
            d *= 2
        rounds.append([(axis, d) for d in distances])
    gy_rounds, gx_rounds = rounds
    far = gy_rounds[1::2] + gx_rounds[2:]
    near = gy_rounds[0::2] + gx_rounds[1:2] + gx_rounds[:1]
    return far + near


def stack_gather(tile, rounds):
    x = tile[None]
    for axis, distance in rounds:
        size = lax.axis_size(axis)
        other = lax.ppermute(x, axis, [(j, j ^ distance) for j in range(size)])
        x = jnp.concatenate([x, other], axis=0)
    return x


def grid_operator(vector, maskf, ocean_term):
    padded = jnp.pad(maskf * vector, 1)
    beside = padded[2:, 1:-1] + padded[:-2, 1:-1] + padded[1:-1, 2:] + padded[1:-1, :-2]
    return maskf * ((4.0 + ocean_term) * vector - beside) + (1.0 - maskf) * vector


HALO = 4
LEVEL_BLOCK = 16


def diffusion_kernel(kappa_ref, weight_ref, core_ref, lanes_ref, rows_ref, mask_ref, out_ref, flux_ref):
    block = pl.program_id(0)
    levels, rows, cols = core_ref.shape

    @pl.when(block == 0)
    def _():
        flux_ref[...] = jnp.zeros_like(flux_ref)

    mask = mask_ref[...]
    mask_side = mask[:rows, cols:]
    mask_low = mask[rows:, :]

    def level(l, carry):
        lev = block * levels + l
        kappa = kappa_ref[lev]
        top = jnp.concatenate([core_ref[l], lanes_ref[l]], axis=1)
        f = jnp.concatenate([top, rows_ref[l]], axis=0)
        height, width = f.shape
        for step in range(STEPS):
            beside = (
                pltpu.roll(f, height - 1, 0)
                + pltpu.roll(f, 1, 0)
                + pltpu.roll(f, width - 1, 1)
                + pltpu.roll(f, 1, 1)
            )
            f = f + kappa * (beside - 4.0 * f)
            top = jnp.concatenate([f[:rows, :cols], f[:rows, cols:] * mask_side], axis=1)
            f = jnp.concatenate([top, f[rows:, :] * mask_low], axis=0)
        core = f[:rows, :cols]
        out_ref[l] = core
        for c in range(flux_ref.shape[0]):
            flux_ref[c] += weight_ref[c, lev] * core
        return carry

    lax.fori_loop(0, levels, level, 0, unroll=8)


def diffuse(field, atm_kappa, vert_weight):
    levels, rows, cols = field.shape
    comps = vert_weight.shape[0]
    count_gx = lax.axis_size("gx")
    count_gy = lax.axis_size("gy")
    gx_index = lax.axis_index("gx")
    gy_index = lax.axis_index("gy")
    up_gx = [(i, i + 1) for i in range(count_gx - 1)]
    down_gx = [(i + 1, i) for i in range(count_gx - 1)]
    up_gy = [(i, i + 1) for i in range(count_gy - 1)]
    down_gy = [(i + 1, i) for i in range(count_gy - 1)]
    pairs = lambda di, dj: [
        ((i + di) * count_gy + j + dj, i * count_gy + j)
        for i in range(count_gx)
        for j in range(count_gy)
        if 0 <= i + di < count_gx and 0 <= j + dj < count_gy
    ]
    both = ("gx", "gy")
    south = lax.ppermute(field[:, :HALO, :], "gy", down_gy)
    north = lax.ppermute(field[:, rows - HALO :, :], "gy", up_gy)
    east = lax.ppermute(field[:, :, :HALO], "gx", down_gx)
    west = lax.ppermute(field[:, :, cols - HALO :], "gx", up_gx)
    south_east = lax.ppermute(field[:, :HALO, :HALO], both, pairs(1, 1))
    south_west = lax.ppermute(field[:, :HALO, cols - HALO :], both, pairs(-1, 1))
    north_east = lax.ppermute(field[:, rows - HALO :, :HALO], both, pairs(1, -1))
    north_west = lax.ppermute(field[:, rows - HALO :, cols - HALO :], both, pairs(-1, -1))
    gap = jnp.zeros((levels, rows, 128 - 2 * HALO), field.dtype)
    lanes = jnp.concatenate([east, gap, west], axis=2)
    corner_gap = jnp.zeros((levels, HALO, 128 - 2 * HALO), field.dtype)
    halo_rows = jnp.concatenate(
        [
            jnp.concatenate([south, south_east, corner_gap, south_west], axis=2),
            jnp.concatenate([north, north_east, corner_gap, north_west], axis=2),
        ],
        axis=1,
    )
    height = rows + 2 * HALO
    width = cols + 128
    r = jnp.arange(height, dtype=jnp.int32)
    c = jnp.arange(width, dtype=jnp.int32)
    global_r = gy_index * rows + jnp.where(r < rows + HALO, r, r - height)
    global_c = gx_index * cols + jnp.where(c < cols + HALO, c, c - width)
    inside_r = (global_r >= 0) & (global_r < count_gy * rows)
    inside_c = (global_c >= 0) & (global_c < count_gx * cols) & ((c < cols + HALO) | (c >= width - HALO))
    mask = (inside_r[:, None] & inside_c[None, :]).astype(jnp.float32)
    blocks = levels // LEVEL_BLOCK
    smem = pl.BlockSpec(memory_space=pltpu.SMEM)
    out, flux = pl.pallas_call(
        diffusion_kernel,
        grid=(blocks,),
        in_specs=[
            smem,
            smem,
            pl.BlockSpec((LEVEL_BLOCK, rows, cols), lambda b: (b, 0, 0)),
            pl.BlockSpec((LEVEL_BLOCK, rows, 128), lambda b: (b, 0, 0)),
            pl.BlockSpec((LEVEL_BLOCK, 2 * HALO, width), lambda b: (b, 0, 0)),
            pl.BlockSpec((height, width), lambda b: (0, 0)),
        ],
        out_specs=[
            pl.BlockSpec((LEVEL_BLOCK, rows, cols), lambda b: (b, 0, 0)),
            pl.BlockSpec((comps, rows, cols), lambda b: (0, 0, 0)),
        ],
        out_shape=[
            jax.ShapeDtypeStruct(field.shape, field.dtype),
            jax.ShapeDtypeStruct((comps, rows, cols), jnp.float32),
        ],
        compiler_params=pltpu.CompilerParams(dimension_semantics=("arbitrary",)),
        cost_estimate=pl.CostEstimate(
            flops=levels * height * width * STEPS * 10,
            transcendentals=0,
            bytes_accessed=2 * field.size * 4,
        ),
    )(atm_kappa, vert_weight, field, lanes, halo_rows, mask)
    return out, flux


def strip_sum(acc):
    return acc.sum(axis=0, keepdims=True).sum(axis=1, keepdims=True)


def cg_kernel(
    rounds, index_ref, rhs_stack, coded_stack, height_out, residual_out,
    rhs_ref, coded_ref, height_ref, residual_ref, pad_ref, dir_ref, img_ref,
):
    rows, cols = rhs_ref.shape
    tile_rows, tile_cols = height_out.shape
    gy = index_ref[0]
    gx = index_ref[1]

    def place(k, carry):
        gy_off = 0
        gx_off = 0
        for bit, (axis, distance) in enumerate(rounds):
            flag = lax.shift_right_logical(k, bit) & 1
            if axis == "gy":
                gy_off = gy_off + flag * distance
            else:
                gx_off = gx_off + flag * distance
        r0 = pl.multiple_of(lax.bitwise_xor(gy, gy_off) * tile_rows, tile_rows)
        c0 = pl.multiple_of(lax.bitwise_xor(gx, gx_off) * tile_cols, tile_cols)
        rhs_ref[pl.ds(r0, tile_rows), pl.ds(c0, tile_cols)] = rhs_stack[k]
        coded_ref[pl.ds(r0, tile_rows), pl.ds(c0, tile_cols)] = coded_stack[k]
        return carry

    lax.fori_loop(0, rhs_stack.shape[0], place, 0, unroll=4)
    strips = rows // 8
    zeros = jnp.zeros((8, cols), jnp.float32)
    pad_ref[0:8, :] = zeros
    pad_ref[rows + 8 : rows + 16, :] = zeros
    row = lax.broadcasted_iota(jnp.int32, (8, cols), 0)
    col = lax.broadcasted_iota(jnp.int32, (8, cols), 1)

    def at(k, offset=0):
        return pl.ds(pl.multiple_of(k * 8 + offset, 8), 8)

    def init(k, acc):
        v = rhs_ref[at(k), :]
        m = (coded_ref[at(k), :] >= 0.0).astype(jnp.float32)
        residual_ref[at(k), :] = v
        dir_ref[at(k), :] = v
        height_ref[at(k), :] = jnp.zeros_like(v)
        pad_ref[at(k, 8), :] = m * v
        return acc + v * v

    def image(k, acc):
        prev = pad_ref[at(k), :]
        cur = pad_ref[at(k, 8), :]
        nxt = pad_ref[at(k, 16), :]
        south = jnp.where(row == 7, pltpu.roll(nxt, 7, 0), pltpu.roll(cur, 7, 0))
        north = jnp.where(row == 0, pltpu.roll(prev, 1, 0), pltpu.roll(cur, 1, 0))
        east = jnp.where(col == cols - 1, 0.0, pltpu.roll(cur, cols - 1, 1))
        west = jnp.where(col == 0, 0.0, pltpu.roll(cur, 1, 1))
        beside = south + north + east + west
        ot = coded_ref[at(k), :]
        m = (ot >= 0.0).astype(jnp.float32)
        v = dir_ref[at(k), :]
        w = m * ((4.0 + ot) * v - beside) + (1.0 - m) * v
        img_ref[at(k), :] = w
        return acc + v * w

    norm_now = strip_sum(lax.fori_loop(0, strips, init, zeros, unroll=8))
    for step in range(ITERS):
        alpha = norm_now / strip_sum(lax.fori_loop(0, strips, image, zeros, unroll=8))

        def update(k, acc):
            v = dir_ref[at(k), :]
            height_ref[at(k), :] = height_ref[at(k), :] + alpha * v
            r = residual_ref[at(k), :] - alpha * img_ref[at(k), :]
            residual_ref[at(k), :] = r
            return acc + r * r

        norm_next = strip_sum(lax.fori_loop(0, strips, update, zeros, unroll=8))
        beta = norm_next / norm_now

        def direct(k, carry):
            d = residual_ref[at(k), :] + beta * dir_ref[at(k), :]
            dir_ref[at(k), :] = d
            m = (coded_ref[at(k), :] >= 0.0).astype(jnp.float32)
            pad_ref[at(k, 8), :] = m * d
            return carry

        if step < ITERS - 1:
            lax.fori_loop(0, strips, direct, 0, unroll=8)
        norm_now = norm_next
    r0 = pl.multiple_of(gy * tile_rows, tile_rows)
    c0 = pl.multiple_of(gx * tile_cols, tile_cols)
    height_out[...] = height_ref[pl.ds(r0, tile_rows), pl.ds(c0, tile_cols)]
    residual_out[...] = residual_ref[pl.ds(r0, tile_rows), pl.ds(c0, tile_cols)]


def solve_grid(rhs_stack, coded_stack, rounds):
    parts, tile_rows, tile_cols = rhs_stack.shape
    rows = lax.axis_size("gy") * tile_rows
    cols = lax.axis_size("gx") * tile_cols
    index = jnp.stack([lax.axis_index("gy"), lax.axis_index("gx")]).astype(jnp.int32)
    whole = pl.BlockSpec(memory_space=pltpu.VMEM)
    grid = pltpu.VMEM((rows, cols), jnp.float32)
    return pl.pallas_call(
        functools.partial(cg_kernel, rounds),
        in_specs=[pl.BlockSpec(memory_space=pltpu.SMEM), whole, whole],
        out_specs=[whole, whole],
        out_shape=[jax.ShapeDtypeStruct((tile_rows, tile_cols), jnp.float32)] * 2,
        scratch_shapes=[grid, grid, grid, grid, pltpu.VMEM((rows + 16, cols), jnp.float32), grid, grid],
    )(index, rhs_stack, coded_stack)


def body(
    atm_state, atm_kappa, vert_weight, remap_src, remap_count, remap_weight, land_mask, ocean_term
):
    levels, tile_lat, tile_lon = atm_state.shape
    kappa = atm_kappa[:, None, None]
    count_gx = lax.axis_size("gx")
    count_gy = lax.axis_size("gy")
    rounds = gather_rounds()
    coded_all = stack_gather(jnp.where(land_mask != 0, ocean_term, -1.0), rounds)
    field, flux = diffuse(atm_state, atm_kappa, vert_weight)
    flux = flux.reshape(flux.shape[0], tile_lat * tile_lon)
    ocean_blocks, lists, width, _ = remap_weight.shape
    comps = vert_weight.shape[0]
    own_blocks = tile_lat * tile_lon // width
    blocks = flux.astype(jnp.bfloat16).reshape(comps, own_blocks, width).transpose(1, 0, 2)
    devices = count_gx * count_gy
    gx_index = lax.axis_index("gx")
    gy_index = lax.axis_index("gy")
    me_index = gx_index * count_gy + gy_index
    east_index = (gx_index + 1) % count_gx * count_gy + gy_index
    west_index = (gx_index + count_gx - 1) % count_gx * count_gy + gy_index
    entries = ocean_blocks * lists
    slots = 2 * land_mask.shape[0]
    src_all = remap_src.reshape(devices, entries)
    live_all = (
        jnp.arange(lists, dtype=jnp.int32)[None, None, :]
        < remap_count.reshape(devices, ocean_blocks)[:, :, None]
    ).reshape(devices, entries)
    owner_all = src_all // own_blocks
    inside_all = src_all % own_blocks
    mine_owner = lax.dynamic_slice_in_dim(owner_all, me_index, 1, 0)[0]
    mine_inside = lax.dynamic_slice_in_dim(inside_all, me_index, 1, 0)[0]
    mine_live = lax.dynamic_slice_in_dim(live_all, me_index, 1, 0)[0]
    from_east = mine_live & (mine_owner == east_index)
    from_self = mine_live & (mine_owner == me_index)
    local_part = blocks[jnp.where(from_self, mine_inside, 0)]
    west_owner = lax.dynamic_slice_in_dim(owner_all, west_index, 1, 0)[0]
    west_inside = lax.dynamic_slice_in_dim(inside_all, west_index, 1, 0)[0]
    west_live = lax.dynamic_slice_in_dim(live_all, west_index, 1, 0)[0]
    wanted = (west_live & (west_owner == me_index)).astype(jnp.int32)
    wanted_rank = jnp.cumsum(wanted) - 1
    slot_ids = jnp.arange(slots, dtype=jnp.int32)
    picker = wanted[None, :] * (wanted_rank[None, :] == slot_ids[:, None]).astype(jnp.int32)
    send_index = jnp.sum(picker * west_inside[None, :], axis=1)
    send_valid = jnp.sum(picker, axis=1).astype(jnp.bfloat16)
    outgoing = blocks[send_index] * send_valid[:, None, None]
    incoming = shifted(outgoing, "gx", -1)
    east_int = from_east.astype(jnp.int32)
    east_rank = jnp.cumsum(east_int) - 1
    remote_part = incoming[jnp.where(from_east, east_rank, 0)]
    gathered = jnp.where(
        from_self[:, None, None],
        local_part,
        jnp.where(from_east[:, None, None], remote_part, jnp.zeros_like(local_part)),
    )
    gathered = gathered.reshape(ocean_blocks, lists, comps, width)
    ocean_rows, ocean_cols = land_mask.shape
    remapped = jnp.einsum(
        "bkij,bkcj->cbi", remap_weight, gathered, preferred_element_type=jnp.float32
    )
    ocean_flux = remapped.reshape(comps, ocean_rows, ocean_cols)
    rhs_tile = land_mask.astype(jnp.float32) * (ocean_flux[0] + ocean_flux[1])
    rhs = stack_gather(rhs_tile, rounds)
    height, residual = solve_grid(rhs, coded_all, rounds)
    return (field, ocean_flux, height, residual)


def solution(mesh):
    return jax.shard_map(
        body,
        mesh=mesh,
        in_specs=(
            P(None, "gy", "gx"),
            P(),
            P(),
            P(),
            P(),
            P(("gx", "gy"), None, None, None),
            P("gy", "gx"),
            P("gy", "gx"),
        ),
        out_specs=(P(None, "gy", "gx"), P(None, "gy", "gx"), P("gy", "gx"), P("gy", "gx")),
        check_vma=False,
    )
```

```python
import functools

import jax
import jax.numpy as jnp
from jax import lax
from jax.sharding import PartitionSpec as P
from jax.experimental import pallas as pl
from jax.experimental.pallas import tpu as pltpu

STEPS = 4
ITERS = 3


def with_halo(x, sides, width):
    for axis, dim in sides:
        size, length = (lax.axis_size(axis), x.shape[dim])
        up = [(i, (i + 1) % size) for i in range(size - 1)]
        down = [(j, i) for i, j in up]
        last = lax.slice_in_dim(x, length - width, length, axis=dim)
        first = lax.slice_in_dim(x, 0, width, axis=dim)
        before = lax.ppermute(last, axis, up)
        after = lax.ppermute(first, axis, down)
        x = jnp.concatenate([before, x, after], axis=dim)
    return x


def shifted(x, axis, by):
    size = lax.axis_size(axis)
    return lax.ppermute(x, axis, [(i, (i + by) % size) for i in range(size)])


def ocean_operator(vector, maskf, ocean_term):
    padded = with_halo(maskf * vector, (("gx", 1), ("gy", 0)), 1)
    beside = padded[2:, 1:-1] + padded[:-2, 1:-1] + padded[1:-1, 2:] + padded[1:-1, :-2]
    return maskf * ((4.0 + ocean_term) * vector - beside) + (1.0 - maskf) * vector


def square_total(residual):
    return lax.psum(jnp.sum(residual * residual), ("gx", "gy"))


def gather_rounds():
    rounds = []
    for axis, bits in (("gy", lax.axis_size("gy")), ("gx", lax.axis_size("gx"))):
        distances = []
        d = 1
        while d < bits:
            distances.append(d)
            d *= 2
        rounds.append([(axis, d) for d in distances])
    gy_rounds, gx_rounds = rounds
    far = gy_rounds[1::2] + gx_rounds[2:]
    near = gy_rounds[0::2] + gx_rounds[1:2] + gx_rounds[:1]
    return far + near


def stack_gather(tile, rounds):
    x = tile[None]
    for axis, distance in rounds:
        size = lax.axis_size(axis)
        other = lax.ppermute(x, axis, [(j, j ^ distance) for j in range(size)])
        x = jnp.concatenate([x, other], axis=0)
    return x


def grid_operator(vector, maskf, ocean_term):
    padded = jnp.pad(maskf * vector, 1)
    beside = padded[2:, 1:-1] + padded[:-2, 1:-1] + padded[1:-1, 2:] + padded[1:-1, :-2]
    return maskf * ((4.0 + ocean_term) * vector - beside) + (1.0 - maskf) * vector


HALO = 4
LEVEL_BLOCK = 16


def diffusion_kernel(kappa_ref, weight_ref, core_ref, lanes_ref, rows_ref, mask_ref, out_ref, flux_ref):
    block = pl.program_id(0)
    levels, rows, cols = core_ref.shape

    @pl.when(block == 0)
    def _():
        flux_ref[...] = jnp.zeros_like(flux_ref)

    mask = mask_ref[...]
    mask_side = mask[:rows, cols:]
    mask_low = mask[rows:, :]

    def level(l, carry):
        lev = block * levels + l
        kappa = kappa_ref[lev]
        top = jnp.concatenate([core_ref[l], lanes_ref[l]], axis=1)
        f = jnp.concatenate([top, rows_ref[l]], axis=0)
        height, width = f.shape
        for step in range(STEPS):
            beside = (
                pltpu.roll(f, height - 1, 0)
                + pltpu.roll(f, 1, 0)
                + pltpu.roll(f, width - 1, 1)
                + pltpu.roll(f, 1, 1)
            )
            f = f + kappa * (beside - 4.0 * f)
            top = jnp.concatenate([f[:rows, :cols], f[:rows, cols:] * mask_side], axis=1)
            f = jnp.concatenate([top, f[rows:, :] * mask_low], axis=0)
        core = f[:rows, :cols]
        out_ref[l] = core
        for c in range(flux_ref.shape[0]):
            flux_ref[c] += weight_ref[c, lev] * core
        return carry

    lax.fori_loop(0, levels, level, 0, unroll=8)


def diffuse(field, atm_kappa, vert_weight):
    levels, rows, cols = field.shape
    comps = vert_weight.shape[0]
    count_gx = lax.axis_size("gx")
    count_gy = lax.axis_size("gy")
    gx_index = lax.axis_index("gx")
    gy_index = lax.axis_index("gy")
    up_gx = [(i, i + 1) for i in range(count_gx - 1)]
    down_gx = [(i + 1, i) for i in range(count_gx - 1)]
    up_gy = [(i, i + 1) for i in range(count_gy - 1)]
    down_gy = [(i + 1, i) for i in range(count_gy - 1)]
    pairs = lambda di, dj: [
        ((i + di) * count_gy + j + dj, i * count_gy + j)
        for i in range(count_gx)
        for j in range(count_gy)
        if 0 <= i + di < count_gx and 0 <= j + dj < count_gy
    ]
    both = ("gx", "gy")
    half = levels // 2
    south = jnp.concatenate(
        [lax.ppermute(field[l : l + half, :HALO, :], "gy", down_gy) for l in (0, half)], axis=0
    )
    north = jnp.concatenate(
        [lax.ppermute(field[l : l + half, rows - HALO :, :], "gy", up_gy) for l in (0, half)], axis=0
    )
    east = lax.ppermute(field[:, :, :HALO], "gx", down_gx)
    west = lax.ppermute(field[:, :, cols - HALO :], "gx", up_gx)
    south_east = lax.ppermute(field[:, :HALO, :HALO], both, pairs(1, 1))
    south_west = lax.ppermute(field[:, :HALO, cols - HALO :], both, pairs(-1, 1))
    north_east = lax.ppermute(field[:, rows - HALO :, :HALO], both, pairs(1, -1))
    north_west = lax.ppermute(field[:, rows - HALO :, cols - HALO :], both, pairs(-1, -1))
    gap = jnp.zeros((levels, rows, 128 - 2 * HALO), field.dtype)
    lanes = jnp.concatenate([east, gap, west], axis=2)
    corner_gap = jnp.zeros((levels, HALO, 128 - 2 * HALO), field.dtype)
    halo_rows = jnp.concatenate(
        [
            jnp.concatenate([south, south_east, corner_gap, south_west], axis=2),
            jnp.concatenate([north, north_east, corner_gap, north_west], axis=2),
        ],
        axis=1,
    )
    height = rows + 2 * HALO
    width = cols + 128
    r = jnp.arange(height, dtype=jnp.int32)
    c = jnp.arange(width, dtype=jnp.int32)
    global_r = gy_index * rows + jnp.where(r < rows + HALO, r, r - height)
    global_c = gx_index * cols + jnp.where(c < cols + HALO, c, c - width)
    inside_r = (global_r >= 0) & (global_r < count_gy * rows)
    inside_c = (global_c >= 0) & (global_c < count_gx * cols) & ((c < cols + HALO) | (c >= width - HALO))
    mask = (inside_r[:, None] & inside_c[None, :]).astype(jnp.float32)
    blocks = levels // LEVEL_BLOCK
    smem = pl.BlockSpec(memory_space=pltpu.SMEM)
    out, flux = pl.pallas_call(
        diffusion_kernel,
        grid=(blocks,),
        in_specs=[
            smem,
            smem,
            pl.BlockSpec((LEVEL_BLOCK, rows, cols), lambda b: (b, 0, 0)),
            pl.BlockSpec((LEVEL_BLOCK, rows, 128), lambda b: (b, 0, 0)),
            pl.BlockSpec((LEVEL_BLOCK, 2 * HALO, width), lambda b: (b, 0, 0)),
            pl.BlockSpec((height, width), lambda b: (0, 0)),
        ],
        out_specs=[
            pl.BlockSpec((LEVEL_BLOCK, rows, cols), lambda b: (b, 0, 0)),
            pl.BlockSpec((comps, rows, cols), lambda b: (0, 0, 0)),
        ],
        out_shape=[
            jax.ShapeDtypeStruct(field.shape, field.dtype),
            jax.ShapeDtypeStruct((comps, rows, cols), jnp.float32),
        ],
        compiler_params=pltpu.CompilerParams(dimension_semantics=("arbitrary",)),
        cost_estimate=pl.CostEstimate(
            flops=levels * height * width * STEPS * 10,
            transcendentals=0,
            bytes_accessed=2 * field.size * 4,
        ),
    )(atm_kappa, vert_weight, field, lanes, halo_rows, mask)
    return out, flux


def strip_sum(acc):
    return acc.sum(axis=0, keepdims=True).sum(axis=1, keepdims=True)


def cg_kernel(
    rounds, index_ref, rhs_stack, coded_stack, height_out, residual_out,
    rhs_ref, coded_ref, height_ref, residual_ref, pad_ref, dir_ref, img_ref,
):
    rows, cols = rhs_ref.shape
    tile_rows, tile_cols = height_out.shape
    gy = index_ref[0]
    gx = index_ref[1]

    def place(k, carry):
        gy_off = 0
        gx_off = 0
        for bit, (axis, distance) in enumerate(rounds):
            flag = lax.shift_right_logical(k, bit) & 1
            if axis == "gy":
                gy_off = gy_off + flag * distance
            else:
                gx_off = gx_off + flag * distance
        r0 = pl.multiple_of(lax.bitwise_xor(gy, gy_off) * tile_rows, tile_rows)
        c0 = pl.multiple_of(lax.bitwise_xor(gx, gx_off) * tile_cols, tile_cols)
        rhs_ref[pl.ds(r0, tile_rows), pl.ds(c0, tile_cols)] = rhs_stack[k]
        coded_ref[pl.ds(r0, tile_rows), pl.ds(c0, tile_cols)] = coded_stack[k]
        return carry

    lax.fori_loop(0, rhs_stack.shape[0], place, 0, unroll=4)
    strips = rows // 8
    zeros = jnp.zeros((8, cols), jnp.float32)
    pad_ref[0:8, :] = zeros
    pad_ref[rows + 8 : rows + 16, :] = zeros
    row = lax.broadcasted_iota(jnp.int32, (8, cols), 0)
    col = lax.broadcasted_iota(jnp.int32, (8, cols), 1)

    def at(k, offset=0):
        return pl.ds(pl.multiple_of(k * 8 + offset, 8), 8)

    def init(k, acc):
        v = rhs_ref[at(k), :]
        m = (coded_ref[at(k), :] >= 0.0).astype(jnp.float32)
        residual_ref[at(k), :] = v
        dir_ref[at(k), :] = v
        height_ref[at(k), :] = jnp.zeros_like(v)
        pad_ref[at(k, 8), :] = m * v
        return acc + v * v

    def image(k, acc):
        prev = pad_ref[at(k), :]
        cur = pad_ref[at(k, 8), :]
        nxt = pad_ref[at(k, 16), :]
        south = jnp.where(row == 7, pltpu.roll(nxt, 7, 0), pltpu.roll(cur, 7, 0))
        north = jnp.where(row == 0, pltpu.roll(prev, 1, 0), pltpu.roll(cur, 1, 0))
        east = jnp.where(col == cols - 1, 0.0, pltpu.roll(cur, cols - 1, 1))
        west = jnp.where(col == 0, 0.0, pltpu.roll(cur, 1, 1))
        beside = south + north + east + west
        ot = coded_ref[at(k), :]
        m = (ot >= 0.0).astype(jnp.float32)
        v = dir_ref[at(k), :]
        w = m * ((4.0 + ot) * v - beside) + (1.0 - m) * v
        img_ref[at(k), :] = w
        return acc + v * w

    norm_now = strip_sum(lax.fori_loop(0, strips, init, zeros, unroll=8))
    for step in range(ITERS):
        alpha = norm_now / strip_sum(lax.fori_loop(0, strips, image, zeros, unroll=8))

        def update(k, acc):
            v = dir_ref[at(k), :]
            height_ref[at(k), :] = height_ref[at(k), :] + alpha * v
            r = residual_ref[at(k), :] - alpha * img_ref[at(k), :]
            residual_ref[at(k), :] = r
            return acc + r * r

        norm_next = strip_sum(lax.fori_loop(0, strips, update, zeros, unroll=8))
        beta = norm_next / norm_now

        def direct(k, carry):
            d = residual_ref[at(k), :] + beta * dir_ref[at(k), :]
            dir_ref[at(k), :] = d
            m = (coded_ref[at(k), :] >= 0.0).astype(jnp.float32)
            pad_ref[at(k, 8), :] = m * d
            return carry

        if step < ITERS - 1:
            lax.fori_loop(0, strips, direct, 0, unroll=8)
        norm_now = norm_next
    r0 = pl.multiple_of(gy * tile_rows, tile_rows)
    c0 = pl.multiple_of(gx * tile_cols, tile_cols)
    height_out[...] = height_ref[pl.ds(r0, tile_rows), pl.ds(c0, tile_cols)]
    residual_out[...] = residual_ref[pl.ds(r0, tile_rows), pl.ds(c0, tile_cols)]


def solve_grid(rhs_stack, coded_stack, rounds):
    parts, tile_rows, tile_cols = rhs_stack.shape
    rows = lax.axis_size("gy") * tile_rows
    cols = lax.axis_size("gx") * tile_cols
    index = jnp.stack([lax.axis_index("gy"), lax.axis_index("gx")]).astype(jnp.int32)
    whole = pl.BlockSpec(memory_space=pltpu.VMEM)
    grid = pltpu.VMEM((rows, cols), jnp.float32)
    return pl.pallas_call(
        functools.partial(cg_kernel, rounds),
        in_specs=[pl.BlockSpec(memory_space=pltpu.SMEM), whole, whole],
        out_specs=[whole, whole],
        out_shape=[jax.ShapeDtypeStruct((tile_rows, tile_cols), jnp.float32)] * 2,
        scratch_shapes=[grid, grid, grid, grid, pltpu.VMEM((rows + 16, cols), jnp.float32), grid, grid],
    )(index, rhs_stack, coded_stack)


def body(
    atm_state, atm_kappa, vert_weight, remap_src, remap_count, remap_weight, land_mask, ocean_term
):
    levels, tile_lat, tile_lon = atm_state.shape
    kappa = atm_kappa[:, None, None]
    count_gx = lax.axis_size("gx")
    count_gy = lax.axis_size("gy")
    rounds = gather_rounds()
    coded_all = stack_gather(jnp.where(land_mask != 0, ocean_term, -1.0), rounds)
    field, flux = diffuse(atm_state, atm_kappa, vert_weight)
    flux = flux.reshape(flux.shape[0], tile_lat * tile_lon)
    ocean_blocks, lists, width, _ = remap_weight.shape
    comps = vert_weight.shape[0]
    own_blocks = tile_lat * tile_lon // width
    blocks = flux.astype(jnp.bfloat16).reshape(comps, own_blocks, width).transpose(1, 0, 2)
    devices = count_gx * count_gy
    gx_index = lax.axis_index("gx")
    gy_index = lax.axis_index("gy")
    me_index = gx_index * count_gy + gy_index
    east_index = (gx_index + 1) % count_gx * count_gy + gy_index
    west_index = (gx_index + count_gx - 1) % count_gx * count_gy + gy_index
    entries = ocean_blocks * lists
    slots = 2 * land_mask.shape[0]
    src_all = remap_src.reshape(devices, entries)
    live_all = (
        jnp.arange(lists, dtype=jnp.int32)[None, None, :]
        < remap_count.reshape(devices, ocean_blocks)[:, :, None]
    ).reshape(devices, entries)
    owner_all = src_all // own_blocks
    inside_all = src_all % own_blocks
    mine_owner = lax.dynamic_slice_in_dim(owner_all, me_index, 1, 0)[0]
    mine_inside = lax.dynamic_slice_in_dim(inside_all, me_index, 1, 0)[0]
    mine_live = lax.dynamic_slice_in_dim(live_all, me_index, 1, 0)[0]
    from_east = mine_live & (mine_owner == east_index)
    from_self = mine_live & (mine_owner == me_index)
    local_part = blocks[jnp.where(from_self, mine_inside, 0)]
    west_owner = lax.dynamic_slice_in_dim(owner_all, west_index, 1, 0)[0]
    west_inside = lax.dynamic_slice_in_dim(inside_all, west_index, 1, 0)[0]
    west_live = lax.dynamic_slice_in_dim(live_all, west_index, 1, 0)[0]
    wanted = (west_live & (west_owner == me_index)).astype(jnp.int32)
    wanted_rank = jnp.cumsum(wanted) - 1
    slot_ids = jnp.arange(slots, dtype=jnp.int32)
    picker = wanted[None, :] * (wanted_rank[None, :] == slot_ids[:, None]).astype(jnp.int32)
    send_index = jnp.sum(picker * west_inside[None, :], axis=1)
    send_valid = jnp.sum(picker, axis=1).astype(jnp.bfloat16)
    outgoing = blocks[send_index] * send_valid[:, None, None]
    incoming = shifted(outgoing, "gx", -1)
    east_int = from_east.astype(jnp.int32)
    east_rank = jnp.cumsum(east_int) - 1
    remote_part = incoming[jnp.where(from_east, east_rank, 0)]
    gathered = jnp.where(
        from_self[:, None, None],
        local_part,
        jnp.where(from_east[:, None, None], remote_part, jnp.zeros_like(local_part)),
    )
    gathered = gathered.reshape(ocean_blocks, lists, comps, width)
    ocean_rows, ocean_cols = land_mask.shape
    remapped = jnp.einsum(
        "bkij,bkcj->cbi", remap_weight, gathered, preferred_element_type=jnp.float32
    )
    ocean_flux = remapped.reshape(comps, ocean_rows, ocean_cols)
    rhs_tile = land_mask.astype(jnp.float32) * (ocean_flux[0] + ocean_flux[1])
    rhs = stack_gather(rhs_tile, rounds)
    height, residual = solve_grid(rhs, coded_all, rounds)
    return (field, ocean_flux, height, residual)


def solution(mesh):
    return jax.shard_map(
        body,
        mesh=mesh,
        in_specs=(
            P(None, "gy", "gx"),
            P(),
            P(),
            P(),
            P(),
            P(("gx", "gy"), None, None, None),
            P("gy", "gx"),
            P("gy", "gx"),
        ),
        out_specs=(P(None, "gy", "gx"), P(None, "gy", "gx"), P("gy", "gx"), P("gy", "gx")),
        check_vma=False,
    )
```

```python
import functools

import jax
import jax.numpy as jnp
from jax import lax
from jax.sharding import PartitionSpec as P
from jax.experimental import pallas as pl
from jax.experimental.pallas import tpu as pltpu

STEPS = 4
ITERS = 3


def with_halo(x, sides, width):
    for axis, dim in sides:
        size, length = (lax.axis_size(axis), x.shape[dim])
        up = [(i, (i + 1) % size) for i in range(size - 1)]
        down = [(j, i) for i, j in up]
        last = lax.slice_in_dim(x, length - width, length, axis=dim)
        first = lax.slice_in_dim(x, 0, width, axis=dim)
        before = lax.ppermute(last, axis, up)
        after = lax.ppermute(first, axis, down)
        x = jnp.concatenate([before, x, after], axis=dim)
    return x


def shifted(x, axis, by):
    size = lax.axis_size(axis)
    return lax.ppermute(x, axis, [(i, (i + by) % size) for i in range(size)])


def ocean_operator(vector, maskf, ocean_term):
    padded = with_halo(maskf * vector, (("gx", 1), ("gy", 0)), 1)
    beside = padded[2:, 1:-1] + padded[:-2, 1:-1] + padded[1:-1, 2:] + padded[1:-1, :-2]
    return maskf * ((4.0 + ocean_term) * vector - beside) + (1.0 - maskf) * vector


def square_total(residual):
    return lax.psum(jnp.sum(residual * residual), ("gx", "gy"))


def gather_rounds():
    rounds = []
    for axis, bits in (("gy", lax.axis_size("gy")), ("gx", lax.axis_size("gx"))):
        distances = []
        d = 1
        while d < bits:
            distances.append(d)
            d *= 2
        rounds.append([(axis, d) for d in distances])
    gy_rounds, gx_rounds = rounds
    far = gy_rounds[1::2] + gx_rounds[2:]
    near = gy_rounds[0::2] + gx_rounds[1:2] + gx_rounds[:1]
    return far + near


def stack_gather(tile, rounds):
    x = tile[None]
    for axis, distance in rounds:
        size = lax.axis_size(axis)
        other = lax.ppermute(x, axis, [(j, j ^ distance) for j in range(size)])
        x = jnp.concatenate([x, other], axis=0)
    return x


def grid_operator(vector, maskf, ocean_term):
    padded = jnp.pad(maskf * vector, 1)
    beside = padded[2:, 1:-1] + padded[:-2, 1:-1] + padded[1:-1, 2:] + padded[1:-1, :-2]
    return maskf * ((4.0 + ocean_term) * vector - beside) + (1.0 - maskf) * vector


HALO = 4
LEVEL_BLOCK = 32


def diffusion_kernel(kappa_ref, weight_ref, core_ref, lanes_ref, rows_ref, mask_ref, out_ref, flux_ref):
    block = pl.program_id(0)
    levels, rows, cols = core_ref.shape

    @pl.when(block == 0)
    def _():
        flux_ref[...] = jnp.zeros_like(flux_ref)

    mask = mask_ref[...]
    mask_side = mask[:rows, cols:]
    mask_low = mask[rows:, :]

    def level(l, carry):
        lev = block * levels + l
        kappa = kappa_ref[lev]
        top = jnp.concatenate([core_ref[l], lanes_ref[l]], axis=1)
        f = jnp.concatenate([top, rows_ref[l]], axis=0)
        height, width = f.shape
        for step in range(STEPS):
            beside = (
                pltpu.roll(f, height - 1, 0)
                + pltpu.roll(f, 1, 0)
                + pltpu.roll(f, width - 1, 1)
                + pltpu.roll(f, 1, 1)
            )
            f = f + kappa * (beside - 4.0 * f)
            top = jnp.concatenate([f[:rows, :cols], f[:rows, cols:] * mask_side], axis=1)
            f = jnp.concatenate([top, f[rows:, :] * mask_low], axis=0)
        core = f[:rows, :cols]
        out_ref[l] = core
        for c in range(flux_ref.shape[0]):
            flux_ref[c] += weight_ref[c, lev] * core
        return carry

    lax.fori_loop(0, levels, level, 0, unroll=8)


def diffuse(field, atm_kappa, vert_weight):
    levels, rows, cols = field.shape
    comps = vert_weight.shape[0]
    count_gx = lax.axis_size("gx")
    count_gy = lax.axis_size("gy")
    gx_index = lax.axis_index("gx")
    gy_index = lax.axis_index("gy")
    up_gx = [(i, i + 1) for i in range(count_gx - 1)]
    down_gx = [(i + 1, i) for i in range(count_gx - 1)]
    up_gy = [(i, i + 1) for i in range(count_gy - 1)]
    down_gy = [(i + 1, i) for i in range(count_gy - 1)]
    pairs = lambda di, dj: [
        ((i + di) * count_gy + j + dj, i * count_gy + j)
        for i in range(count_gx)
        for j in range(count_gy)
        if 0 <= i + di < count_gx and 0 <= j + dj < count_gy
    ]
    both = ("gx", "gy")
    south = lax.ppermute(field[:, :HALO, :], "gy", down_gy)
    north = lax.ppermute(field[:, rows - HALO :, :], "gy", up_gy)
    east = lax.ppermute(field[:, :, :HALO], "gx", down_gx)
    west = lax.ppermute(field[:, :, cols - HALO :], "gx", up_gx)
    south_east = lax.ppermute(field[:, :HALO, :HALO], both, pairs(1, 1))
    south_west = lax.ppermute(field[:, :HALO, cols - HALO :], both, pairs(-1, 1))
    north_east = lax.ppermute(field[:, rows - HALO :, :HALO], both, pairs(1, -1))
    north_west = lax.ppermute(field[:, rows - HALO :, cols - HALO :], both, pairs(-1, -1))
    gap = jnp.zeros((levels, rows, 128 - 2 * HALO), field.dtype)
    lanes = jnp.concatenate([east, gap, west], axis=2)
    corner_gap = jnp.zeros((levels, HALO, 128 - 2 * HALO), field.dtype)
    halo_rows = jnp.concatenate(
        [
            jnp.concatenate([south, south_east, corner_gap, south_west], axis=2),
            jnp.concatenate([north, north_east, corner_gap, north_west], axis=2),
        ],
        axis=1,
    )
    height = rows + 2 * HALO
    width = cols + 128
    r = jnp.arange(height, dtype=jnp.int32)
    c = jnp.arange(width, dtype=jnp.int32)
    global_r = gy_index * rows + jnp.where(r < rows + HALO, r, r - height)
    global_c = gx_index * cols + jnp.where(c < cols + HALO, c, c - width)
    inside_r = (global_r >= 0) & (global_r < count_gy * rows)
    inside_c = (global_c >= 0) & (global_c < count_gx * cols) & ((c < cols + HALO) | (c >= width - HALO))
    mask = (inside_r[:, None] & inside_c[None, :]).astype(jnp.float32)
    blocks = levels // LEVEL_BLOCK
    smem = pl.BlockSpec(memory_space=pltpu.SMEM)
    out, flux = pl.pallas_call(
        diffusion_kernel,
        grid=(blocks,),
        in_specs=[
            smem,
            smem,
            pl.BlockSpec((LEVEL_BLOCK, rows, cols), lambda b: (b, 0, 0)),
            pl.BlockSpec((LEVEL_BLOCK, rows, 128), lambda b: (b, 0, 0)),
            pl.BlockSpec((LEVEL_BLOCK, 2 * HALO, width), lambda b: (b, 0, 0)),
            pl.BlockSpec((height, width), lambda b: (0, 0)),
        ],
        out_specs=[
            pl.BlockSpec((LEVEL_BLOCK, rows, cols), lambda b: (b, 0, 0)),
            pl.BlockSpec((comps, rows, cols), lambda b: (0, 0, 0)),
        ],
        out_shape=[
            jax.ShapeDtypeStruct(field.shape, field.dtype),
            jax.ShapeDtypeStruct((comps, rows, cols), jnp.float32),
        ],
        compiler_params=pltpu.CompilerParams(dimension_semantics=("arbitrary",)),
        cost_estimate=pl.CostEstimate(
            flops=levels * height * width * STEPS * 10,
            transcendentals=0,
            bytes_accessed=2 * field.size * 4,
        ),
    )(atm_kappa, vert_weight, field, lanes, halo_rows, mask)
    return out, flux


def strip_sum(acc):
    return acc.sum(axis=0, keepdims=True).sum(axis=1, keepdims=True)


def cg_kernel(
    rounds, index_ref, rhs_stack, coded_stack, height_out, residual_out,
    rhs_ref, coded_ref, height_ref, residual_ref, pad_ref, dir_ref, img_ref,
):
    rows, cols = rhs_ref.shape
    tile_rows, tile_cols = height_out.shape
    gy = index_ref[0]
    gx = index_ref[1]

    def place(k, carry):
        gy_off = 0
        gx_off = 0
        for bit, (axis, distance) in enumerate(rounds):
            flag = lax.shift_right_logical(k, bit) & 1
            if axis == "gy":
                gy_off = gy_off + flag * distance
            else:
                gx_off = gx_off + flag * distance
        r0 = pl.multiple_of(lax.bitwise_xor(gy, gy_off) * tile_rows, tile_rows)
        c0 = pl.multiple_of(lax.bitwise_xor(gx, gx_off) * tile_cols, tile_cols)
        rhs_ref[pl.ds(r0, tile_rows), pl.ds(c0, tile_cols)] = rhs_stack[k]
        coded_ref[pl.ds(r0, tile_rows), pl.ds(c0, tile_cols)] = coded_stack[k]
        return carry

    lax.fori_loop(0, rhs_stack.shape[0], place, 0, unroll=4)
    strips = rows // 8
    zeros = jnp.zeros((8, cols), jnp.float32)
    pad_ref[0:8, :] = zeros
    pad_ref[rows + 8 : rows + 16, :] = zeros
    row = lax.broadcasted_iota(jnp.int32, (8, cols), 0)
    col = lax.broadcasted_iota(jnp.int32, (8, cols), 1)

    def at(k, offset=0):
        return pl.ds(pl.multiple_of(k * 8 + offset, 8), 8)

    def init(k, acc):
        v = rhs_ref[at(k), :]
        m = (coded_ref[at(k), :] >= 0.0).astype(jnp.float32)
        residual_ref[at(k), :] = v
        dir_ref[at(k), :] = v
        height_ref[at(k), :] = jnp.zeros_like(v)
        pad_ref[at(k, 8), :] = m * v
        return acc + v * v

    def image(k, acc):
        prev = pad_ref[at(k), :]
        cur = pad_ref[at(k, 8), :]
        nxt = pad_ref[at(k, 16), :]
        south = jnp.where(row == 7, pltpu.roll(nxt, 7, 0), pltpu.roll(cur, 7, 0))
        north = jnp.where(row == 0, pltpu.roll(prev, 1, 0), pltpu.roll(cur, 1, 0))
        east = jnp.where(col == cols - 1, 0.0, pltpu.roll(cur, cols - 1, 1))
        west = jnp.where(col == 0, 0.0, pltpu.roll(cur, 1, 1))
        beside = south + north + east + west
        ot = coded_ref[at(k), :]
        m = (ot >= 0.0).astype(jnp.float32)
        v = dir_ref[at(k), :]
        w = m * ((4.0 + ot) * v - beside) + (1.0 - m) * v
        img_ref[at(k), :] = w
        return acc + v * w

    norm_now = strip_sum(lax.fori_loop(0, strips, init, zeros, unroll=8))
    for step in range(ITERS):
        alpha = norm_now / strip_sum(lax.fori_loop(0, strips, image, zeros, unroll=8))

        def update(k, acc):
            v = dir_ref[at(k), :]
            height_ref[at(k), :] = height_ref[at(k), :] + alpha * v
            r = residual_ref[at(k), :] - alpha * img_ref[at(k), :]
            residual_ref[at(k), :] = r
            return acc + r * r

        norm_next = strip_sum(lax.fori_loop(0, strips, update, zeros, unroll=8))
        beta = norm_next / norm_now

        def direct(k, carry):
            d = residual_ref[at(k), :] + beta * dir_ref[at(k), :]
            dir_ref[at(k), :] = d
            m = (coded_ref[at(k), :] >= 0.0).astype(jnp.float32)
            pad_ref[at(k, 8), :] = m * d
            return carry

        if step < ITERS - 1:
            lax.fori_loop(0, strips, direct, 0, unroll=8)
        norm_now = norm_next
    r0 = pl.multiple_of(gy * tile_rows, tile_rows)
    c0 = pl.multiple_of(gx * tile_cols, tile_cols)
    height_out[...] = height_ref[pl.ds(r0, tile_rows), pl.ds(c0, tile_cols)]
    residual_out[...] = residual_ref[pl.ds(r0, tile_rows), pl.ds(c0, tile_cols)]


def solve_grid(rhs_stack, coded_stack, rounds):
    parts, tile_rows, tile_cols = rhs_stack.shape
    rows = lax.axis_size("gy") * tile_rows
    cols = lax.axis_size("gx") * tile_cols
    index = jnp.stack([lax.axis_index("gy"), lax.axis_index("gx")]).astype(jnp.int32)
    whole = pl.BlockSpec(memory_space=pltpu.VMEM)
    grid = pltpu.VMEM((rows, cols), jnp.float32)
    return pl.pallas_call(
        functools.partial(cg_kernel, rounds),
        in_specs=[pl.BlockSpec(memory_space=pltpu.SMEM), whole, whole],
        out_specs=[whole, whole],
        out_shape=[jax.ShapeDtypeStruct((tile_rows, tile_cols), jnp.float32)] * 2,
        scratch_shapes=[grid, grid, grid, grid, pltpu.VMEM((rows + 16, cols), jnp.float32), grid, grid],
    )(index, rhs_stack, coded_stack)


def body(
    atm_state, atm_kappa, vert_weight, remap_src, remap_count, remap_weight, land_mask, ocean_term
):
    levels, tile_lat, tile_lon = atm_state.shape
    kappa = atm_kappa[:, None, None]
    count_gx = lax.axis_size("gx")
    count_gy = lax.axis_size("gy")
    rounds = gather_rounds()
    coded_all = stack_gather(jnp.where(land_mask != 0, ocean_term, -1.0), rounds)
    field, flux = diffuse(atm_state, atm_kappa, vert_weight)
    flux = flux.reshape(flux.shape[0], tile_lat * tile_lon)
    ocean_blocks, lists, width, _ = remap_weight.shape
    comps = vert_weight.shape[0]
    own_blocks = tile_lat * tile_lon // width
    blocks = flux.astype(jnp.bfloat16).reshape(comps, own_blocks, width).transpose(1, 0, 2)
    devices = count_gx * count_gy
    gx_index = lax.axis_index("gx")
    gy_index = lax.axis_index("gy")
    me_index = gx_index * count_gy + gy_index
    east_index = (gx_index + 1) % count_gx * count_gy + gy_index
    west_index = (gx_index + count_gx - 1) % count_gx * count_gy + gy_index
    entries = ocean_blocks * lists
    slots = 2 * land_mask.shape[0]
    src_all = remap_src.reshape(devices, entries)
    live_all = (
        jnp.arange(lists, dtype=jnp.int32)[None, None, :]
        < remap_count.reshape(devices, ocean_blocks)[:, :, None]
    ).reshape(devices, entries)
    owner_all = src_all // own_blocks
    inside_all = src_all % own_blocks
    mine_owner = lax.dynamic_slice_in_dim(owner_all, me_index, 1, 0)[0]
    mine_inside = lax.dynamic_slice_in_dim(inside_all, me_index, 1, 0)[0]
    mine_live = lax.dynamic_slice_in_dim(live_all, me_index, 1, 0)[0]
    from_east = mine_live & (mine_owner == east_index)
    from_self = mine_live & (mine_owner == me_index)
    local_part = blocks[jnp.where(from_self, mine_inside, 0)]
    west_owner = lax.dynamic_slice_in_dim(owner_all, west_index, 1, 0)[0]
    west_inside = lax.dynamic_slice_in_dim(inside_all, west_index, 1, 0)[0]
    west_live = lax.dynamic_slice_in_dim(live_all, west_index, 1, 0)[0]
    wanted = (west_live & (west_owner == me_index)).astype(jnp.int32)
    wanted_rank = jnp.cumsum(wanted) - 1
    slot_ids = jnp.arange(slots, dtype=jnp.int32)
    picker = wanted[None, :] * (wanted_rank[None, :] == slot_ids[:, None]).astype(jnp.int32)
    send_index = jnp.sum(picker * west_inside[None, :], axis=1)
    send_valid = jnp.sum(picker, axis=1).astype(jnp.bfloat16)
    outgoing = blocks[send_index] * send_valid[:, None, None]
    incoming = shifted(outgoing, "gx", -1)
    east_int = from_east.astype(jnp.int32)
    east_rank = jnp.cumsum(east_int) - 1
    remote_part = incoming[jnp.where(from_east, east_rank, 0)]
    gathered = jnp.where(
        from_self[:, None, None],
        local_part,
        jnp.where(from_east[:, None, None], remote_part, jnp.zeros_like(local_part)),
    )
    gathered = gathered.reshape(ocean_blocks, lists, comps, width)
    ocean_rows, ocean_cols = land_mask.shape
    remapped = jnp.einsum(
        "bkij,bkcj->cbi", remap_weight, gathered, preferred_element_type=jnp.float32
    )
    ocean_flux = remapped.reshape(comps, ocean_rows, ocean_cols)
    rhs_tile = land_mask.astype(jnp.float32) * (ocean_flux[0] + ocean_flux[1])
    rhs = stack_gather(rhs_tile, rounds)
    height, residual = solve_grid(rhs, coded_all, rounds)
    return (field, ocean_flux, height, residual)


def solution(mesh):
    return jax.shard_map(
        body,
        mesh=mesh,
        in_specs=(
            P(None, "gy", "gx"),
            P(),
            P(),
            P(),
            P(),
            P(("gx", "gy"), None, None, None),
            P("gy", "gx"),
            P("gy", "gx"),
        ),
        out_specs=(P(None, "gy", "gx"), P(None, "gy", "gx"), P("gy", "gx"), P("gy", "gx")),
        check_vma=False,
    )
```

```python
import functools

import jax
import jax.numpy as jnp
from jax import lax
from jax.sharding import PartitionSpec as P
from jax.experimental import pallas as pl
from jax.experimental.pallas import tpu as pltpu

STEPS = 4
ITERS = 3


def with_halo(x, sides, width):
    for axis, dim in sides:
        size, length = (lax.axis_size(axis), x.shape[dim])
        up = [(i, (i + 1) % size) for i in range(size - 1)]
        down = [(j, i) for i, j in up]
        last = lax.slice_in_dim(x, length - width, length, axis=dim)
        first = lax.slice_in_dim(x, 0, width, axis=dim)
        before = lax.ppermute(last, axis, up)
        after = lax.ppermute(first, axis, down)
        x = jnp.concatenate([before, x, after], axis=dim)
    return x


def shifted(x, axis, by):
    size = lax.axis_size(axis)
    return lax.ppermute(x, axis, [(i, (i + by) % size) for i in range(size)])


def ocean_operator(vector, maskf, ocean_term):
    padded = with_halo(maskf * vector, (("gx", 1), ("gy", 0)), 1)
    beside = padded[2:, 1:-1] + padded[:-2, 1:-1] + padded[1:-1, 2:] + padded[1:-1, :-2]
    return maskf * ((4.0 + ocean_term) * vector - beside) + (1.0 - maskf) * vector


def square_total(residual):
    return lax.psum(jnp.sum(residual * residual), ("gx", "gy"))


def gather_rounds():
    rounds = []
    for axis, bits in (("gy", lax.axis_size("gy")), ("gx", lax.axis_size("gx"))):
        distances = []
        d = 1
        while d < bits:
            distances.append(d)
            d *= 2
        rounds.append([(axis, d) for d in distances])
    gy_rounds, gx_rounds = rounds
    far = gy_rounds[1::2] + gx_rounds[2:]
    near = gy_rounds[0::2] + gx_rounds[1:2] + gx_rounds[:1]
    return far + near


def stack_gather(tile, rounds):
    x = tile[None]
    for axis, distance in rounds:
        size = lax.axis_size(axis)
        other = lax.ppermute(x, axis, [(j, j ^ distance) for j in range(size)])
        x = jnp.concatenate([x, other], axis=0)
    return x


def grid_operator(vector, maskf, ocean_term):
    padded = jnp.pad(maskf * vector, 1)
    beside = padded[2:, 1:-1] + padded[:-2, 1:-1] + padded[1:-1, 2:] + padded[1:-1, :-2]
    return maskf * ((4.0 + ocean_term) * vector - beside) + (1.0 - maskf) * vector


HALO = 4
LEVEL_BLOCK = 16


def diffusion_kernel(kappa_ref, weight_ref, core_ref, lanes_ref, rows_ref, mask_ref, out_ref, flux_ref):
    block = pl.program_id(0)
    levels, rows, cols = core_ref.shape

    @pl.when(block == 0)
    def _():
        flux_ref[...] = jnp.zeros_like(flux_ref)

    mask = mask_ref[...]
    mask_side = mask[:rows, cols:]
    mask_low = mask[rows:, :]

    def level(l, carry):
        lev = block * levels + l
        kappa = kappa_ref[lev]
        top = jnp.concatenate([core_ref[l], lanes_ref[l]], axis=1)
        f = jnp.concatenate([top, rows_ref[l]], axis=0)
        height, width = f.shape
        for step in range(STEPS):
            beside = (
                pltpu.roll(f, height - 1, 0)
                + pltpu.roll(f, 1, 0)
                + pltpu.roll(f, width - 1, 1)
                + pltpu.roll(f, 1, 1)
            )
            f = f + kappa * (beside - 4.0 * f)
            top = jnp.concatenate([f[:rows, :cols], f[:rows, cols:] * mask_side], axis=1)
            f = jnp.concatenate([top, f[rows:, :] * mask_low], axis=0)
        core = f[:rows, :cols]
        out_ref[l] = core
        for c in range(flux_ref.shape[0]):
            flux_ref[c] += weight_ref[c, lev] * core
        return carry

    lax.fori_loop(0, levels, level, 0, unroll=8)


def diffuse(field, atm_kappa, vert_weight):
    levels, rows, cols = field.shape
    comps = vert_weight.shape[0]
    count_gx = lax.axis_size("gx")
    count_gy = lax.axis_size("gy")
    gx_index = lax.axis_index("gx")
    gy_index = lax.axis_index("gy")
    up_gx = [(i, i + 1) for i in range(count_gx - 1)]
    down_gx = [(i + 1, i) for i in range(count_gx - 1)]
    up_gy = [(i, i + 1) for i in range(count_gy - 1)]
    down_gy = [(i + 1, i) for i in range(count_gy - 1)]
    pairs = lambda di, dj: [
        ((i + di) * count_gy + j + dj, i * count_gy + j)
        for i in range(count_gx)
        for j in range(count_gy)
        if 0 <= i + di < count_gx and 0 <= j + dj < count_gy
    ]
    both = ("gx", "gy")
    south = lax.ppermute(field[:, :HALO, :], "gy", down_gy)
    north = lax.ppermute(field[:, rows - HALO :, :], "gy", up_gy)
    east = lax.ppermute(field[:, :, :HALO], "gx", down_gx)
    west = lax.ppermute(field[:, :, cols - HALO :], "gx", up_gx)
    south_east = lax.ppermute(field[:, :HALO, :HALO], both, pairs(1, 1))
    south_west = lax.ppermute(field[:, :HALO, cols - HALO :], both, pairs(-1, 1))
    north_east = lax.ppermute(field[:, rows - HALO :, :HALO], both, pairs(1, -1))
    north_west = lax.ppermute(field[:, rows - HALO :, cols - HALO :], both, pairs(-1, -1))
    gap = jnp.zeros((levels, rows, 128 - 2 * HALO), field.dtype)
    lanes = jnp.concatenate([east, gap, west], axis=2)
    corner_gap = jnp.zeros((levels, HALO, 128 - 2 * HALO), field.dtype)
    halo_rows = jnp.concatenate(
        [
            jnp.concatenate([south, south_east, corner_gap, south_west], axis=2),
            jnp.concatenate([north, north_east, corner_gap, north_west], axis=2),
        ],
        axis=1,
    )
    height = rows + 2 * HALO
    width = cols + 128
    r = jnp.arange(height, dtype=jnp.int32)
    c = jnp.arange(width, dtype=jnp.int32)
    global_r = gy_index * rows + jnp.where(r < rows + HALO, r, r - height)
    global_c = gx_index * cols + jnp.where(c < cols + HALO, c, c - width)
    inside_r = (global_r >= 0) & (global_r < count_gy * rows)
    inside_c = (global_c >= 0) & (global_c < count_gx * cols) & ((c < cols + HALO) | (c >= width - HALO))
    mask = (inside_r[:, None] & inside_c[None, :]).astype(jnp.float32)
    blocks = levels // LEVEL_BLOCK
    smem = pl.BlockSpec(memory_space=pltpu.SMEM)
    out, flux = pl.pallas_call(
        diffusion_kernel,
        grid=(blocks,),
        in_specs=[
            smem,
            smem,
            pl.BlockSpec((LEVEL_BLOCK, rows, cols), lambda b: (b, 0, 0)),
            pl.BlockSpec((LEVEL_BLOCK, rows, 128), lambda b: (b, 0, 0)),
            pl.BlockSpec((LEVEL_BLOCK, 2 * HALO, width), lambda b: (b, 0, 0)),
            pl.BlockSpec((height, width), lambda b: (0, 0)),
        ],
        out_specs=[
            pl.BlockSpec((LEVEL_BLOCK, rows, cols), lambda b: (b, 0, 0)),
            pl.BlockSpec((comps, rows, cols), lambda b: (0, 0, 0)),
        ],
        out_shape=[
            jax.ShapeDtypeStruct(field.shape, field.dtype),
            jax.ShapeDtypeStruct((comps, rows, cols), jnp.float32),
        ],
        compiler_params=pltpu.CompilerParams(dimension_semantics=("arbitrary",)),
        cost_estimate=pl.CostEstimate(
            flops=levels * height * width * STEPS * 10,
            transcendentals=0,
            bytes_accessed=2 * field.size * 4,
        ),
    )(atm_kappa, vert_weight, field, lanes, halo_rows, mask)
    return out, flux


def strip_sum(acc):
    return acc.sum(axis=0, keepdims=True).sum(axis=1, keepdims=True)


def cg_kernel(
    rounds, index_ref, rhs_stack, coded_stack, height_out, residual_out,
    rhs_ref, coded_ref, height_ref, residual_ref, pad_ref, dir_ref, img_ref,
):
    rows, cols = rhs_ref.shape
    tile_rows, tile_cols = height_out.shape
    gy = index_ref[0]
    gx = index_ref[1]

    def place(k, carry):
        gy_off = 0
        gx_off = 0
        for bit, (axis, distance) in enumerate(rounds):
            flag = lax.shift_right_logical(k, bit) & 1
            if axis == "gy":
                gy_off = gy_off + flag * distance
            else:
                gx_off = gx_off + flag * distance
        r0 = pl.multiple_of(lax.bitwise_xor(gy, gy_off) * tile_rows, tile_rows)
        c0 = pl.multiple_of(lax.bitwise_xor(gx, gx_off) * tile_cols, tile_cols)
        rhs_ref[pl.ds(r0, tile_rows), pl.ds(c0, tile_cols)] = rhs_stack[k]
        coded_ref[pl.ds(r0, tile_rows), pl.ds(c0, tile_cols)] = coded_stack[k]
        return carry

    lax.fori_loop(0, rhs_stack.shape[0], place, 0, unroll=4)
    strips = rows // 8
    zeros = jnp.zeros((8, cols), jnp.float32)
    pad_ref[0:8, :] = zeros
    pad_ref[rows + 8 : rows + 16, :] = zeros
    row = lax.broadcasted_iota(jnp.int32, (8, cols), 0)
    col = lax.broadcasted_iota(jnp.int32, (8, cols), 1)

    def at(k, offset=0):
        return pl.ds(pl.multiple_of(k * 8 + offset, 8), 8)

    def init(k, acc):
        v = rhs_ref[at(k), :]
        m = (coded_ref[at(k), :] >= 0.0).astype(jnp.float32)
        residual_ref[at(k), :] = v
        dir_ref[at(k), :] = v
        height_ref[at(k), :] = jnp.zeros_like(v)
        pad_ref[at(k, 8), :] = m * v
        return acc + v * v

    def image(k, acc):
        prev = pad_ref[at(k), :]
        cur = pad_ref[at(k, 8), :]
        nxt = pad_ref[at(k, 16), :]
        south = jnp.where(row == 7, pltpu.roll(nxt, 7, 0), pltpu.roll(cur, 7, 0))
        north = jnp.where(row == 0, pltpu.roll(prev, 1, 0), pltpu.roll(cur, 1, 0))
        east = jnp.where(col == cols - 1, 0.0, pltpu.roll(cur, cols - 1, 1))
        west = jnp.where(col == 0, 0.0, pltpu.roll(cur, 1, 1))
        beside = south + north + east + west
        ot = coded_ref[at(k), :]
        m = (ot >= 0.0).astype(jnp.float32)
        v = dir_ref[at(k), :]
        w = m * ((4.0 + ot) * v - beside) + (1.0 - m) * v
        img_ref[at(k), :] = w
        return acc + v * w

    norm_now = strip_sum(lax.fori_loop(0, strips, init, zeros, unroll=8))
    dot = strip_sum(lax.fori_loop(0, strips, image, zeros, unroll=8))
    for step in range(ITERS):
        alpha = norm_now / dot

        def update(k, acc):
            v = dir_ref[at(k), :]
            height_ref[at(k), :] = height_ref[at(k), :] + alpha * v
            r = residual_ref[at(k), :] - alpha * img_ref[at(k), :]
            residual_ref[at(k), :] = r
            return acc + r * r

        norm_next = strip_sum(lax.fori_loop(0, strips, update, zeros, unroll=8))
        beta = norm_next / norm_now

        def direct(k, carry):
            d = residual_ref[at(k), :] + beta * dir_ref[at(k), :]
            dir_ref[at(k), :] = d
            m = (coded_ref[at(k), :] >= 0.0).astype(jnp.float32)
            pad_ref[at(k, 8), :] = m * d
            return carry

        def direct_then_image(k, acc):
            direct(k, 0)
            return image(k - 1, acc)

        if step < ITERS - 1:
            direct(0, 0)
            acc = lax.fori_loop(1, strips, direct_then_image, zeros, unroll=8)
            dot = strip_sum(image(strips - 1, acc))
        norm_now = norm_next
    r0 = pl.multiple_of(gy * tile_rows, tile_rows)
    c0 = pl.multiple_of(gx * tile_cols, tile_cols)
    height_out[...] = height_ref[pl.ds(r0, tile_rows), pl.ds(c0, tile_cols)]
    residual_out[...] = residual_ref[pl.ds(r0, tile_rows), pl.ds(c0, tile_cols)]


def solve_grid(rhs_stack, coded_stack, rounds):
    parts, tile_rows, tile_cols = rhs_stack.shape
    rows = lax.axis_size("gy") * tile_rows
    cols = lax.axis_size("gx") * tile_cols
    index = jnp.stack([lax.axis_index("gy"), lax.axis_index("gx")]).astype(jnp.int32)
    whole = pl.BlockSpec(memory_space=pltpu.VMEM)
    grid = pltpu.VMEM((rows, cols), jnp.float32)
    return pl.pallas_call(
        functools.partial(cg_kernel, rounds),
        in_specs=[pl.BlockSpec(memory_space=pltpu.SMEM), whole, whole],
        out_specs=[whole, whole],
        out_shape=[jax.ShapeDtypeStruct((tile_rows, tile_cols), jnp.float32)] * 2,
        scratch_shapes=[grid, grid, grid, grid, pltpu.VMEM((rows + 16, cols), jnp.float32), grid, grid],
    )(index, rhs_stack, coded_stack)


def body(
    atm_state, atm_kappa, vert_weight, remap_src, remap_count, remap_weight, land_mask, ocean_term
):
    levels, tile_lat, tile_lon = atm_state.shape
    kappa = atm_kappa[:, None, None]
    count_gx = lax.axis_size("gx")
    count_gy = lax.axis_size("gy")
    rounds = gather_rounds()
    coded_all = stack_gather(jnp.where(land_mask != 0, ocean_term, -1.0), rounds)
    field, flux = diffuse(atm_state, atm_kappa, vert_weight)
    flux = flux.reshape(flux.shape[0], tile_lat * tile_lon)
    ocean_blocks, lists, width, _ = remap_weight.shape
    comps = vert_weight.shape[0]
    own_blocks = tile_lat * tile_lon // width
    blocks = flux.astype(jnp.bfloat16).reshape(comps, own_blocks, width).transpose(1, 0, 2)
    devices = count_gx * count_gy
    gx_index = lax.axis_index("gx")
    gy_index = lax.axis_index("gy")
    me_index = gx_index * count_gy + gy_index
    east_index = (gx_index + 1) % count_gx * count_gy + gy_index
    west_index = (gx_index + count_gx - 1) % count_gx * count_gy + gy_index
    entries = ocean_blocks * lists
    slots = 2 * land_mask.shape[0]
    src_all = remap_src.reshape(devices, entries)
    live_all = (
        jnp.arange(lists, dtype=jnp.int32)[None, None, :]
        < remap_count.reshape(devices, ocean_blocks)[:, :, None]
    ).reshape(devices, entries)
    owner_all = src_all // own_blocks
    inside_all = src_all % own_blocks
    mine_owner = lax.dynamic_slice_in_dim(owner_all, me_index, 1, 0)[0]
    mine_inside = lax.dynamic_slice_in_dim(inside_all, me_index, 1, 0)[0]
    mine_live = lax.dynamic_slice_in_dim(live_all, me_index, 1, 0)[0]
    from_east = mine_live & (mine_owner == east_index)
    from_self = mine_live & (mine_owner == me_index)
    local_part = blocks[jnp.where(from_self, mine_inside, 0)]
    west_owner = lax.dynamic_slice_in_dim(owner_all, west_index, 1, 0)[0]
    west_inside = lax.dynamic_slice_in_dim(inside_all, west_index, 1, 0)[0]
    west_live = lax.dynamic_slice_in_dim(live_all, west_index, 1, 0)[0]
    wanted = (west_live & (west_owner == me_index)).astype(jnp.int32)
    wanted_rank = jnp.cumsum(wanted) - 1
    slot_ids = jnp.arange(slots, dtype=jnp.int32)
    picker = wanted[None, :] * (wanted_rank[None, :] == slot_ids[:, None]).astype(jnp.int32)
    send_index = jnp.sum(picker * west_inside[None, :], axis=1)
    send_valid = jnp.sum(picker, axis=1).astype(jnp.bfloat16)
    outgoing = blocks[send_index] * send_valid[:, None, None]
    incoming = shifted(outgoing, "gx", -1)
    east_int = from_east.astype(jnp.int32)
    east_rank = jnp.cumsum(east_int) - 1
    remote_part = incoming[jnp.where(from_east, east_rank, 0)]
    gathered = jnp.where(
        from_self[:, None, None],
        local_part,
        jnp.where(from_east[:, None, None], remote_part, jnp.zeros_like(local_part)),
    )
    gathered = gathered.reshape(ocean_blocks, lists, comps, width)
    ocean_rows, ocean_cols = land_mask.shape
    remapped = jnp.einsum(
        "bkij,bkcj->cbi", remap_weight, gathered, preferred_element_type=jnp.float32
    )
    ocean_flux = remapped.reshape(comps, ocean_rows, ocean_cols)
    rhs_tile = land_mask.astype(jnp.float32) * (ocean_flux[0] + ocean_flux[1])
    rhs = stack_gather(rhs_tile, rounds)
    height, residual = solve_grid(rhs, coded_all, rounds)
    return (field, ocean_flux, height, residual)


def solution(mesh):
    return jax.shard_map(
        body,
        mesh=mesh,
        in_specs=(
            P(None, "gy", "gx"),
            P(),
            P(),
            P(),
            P(),
            P(("gx", "gy"), None, None, None),
            P("gy", "gx"),
            P("gy", "gx"),
        ),
        out_specs=(P(None, "gy", "gx"), P(None, "gy", "gx"), P("gy", "gx"), P("gy", "gx")),
        check_vma=False,
    )
```

```python
import functools

import jax
import jax.numpy as jnp
from jax import lax
from jax.sharding import PartitionSpec as P
from jax.experimental import pallas as pl
from jax.experimental.pallas import tpu as pltpu

STEPS = 4
ITERS = 3


def with_halo(x, sides, width):
    for axis, dim in sides:
        size, length = (lax.axis_size(axis), x.shape[dim])
        up = [(i, (i + 1) % size) for i in range(size - 1)]
        down = [(j, i) for i, j in up]
        last = lax.slice_in_dim(x, length - width, length, axis=dim)
        first = lax.slice_in_dim(x, 0, width, axis=dim)
        before = lax.ppermute(last, axis, up)
        after = lax.ppermute(first, axis, down)
        x = jnp.concatenate([before, x, after], axis=dim)
    return x


def shifted(x, axis, by):
    size = lax.axis_size(axis)
    return lax.ppermute(x, axis, [(i, (i + by) % size) for i in range(size)])


def ocean_operator(vector, maskf, ocean_term):
    padded = with_halo(maskf * vector, (("gx", 1), ("gy", 0)), 1)
    beside = padded[2:, 1:-1] + padded[:-2, 1:-1] + padded[1:-1, 2:] + padded[1:-1, :-2]
    return maskf * ((4.0 + ocean_term) * vector - beside) + (1.0 - maskf) * vector


def square_total(residual):
    return lax.psum(jnp.sum(residual * residual), ("gx", "gy"))


def gather_rounds():
    rounds = []
    for axis, bits in (("gy", lax.axis_size("gy")), ("gx", lax.axis_size("gx"))):
        distances = []
        d = 1
        while d < bits:
            distances.append(d)
            d *= 2
        rounds.append([(axis, d) for d in distances])
    gy_rounds, gx_rounds = rounds
    far = gy_rounds[1::2] + gx_rounds[2:]
    near = gy_rounds[0::2] + gx_rounds[1:2] + gx_rounds[:1]
    return far + near


def stack_gather(tile, rounds):
    x = tile[None]
    for axis, distance in rounds:
        size = lax.axis_size(axis)
        other = lax.ppermute(x, axis, [(j, j ^ distance) for j in range(size)])
        x = jnp.concatenate([x, other], axis=0)
    return x


def grid_operator(vector, maskf, ocean_term):
    padded = jnp.pad(maskf * vector, 1)
    beside = padded[2:, 1:-1] + padded[:-2, 1:-1] + padded[1:-1, 2:] + padded[1:-1, :-2]
    return maskf * ((4.0 + ocean_term) * vector - beside) + (1.0 - maskf) * vector


HALO = 4
LEVEL_BLOCK = 16


def diffusion_kernel(kappa_ref, weight_ref, core_ref, lanes_ref, rows_ref, mask_ref, out_ref, flux_ref):
    block = pl.program_id(0)
    levels, rows, cols = core_ref.shape

    @pl.when(block == 0)
    def _():
        flux_ref[...] = jnp.zeros_like(flux_ref)

    mask = mask_ref[...]
    mask_side = mask[:rows, cols:]
    mask_low = mask[rows:, :]

    def level(l, carry):
        lev = block * levels + l
        kappa = kappa_ref[lev]
        top = jnp.concatenate([core_ref[l], lanes_ref[l]], axis=1)
        f = jnp.concatenate([top, rows_ref[l]], axis=0)
        height, width = f.shape
        for step in range(STEPS):
            beside = (
                pltpu.roll(f, height - 1, 0)
                + pltpu.roll(f, 1, 0)
                + pltpu.roll(f, width - 1, 1)
                + pltpu.roll(f, 1, 1)
            )
            f = f + kappa * (beside - 4.0 * f)
            top = jnp.concatenate([f[:rows, :cols], f[:rows, cols:] * mask_side], axis=1)
            f = jnp.concatenate([top, f[rows:, :] * mask_low], axis=0)
        core = f[:rows, :cols]
        out_ref[l] = core
        for c in range(flux_ref.shape[0]):
            flux_ref[c] += weight_ref[c, lev] * core
        return carry

    lax.fori_loop(0, levels, level, 0, unroll=8)


def diffuse(field, atm_kappa, vert_weight):
    levels, rows, cols = field.shape
    comps = vert_weight.shape[0]
    count_gx = lax.axis_size("gx")
    count_gy = lax.axis_size("gy")
    gx_index = lax.axis_index("gx")
    gy_index = lax.axis_index("gy")
    up_gx = [(i, i + 1) for i in range(count_gx - 1)]
    down_gx = [(i + 1, i) for i in range(count_gx - 1)]
    up_gy = [(i, i + 1) for i in range(count_gy - 1)]
    down_gy = [(i + 1, i) for i in range(count_gy - 1)]
    pairs = lambda di, dj: [
        ((i + di) * count_gy + j + dj, i * count_gy + j)
        for i in range(count_gx)
        for j in range(count_gy)
        if 0 <= i + di < count_gx and 0 <= j + dj < count_gy
    ]
    both = ("gx", "gy")
    south = lax.ppermute(field[:, :HALO, :], "gy", down_gy)
    north = lax.ppermute(field[:, rows - HALO :, :], "gy", up_gy)
    east = lax.ppermute(field[:, :, :HALO], "gx", down_gx)
    west = lax.ppermute(field[:, :, cols - HALO :], "gx", up_gx)
    south_east = lax.ppermute(field[:, :HALO, :HALO], both, pairs(1, 1))
    south_west = lax.ppermute(field[:, :HALO, cols - HALO :], both, pairs(-1, 1))
    north_east = lax.ppermute(field[:, rows - HALO :, :HALO], both, pairs(1, -1))
    north_west = lax.ppermute(field[:, rows - HALO :, cols - HALO :], both, pairs(-1, -1))
    gap = jnp.zeros((levels, rows, 128 - 2 * HALO), field.dtype)
    lanes = jnp.concatenate([east, gap, west], axis=2)
    corner_gap = jnp.zeros((levels, HALO, 128 - 2 * HALO), field.dtype)
    halo_rows = jnp.concatenate(
        [
            jnp.concatenate([south, south_east, corner_gap, south_west], axis=2),
            jnp.concatenate([north, north_east, corner_gap, north_west], axis=2),
        ],
        axis=1,
    )
    height = rows + 2 * HALO
    width = cols + 128
    r = jnp.arange(height, dtype=jnp.int32)
    c = jnp.arange(width, dtype=jnp.int32)
    global_r = gy_index * rows + jnp.where(r < rows + HALO, r, r - height)
    global_c = gx_index * cols + jnp.where(c < cols + HALO, c, c - width)
    inside_r = (global_r >= 0) & (global_r < count_gy * rows)
    inside_c = (global_c >= 0) & (global_c < count_gx * cols) & ((c < cols + HALO) | (c >= width - HALO))
    mask = (inside_r[:, None] & inside_c[None, :]).astype(jnp.float32)
    blocks = levels // LEVEL_BLOCK
    smem = pl.BlockSpec(memory_space=pltpu.SMEM)
    out, flux = pl.pallas_call(
        diffusion_kernel,
        grid=(blocks,),
        in_specs=[
            smem,
            smem,
            pl.BlockSpec((LEVEL_BLOCK, rows, cols), lambda b: (b, 0, 0)),
            pl.BlockSpec((LEVEL_BLOCK, rows, 128), lambda b: (b, 0, 0)),
            pl.BlockSpec((LEVEL_BLOCK, 2 * HALO, width), lambda b: (b, 0, 0)),
            pl.BlockSpec((height, width), lambda b: (0, 0)),
        ],
        out_specs=[
            pl.BlockSpec((LEVEL_BLOCK, rows, cols), lambda b: (b, 0, 0)),
            pl.BlockSpec((comps, rows, cols), lambda b: (0, 0, 0)),
        ],
        out_shape=[
            jax.ShapeDtypeStruct(field.shape, field.dtype),
            jax.ShapeDtypeStruct((comps, rows, cols), jnp.float32),
        ],
        compiler_params=pltpu.CompilerParams(dimension_semantics=("arbitrary",)),
        cost_estimate=pl.CostEstimate(
            flops=levels * height * width * STEPS * 10,
            transcendentals=0,
            bytes_accessed=2 * field.size * 4,
        ),
    )(atm_kappa, vert_weight, field, lanes, halo_rows, mask)
    return out, flux


def strip_sum(acc):
    return acc.sum(axis=0, keepdims=True).sum(axis=1, keepdims=True)


def cg_kernel(
    rounds, index_ref, rhs_stack, coded_stack, height_out, residual_out,
    rhs_ref, coded_ref, height_ref, residual_ref, pad_ref, dir_ref, img_ref,
):
    rows, cols = rhs_ref.shape
    tile_rows, tile_cols = height_out.shape
    gy = index_ref[0]
    gx = index_ref[1]

    def place(k, carry):
        gy_off = 0
        gx_off = 0
        for bit, (axis, distance) in enumerate(rounds):
            flag = lax.shift_right_logical(k, bit) & 1
            if axis == "gy":
                gy_off = gy_off + flag * distance
            else:
                gx_off = gx_off + flag * distance
        r0 = pl.multiple_of(lax.bitwise_xor(gy, gy_off) * tile_rows, tile_rows)
        c0 = pl.multiple_of(lax.bitwise_xor(gx, gx_off) * tile_cols, tile_cols)
        rhs_ref[pl.ds(r0, tile_rows), pl.ds(c0, tile_cols)] = rhs_stack[k]
        coded_ref[pl.ds(r0, tile_rows), pl.ds(c0, tile_cols)] = coded_stack[k]
        return carry

    lax.fori_loop(0, rhs_stack.shape[0], place, 0, unroll=8)
    strips = rows // 8
    zeros = jnp.zeros((8, cols), jnp.float32)
    pad_ref[0:8, :] = zeros
    pad_ref[rows + 8 : rows + 16, :] = zeros
    row = lax.broadcasted_iota(jnp.int32, (8, cols), 0)
    col = lax.broadcasted_iota(jnp.int32, (8, cols), 1)

    def at(k, offset=0):
        return pl.ds(pl.multiple_of(k * 8 + offset, 8), 8)

    def init(k, acc):
        v = rhs_ref[at(k), :]
        m = (coded_ref[at(k), :] >= 0.0).astype(jnp.float32)
        residual_ref[at(k), :] = v
        dir_ref[at(k), :] = v
        height_ref[at(k), :] = jnp.zeros_like(v)
        pad_ref[at(k, 8), :] = m * v
        return acc + v * v

    def image(k, acc):
        prev = pad_ref[at(k), :]
        cur = pad_ref[at(k, 8), :]
        nxt = pad_ref[at(k, 16), :]
        south = jnp.where(row == 7, pltpu.roll(nxt, 7, 0), pltpu.roll(cur, 7, 0))
        north = jnp.where(row == 0, pltpu.roll(prev, 1, 0), pltpu.roll(cur, 1, 0))
        east = jnp.where(col == cols - 1, 0.0, pltpu.roll(cur, cols - 1, 1))
        west = jnp.where(col == 0, 0.0, pltpu.roll(cur, 1, 1))
        beside = south + north + east + west
        ot = coded_ref[at(k), :]
        m = (ot >= 0.0).astype(jnp.float32)
        v = dir_ref[at(k), :]
        w = m * ((4.0 + ot) * v - beside) + (1.0 - m) * v
        img_ref[at(k), :] = w
        return acc + v * w

    def init_then_image(k, accs):
        squares, dots = accs
        return init(k, squares), image(k - 1, dots)

    first = init(0, zeros)
    squares, dots = lax.fori_loop(1, strips, init_then_image, (first, zeros), unroll=8)
    norm_now = strip_sum(squares)
    dot = strip_sum(image(strips - 1, dots))
    for step in range(ITERS):
        alpha = norm_now / dot

        def update(k, acc):
            v = dir_ref[at(k), :]
            height_ref[at(k), :] = height_ref[at(k), :] + alpha * v
            r = residual_ref[at(k), :] - alpha * img_ref[at(k), :]
            residual_ref[at(k), :] = r
            return acc + r * r

        norm_next = strip_sum(lax.fori_loop(0, strips, update, zeros, unroll=8))
        beta = norm_next / norm_now

        def direct(k, carry):
            d = residual_ref[at(k), :] + beta * dir_ref[at(k), :]
            dir_ref[at(k), :] = d
            m = (coded_ref[at(k), :] >= 0.0).astype(jnp.float32)
            pad_ref[at(k, 8), :] = m * d
            return carry

        def direct_then_image(k, acc):
            direct(k, 0)
            return image(k - 1, acc)

        if step < ITERS - 1:
            direct(0, 0)
            acc = lax.fori_loop(1, strips, direct_then_image, zeros, unroll=8)
            dot = strip_sum(image(strips - 1, acc))
        norm_now = norm_next
    r0 = pl.multiple_of(gy * tile_rows, tile_rows)
    c0 = pl.multiple_of(gx * tile_cols, tile_cols)
    height_out[...] = height_ref[pl.ds(r0, tile_rows), pl.ds(c0, tile_cols)]
    residual_out[...] = residual_ref[pl.ds(r0, tile_rows), pl.ds(c0, tile_cols)]


def solve_grid(rhs_stack, coded_stack, rounds):
    parts, tile_rows, tile_cols = rhs_stack.shape
    rows = lax.axis_size("gy") * tile_rows
    cols = lax.axis_size("gx") * tile_cols
    index = jnp.stack([lax.axis_index("gy"), lax.axis_index("gx")]).astype(jnp.int32)
    whole = pl.BlockSpec(memory_space=pltpu.VMEM)
    grid = pltpu.VMEM((rows, cols), jnp.float32)
    return pl.pallas_call(
        functools.partial(cg_kernel, rounds),
        in_specs=[pl.BlockSpec(memory_space=pltpu.SMEM), whole, whole],
        out_specs=[whole, whole],
        out_shape=[jax.ShapeDtypeStruct((tile_rows, tile_cols), jnp.float32)] * 2,
        scratch_shapes=[grid, grid, grid, grid, pltpu.VMEM((rows + 16, cols), jnp.float32), grid, grid],
    )(index, rhs_stack, coded_stack)


def body(
    atm_state, atm_kappa, vert_weight, remap_src, remap_count, remap_weight, land_mask, ocean_term
):
    levels, tile_lat, tile_lon = atm_state.shape
    kappa = atm_kappa[:, None, None]
    count_gx = lax.axis_size("gx")
    count_gy = lax.axis_size("gy")
    rounds = gather_rounds()
    coded_all = stack_gather(jnp.where(land_mask != 0, ocean_term, -1.0), rounds)
    field, flux = diffuse(atm_state, atm_kappa, vert_weight)
    flux = flux.reshape(flux.shape[0], tile_lat * tile_lon)
    ocean_blocks, lists, width, _ = remap_weight.shape
    comps = vert_weight.shape[0]
    own_blocks = tile_lat * tile_lon // width
    blocks = flux.astype(jnp.bfloat16).reshape(comps, own_blocks, width).transpose(1, 0, 2)
    devices = count_gx * count_gy
    gx_index = lax.axis_index("gx")
    gy_index = lax.axis_index("gy")
    me_index = gx_index * count_gy + gy_index
    east_index = (gx_index + 1) % count_gx * count_gy + gy_index
    west_index = (gx_index + count_gx - 1) % count_gx * count_gy + gy_index
    entries = ocean_blocks * lists
    slots = 2 * land_mask.shape[0]
    src_all = remap_src.reshape(devices, entries)
    live_all = (
        jnp.arange(lists, dtype=jnp.int32)[None, None, :]
        < remap_count.reshape(devices, ocean_blocks)[:, :, None]
    ).reshape(devices, entries)
    owner_all = src_all // own_blocks
    inside_all = src_all % own_blocks
    mine_owner = lax.dynamic_slice_in_dim(owner_all, me_index, 1, 0)[0]
    mine_inside = lax.dynamic_slice_in_dim(inside_all, me_index, 1, 0)[0]
    mine_live = lax.dynamic_slice_in_dim(live_all, me_index, 1, 0)[0]
    from_east = mine_live & (mine_owner == east_index)
    from_self = mine_live & (mine_owner == me_index)
    local_part = blocks[jnp.where(from_self, mine_inside, 0)]
    west_owner = lax.dynamic_slice_in_dim(owner_all, west_index, 1, 0)[0]
    west_inside = lax.dynamic_slice_in_dim(inside_all, west_index, 1, 0)[0]
    west_live = lax.dynamic_slice_in_dim(live_all, west_index, 1, 0)[0]
    wanted = (west_live & (west_owner == me_index)).astype(jnp.int32)
    wanted_rank = jnp.cumsum(wanted) - 1
    slot_ids = jnp.arange(slots, dtype=jnp.int32)
    picker = wanted[None, :] * (wanted_rank[None, :] == slot_ids[:, None]).astype(jnp.int32)
    send_index = jnp.sum(picker * west_inside[None, :], axis=1)
    send_valid = jnp.sum(picker, axis=1).astype(jnp.bfloat16)
    outgoing = blocks[send_index] * send_valid[:, None, None]
    incoming = shifted(outgoing, "gx", -1)
    east_int = from_east.astype(jnp.int32)
    east_rank = jnp.cumsum(east_int) - 1
    remote_part = incoming[jnp.where(from_east, east_rank, 0)]
    gathered = jnp.where(
        from_self[:, None, None],
        local_part,
        jnp.where(from_east[:, None, None], remote_part, jnp.zeros_like(local_part)),
    )
    gathered = gathered.reshape(ocean_blocks, lists, comps, width)
    ocean_rows, ocean_cols = land_mask.shape
    remapped = jnp.einsum(
        "bkij,bkcj->cbi", remap_weight, gathered, preferred_element_type=jnp.float32
    )
    ocean_flux = remapped.reshape(comps, ocean_rows, ocean_cols)
    rhs_tile = land_mask.astype(jnp.float32) * (ocean_flux[0] + ocean_flux[1])
    rhs = stack_gather(rhs_tile, rounds)
    height, residual = solve_grid(rhs, coded_all, rounds)
    return (field, ocean_flux, height, residual)


def solution(mesh):
    return jax.shard_map(
        body,
        mesh=mesh,
        in_specs=(
            P(None, "gy", "gx"),
            P(),
            P(),
            P(),
            P(),
            P(("gx", "gy"), None, None, None),
            P("gy", "gx"),
            P("gy", "gx"),
        ),
        out_specs=(P(None, "gy", "gx"), P(None, "gy", "gx"), P("gy", "gx"), P("gy", "gx")),
        check_vma=False,
    )
```

```python
import functools

import jax
import jax.numpy as jnp
from jax import lax
from jax.sharding import PartitionSpec as P
from jax.experimental import pallas as pl
from jax.experimental.pallas import tpu as pltpu

STEPS = 4
ITERS = 3


def with_halo(x, sides, width):
    for axis, dim in sides:
        size, length = (lax.axis_size(axis), x.shape[dim])
        up = [(i, (i + 1) % size) for i in range(size - 1)]
        down = [(j, i) for i, j in up]
        last = lax.slice_in_dim(x, length - width, length, axis=dim)
        first = lax.slice_in_dim(x, 0, width, axis=dim)
        before = lax.ppermute(last, axis, up)
        after = lax.ppermute(first, axis, down)
        x = jnp.concatenate([before, x, after], axis=dim)
    return x


def shifted(x, axis, by):
    size = lax.axis_size(axis)
    return lax.ppermute(x, axis, [(i, (i + by) % size) for i in range(size)])


def ocean_operator(vector, maskf, ocean_term):
    padded = with_halo(maskf * vector, (("gx", 1), ("gy", 0)), 1)
    beside = padded[2:, 1:-1] + padded[:-2, 1:-1] + padded[1:-1, 2:] + padded[1:-1, :-2]
    return maskf * ((4.0 + ocean_term) * vector - beside) + (1.0 - maskf) * vector


def square_total(residual):
    return lax.psum(jnp.sum(residual * residual), ("gx", "gy"))


def gather_rounds():
    rounds = []
    for axis, bits in (("gy", lax.axis_size("gy")), ("gx", lax.axis_size("gx"))):
        distances = []
        d = 1
        while d < bits:
            distances.append(d)
            d *= 2
        rounds.append([(axis, d) for d in distances])
    gy_rounds, gx_rounds = rounds
    far = gy_rounds[1::2] + gx_rounds[2:]
    near = gy_rounds[0::2] + gx_rounds[1:2] + gx_rounds[:1]
    return far + near


def stack_gather(tile, rounds):
    x = tile[None]
    for axis, distance in rounds:
        size = lax.axis_size(axis)
        other = lax.ppermute(x, axis, [(j, j ^ distance) for j in range(size)])
        x = jnp.concatenate([x, other], axis=0)
    return x


def grid_operator(vector, maskf, ocean_term):
    padded = jnp.pad(maskf * vector, 1)
    beside = padded[2:, 1:-1] + padded[:-2, 1:-1] + padded[1:-1, 2:] + padded[1:-1, :-2]
    return maskf * ((4.0 + ocean_term) * vector - beside) + (1.0 - maskf) * vector


HALO = 4
LEVEL_BLOCK = 16


def diffusion_kernel(grid_rows, grid_cols, kappa_ref, weight_ref, core_ref, lanes_ref, rows_ref, index_ref, out_ref, flux_ref):
    block = pl.program_id(0)
    levels, rows, cols = core_ref.shape

    @pl.when(block == 0)
    def _():
        flux_ref[...] = jnp.zeros_like(flux_ref)

    height, width = rows + 2 * HALO, cols + 128
    r = lax.broadcasted_iota(jnp.int32, (height, width), 0)
    c = lax.broadcasted_iota(jnp.int32, (height, width), 1)
    global_r = index_ref[0] * rows + jnp.where(r < rows + HALO, r, r - height)
    global_c = index_ref[1] * cols + jnp.where(c < cols + HALO, c, c - width)
    inside = (global_r >= 0) & (global_r < grid_rows) & (global_c >= 0) & (global_c < grid_cols)
    inside = inside & ((c < cols + HALO) | (c >= width - HALO))
    mask = inside.astype(jnp.float32)
    mask_side = mask[:rows, cols:]
    mask_low = mask[rows:, :]

    def level(l, carry):
        lev = block * levels + l
        kappa = kappa_ref[lev]
        top = jnp.concatenate([core_ref[l], lanes_ref[l]], axis=1)
        f = jnp.concatenate([top, rows_ref[l]], axis=0)
        height, width = f.shape
        for step in range(STEPS):
            beside = (
                pltpu.roll(f, height - 1, 0)
                + pltpu.roll(f, 1, 0)
                + pltpu.roll(f, width - 1, 1)
                + pltpu.roll(f, 1, 1)
            )
            f = f + kappa * (beside - 4.0 * f)
            top = jnp.concatenate([f[:rows, :cols], f[:rows, cols:] * mask_side], axis=1)
            f = jnp.concatenate([top, f[rows:, :] * mask_low], axis=0)
        core = f[:rows, :cols]
        out_ref[l] = core
        for c in range(flux_ref.shape[0]):
            flux_ref[c] += weight_ref[c, lev] * core
        return carry

    lax.fori_loop(0, levels, level, 0, unroll=8)


def diffuse(field, atm_kappa, vert_weight):
    levels, rows, cols = field.shape
    comps = vert_weight.shape[0]
    count_gx = lax.axis_size("gx")
    count_gy = lax.axis_size("gy")
    gx_index = lax.axis_index("gx")
    gy_index = lax.axis_index("gy")
    up_gx = [(i, i + 1) for i in range(count_gx - 1)]
    down_gx = [(i + 1, i) for i in range(count_gx - 1)]
    up_gy = [(i, i + 1) for i in range(count_gy - 1)]
    down_gy = [(i + 1, i) for i in range(count_gy - 1)]
    pairs = lambda di, dj: [
        ((i + di) * count_gy + j + dj, i * count_gy + j)
        for i in range(count_gx)
        for j in range(count_gy)
        if 0 <= i + di < count_gx and 0 <= j + dj < count_gy
    ]
    both = ("gx", "gy")
    south = lax.ppermute(field[:, :HALO, :], "gy", down_gy)
    north = lax.ppermute(field[:, rows - HALO :, :], "gy", up_gy)
    east = lax.ppermute(field[:, :, :HALO], "gx", down_gx)
    west = lax.ppermute(field[:, :, cols - HALO :], "gx", up_gx)
    south_east = lax.ppermute(field[:, :HALO, :HALO], both, pairs(1, 1))
    south_west = lax.ppermute(field[:, :HALO, cols - HALO :], both, pairs(-1, 1))
    north_east = lax.ppermute(field[:, rows - HALO :, :HALO], both, pairs(1, -1))
    north_west = lax.ppermute(field[:, rows - HALO :, cols - HALO :], both, pairs(-1, -1))
    gap = jnp.zeros((levels, rows, 128 - 2 * HALO), field.dtype)
    lanes = jnp.concatenate([east, gap, west], axis=2)
    corner_gap = jnp.zeros((levels, HALO, 128 - 2 * HALO), field.dtype)
    halo_rows = jnp.concatenate(
        [
            jnp.concatenate([south, south_east, corner_gap, south_west], axis=2),
            jnp.concatenate([north, north_east, corner_gap, north_west], axis=2),
        ],
        axis=1,
    )
    height = rows + 2 * HALO
    width = cols + 128
    index = jnp.stack([gy_index, gx_index]).astype(jnp.int32)
    blocks = levels // LEVEL_BLOCK
    smem = pl.BlockSpec(memory_space=pltpu.SMEM)
    out, flux = pl.pallas_call(
        functools.partial(diffusion_kernel, count_gy * rows, count_gx * cols),
        grid=(blocks,),
        in_specs=[
            smem,
            smem,
            pl.BlockSpec((LEVEL_BLOCK, rows, cols), lambda b: (b, 0, 0)),
            pl.BlockSpec((LEVEL_BLOCK, rows, 128), lambda b: (b, 0, 0)),
            pl.BlockSpec((LEVEL_BLOCK, 2 * HALO, width), lambda b: (b, 0, 0)),
            smem,
        ],
        out_specs=[
            pl.BlockSpec((LEVEL_BLOCK, rows, cols), lambda b: (b, 0, 0)),
            pl.BlockSpec((comps, rows, cols), lambda b: (0, 0, 0)),
        ],
        out_shape=[
            jax.ShapeDtypeStruct(field.shape, field.dtype),
            jax.ShapeDtypeStruct((comps, rows, cols), jnp.float32),
        ],
        compiler_params=pltpu.CompilerParams(dimension_semantics=("arbitrary",)),
        cost_estimate=pl.CostEstimate(
            flops=levels * height * width * STEPS * 10,
            transcendentals=0,
            bytes_accessed=2 * field.size * 4,
        ),
    )(atm_kappa, vert_weight, field, lanes, halo_rows, index)
    return out, flux


def strip_sum(acc):
    return acc.sum(axis=0, keepdims=True).sum(axis=1, keepdims=True)


def cg_kernel(
    rounds, index_ref, rhs_stack, coded_stack, height_out, residual_out,
    rhs_ref, coded_ref, height_ref, residual_ref, pad_ref, dir_ref, img_ref,
):
    rows, cols = rhs_ref.shape
    tile_rows, tile_cols = height_out.shape
    gy = index_ref[0]
    gx = index_ref[1]

    def place(k, carry):
        gy_off = 0
        gx_off = 0
        for bit, (axis, distance) in enumerate(rounds):
            flag = lax.shift_right_logical(k, bit) & 1
            if axis == "gy":
                gy_off = gy_off + flag * distance
            else:
                gx_off = gx_off + flag * distance
        r0 = pl.multiple_of(lax.bitwise_xor(gy, gy_off) * tile_rows, tile_rows)
        c0 = pl.multiple_of(lax.bitwise_xor(gx, gx_off) * tile_cols, tile_cols)
        rhs_ref[pl.ds(r0, tile_rows), pl.ds(c0, tile_cols)] = rhs_stack[k]
        coded_ref[pl.ds(r0, tile_rows), pl.ds(c0, tile_cols)] = coded_stack[k]
        return carry

    lax.fori_loop(0, rhs_stack.shape[0], place, 0, unroll=4)
    strips = rows // 8
    zeros = jnp.zeros((8, cols), jnp.float32)
    pad_ref[0:8, :] = zeros
    pad_ref[rows + 8 : rows + 16, :] = zeros
    row = lax.broadcasted_iota(jnp.int32, (8, cols), 0)
    col = lax.broadcasted_iota(jnp.int32, (8, cols), 1)

    def at(k, offset=0):
        return pl.ds(pl.multiple_of(k * 8 + offset, 8), 8)

    def init(k, acc):
        v = rhs_ref[at(k), :]
        m = (coded_ref[at(k), :] >= 0.0).astype(jnp.float32)
        residual_ref[at(k), :] = v
        dir_ref[at(k), :] = v
        height_ref[at(k), :] = jnp.zeros_like(v)
        pad_ref[at(k, 8), :] = m * v
        return acc + v * v

    def image(k, acc):
        prev = pad_ref[at(k), :]
        cur = pad_ref[at(k, 8), :]
        nxt = pad_ref[at(k, 16), :]
        south = jnp.where(row == 7, pltpu.roll(nxt, 7, 0), pltpu.roll(cur, 7, 0))
        north = jnp.where(row == 0, pltpu.roll(prev, 1, 0), pltpu.roll(cur, 1, 0))
        east = jnp.where(col == cols - 1, 0.0, pltpu.roll(cur, cols - 1, 1))
        west = jnp.where(col == 0, 0.0, pltpu.roll(cur, 1, 1))
        beside = south + north + east + west
        ot = coded_ref[at(k), :]
        m = (ot >= 0.0).astype(jnp.float32)
        v = dir_ref[at(k), :]
        w = m * ((4.0 + ot) * v - beside) + (1.0 - m) * v
        img_ref[at(k), :] = w
        return acc + v * w

    norm_now = strip_sum(lax.fori_loop(0, strips, init, zeros, unroll=8))
    for step in range(ITERS):
        alpha = norm_now / strip_sum(lax.fori_loop(0, strips, image, zeros, unroll=8))

        def update(k, acc):
            v = dir_ref[at(k), :]
            height_ref[at(k), :] = height_ref[at(k), :] + alpha * v
            r = residual_ref[at(k), :] - alpha * img_ref[at(k), :]
            residual_ref[at(k), :] = r
            return acc + r * r

        norm_next = strip_sum(lax.fori_loop(0, strips, update, zeros, unroll=8))
        beta = norm_next / norm_now

        def direct(k, carry):
            d = residual_ref[at(k), :] + beta * dir_ref[at(k), :]
            dir_ref[at(k), :] = d
            m = (coded_ref[at(k), :] >= 0.0).astype(jnp.float32)
            pad_ref[at(k, 8), :] = m * d
            return carry

        if step < ITERS - 1:
            lax.fori_loop(0, strips, direct, 0, unroll=8)
        norm_now = norm_next
    r0 = pl.multiple_of(gy * tile_rows, tile_rows)
    c0 = pl.multiple_of(gx * tile_cols, tile_cols)
    height_out[...] = height_ref[pl.ds(r0, tile_rows), pl.ds(c0, tile_cols)]
    residual_out[...] = residual_ref[pl.ds(r0, tile_rows), pl.ds(c0, tile_cols)]


def solve_grid(rhs_stack, coded_stack, rounds):
    parts, tile_rows, tile_cols = rhs_stack.shape
    rows = lax.axis_size("gy") * tile_rows
    cols = lax.axis_size("gx") * tile_cols
    index = jnp.stack([lax.axis_index("gy"), lax.axis_index("gx")]).astype(jnp.int32)
    whole = pl.BlockSpec(memory_space=pltpu.VMEM)
    grid = pltpu.VMEM((rows, cols), jnp.float32)
    return pl.pallas_call(
        functools.partial(cg_kernel, rounds),
        in_specs=[pl.BlockSpec(memory_space=pltpu.SMEM), whole, whole],
        out_specs=[whole, whole],
        out_shape=[jax.ShapeDtypeStruct((tile_rows, tile_cols), jnp.float32)] * 2,
        scratch_shapes=[grid, grid, grid, grid, pltpu.VMEM((rows + 16, cols), jnp.float32), grid, grid],
    )(index, rhs_stack, coded_stack)


def body(
    atm_state, atm_kappa, vert_weight, remap_src, remap_count, remap_weight, land_mask, ocean_term
):
    levels, tile_lat, tile_lon = atm_state.shape
    kappa = atm_kappa[:, None, None]
    count_gx = lax.axis_size("gx")
    count_gy = lax.axis_size("gy")
    rounds = gather_rounds()
    coded_all = stack_gather(jnp.where(land_mask != 0, ocean_term, -1.0), rounds)
    field, flux = diffuse(atm_state, atm_kappa, vert_weight)
    flux = flux.reshape(flux.shape[0], tile_lat * tile_lon)
    ocean_blocks, lists, width, _ = remap_weight.shape
    comps = vert_weight.shape[0]
    own_blocks = tile_lat * tile_lon // width
    blocks = flux.astype(jnp.bfloat16).reshape(comps, own_blocks, width).transpose(1, 0, 2)
    devices = count_gx * count_gy
    gx_index = lax.axis_index("gx")
    gy_index = lax.axis_index("gy")
    me_index = gx_index * count_gy + gy_index
    east_index = (gx_index + 1) % count_gx * count_gy + gy_index
    west_index = (gx_index + count_gx - 1) % count_gx * count_gy + gy_index
    entries = ocean_blocks * lists
    slots = 2 * land_mask.shape[0]
    src_all = remap_src.reshape(devices, entries)
    live_all = (
        jnp.arange(lists, dtype=jnp.int32)[None, None, :]
        < remap_count.reshape(devices, ocean_blocks)[:, :, None]
    ).reshape(devices, entries)
    owner_all = src_all // own_blocks
    inside_all = src_all % own_blocks
    mine_owner = lax.dynamic_slice_in_dim(owner_all, me_index, 1, 0)[0]
    mine_inside = lax.dynamic_slice_in_dim(inside_all, me_index, 1, 0)[0]
    mine_live = lax.dynamic_slice_in_dim(live_all, me_index, 1, 0)[0]
    from_east = mine_live & (mine_owner == east_index)
    from_self = mine_live & (mine_owner == me_index)
    local_part = blocks[jnp.where(from_self, mine_inside, 0)]
    west_owner = lax.dynamic_slice_in_dim(owner_all, west_index, 1, 0)[0]
    west_inside = lax.dynamic_slice_in_dim(inside_all, west_index, 1, 0)[0]
    west_live = lax.dynamic_slice_in_dim(live_all, west_index, 1, 0)[0]
    wanted = (west_live & (west_owner == me_index)).astype(jnp.int32)
    wanted_rank = jnp.cumsum(wanted) - 1
    slot_ids = jnp.arange(slots, dtype=jnp.int32)
    picker = wanted[None, :] * (wanted_rank[None, :] == slot_ids[:, None]).astype(jnp.int32)
    send_index = jnp.sum(picker * west_inside[None, :], axis=1)
    send_valid = jnp.sum(picker, axis=1).astype(jnp.bfloat16)
    outgoing = blocks[send_index] * send_valid[:, None, None]
    incoming = shifted(outgoing, "gx", -1)
    east_int = from_east.astype(jnp.int32)
    east_rank = jnp.cumsum(east_int) - 1
    remote_part = incoming[jnp.where(from_east, east_rank, 0)]
    gathered = jnp.where(
        from_self[:, None, None],
        local_part,
        jnp.where(from_east[:, None, None], remote_part, jnp.zeros_like(local_part)),
    )
    gathered = gathered.reshape(ocean_blocks, lists, comps, width)
    ocean_rows, ocean_cols = land_mask.shape
    remapped = jnp.einsum(
        "bkij,bkcj->cbi", remap_weight, gathered, preferred_element_type=jnp.float32
    )
    ocean_flux = remapped.reshape(comps, ocean_rows, ocean_cols)
    rhs_tile = land_mask.astype(jnp.float32) * (ocean_flux[0] + ocean_flux[1])
    rhs = stack_gather(rhs_tile, rounds)
    height, residual = solve_grid(rhs, coded_all, rounds)
    return (field, ocean_flux, height, residual)


def solution(mesh):
    return jax.shard_map(
        body,
        mesh=mesh,
        in_specs=(
            P(None, "gy", "gx"),
            P(),
            P(),
            P(),
            P(),
            P(("gx", "gy"), None, None, None),
            P("gy", "gx"),
            P("gy", "gx"),
        ),
        out_specs=(P(None, "gy", "gx"), P(None, "gy", "gx"), P("gy", "gx"), P("gy", "gx")),
        check_vma=False,
    )
```

```python
import functools

import jax
import jax.numpy as jnp
from jax import lax
from jax.sharding import PartitionSpec as P
from jax.experimental import pallas as pl
from jax.experimental.pallas import tpu as pltpu

STEPS = 4
ITERS = 3


def with_halo(x, sides, width):
    for axis, dim in sides:
        size, length = (lax.axis_size(axis), x.shape[dim])
        up = [(i, (i + 1) % size) for i in range(size - 1)]
        down = [(j, i) for i, j in up]
        last = lax.slice_in_dim(x, length - width, length, axis=dim)
        first = lax.slice_in_dim(x, 0, width, axis=dim)
        before = lax.ppermute(last, axis, up)
        after = lax.ppermute(first, axis, down)
        x = jnp.concatenate([before, x, after], axis=dim)
    return x


def shifted(x, axis, by):
    size = lax.axis_size(axis)
    return lax.ppermute(x, axis, [(i, (i + by) % size) for i in range(size)])


def ocean_operator(vector, maskf, ocean_term):
    padded = with_halo(maskf * vector, (("gx", 1), ("gy", 0)), 1)
    beside = padded[2:, 1:-1] + padded[:-2, 1:-1] + padded[1:-1, 2:] + padded[1:-1, :-2]
    return maskf * ((4.0 + ocean_term) * vector - beside) + (1.0 - maskf) * vector


def square_total(residual):
    return lax.psum(jnp.sum(residual * residual), ("gx", "gy"))


def gather_rounds():
    rounds = []
    for axis, bits in (("gy", lax.axis_size("gy")), ("gx", lax.axis_size("gx"))):
        distances = []
        d = 1
        while d < bits:
            distances.append(d)
            d *= 2
        rounds.append([(axis, d) for d in distances])
    gy_rounds, gx_rounds = rounds
    far = gy_rounds[1::2] + gx_rounds[2:]
    near = gy_rounds[0::2] + gx_rounds[1:2] + gx_rounds[:1]
    return far + near


def stack_gather(tile, rounds):
    x = tile[None]
    for axis, distance in rounds:
        size = lax.axis_size(axis)
        other = lax.ppermute(x, axis, [(j, j ^ distance) for j in range(size)])
        x = jnp.concatenate([x, other], axis=0)
    return x


def grid_operator(vector, maskf, ocean_term):
    padded = jnp.pad(maskf * vector, 1)
    beside = padded[2:, 1:-1] + padded[:-2, 1:-1] + padded[1:-1, 2:] + padded[1:-1, :-2]
    return maskf * ((4.0 + ocean_term) * vector - beside) + (1.0 - maskf) * vector


HALO = 4
LEVEL_BLOCK = 16


def diffusion_kernel(grid_rows, grid_cols, kappa_ref, weight_ref, core_ref, lanes_ref, rows_ref, index_ref, out_ref, flux_ref):
    block = pl.program_id(0)
    levels, rows, cols = core_ref.shape

    @pl.when(block == 0)
    def _():
        flux_ref[...] = jnp.zeros_like(flux_ref)

    height, width = rows + 2 * HALO, cols + 128
    r = lax.broadcasted_iota(jnp.int32, (height, width), 0)
    c = lax.broadcasted_iota(jnp.int32, (height, width), 1)
    global_r = index_ref[0] * rows + jnp.where(r < rows + HALO, r, r - height)
    global_c = index_ref[1] * cols + jnp.where(c < cols + HALO, c, c - width)
    inside = (global_r >= 0) & (global_r < grid_rows) & (global_c >= 0) & (global_c < grid_cols)
    inside = inside & ((c < cols + HALO) | (c >= width - HALO))
    mask = inside.astype(jnp.float32)
    mask_side = mask[:rows, cols:]
    mask_low = mask[rows:, :]

    def level(l, carry):
        lev = block * levels + l
        kappa = kappa_ref[lev]
        top = jnp.concatenate([core_ref[l], lanes_ref[l]], axis=1)
        f = jnp.concatenate([top, rows_ref[l]], axis=0)
        height, width = f.shape
        for step in range(STEPS):
            beside = (
                pltpu.roll(f, height - 1, 0)
                + pltpu.roll(f, 1, 0)
                + pltpu.roll(f, width - 1, 1)
                + pltpu.roll(f, 1, 1)
            )
            f = f + kappa * (beside - 4.0 * f)
            top = jnp.concatenate([f[:rows, :cols], f[:rows, cols:] * mask_side], axis=1)
            f = jnp.concatenate([top, f[rows:, :] * mask_low], axis=0)
        core = f[:rows, :cols]
        out_ref[l] = core
        for c in range(flux_ref.shape[0]):
            flux_ref[c] += weight_ref[c, lev] * core
        return carry

    lax.fori_loop(0, levels, level, 0, unroll=16)


def diffuse(field, atm_kappa, vert_weight):
    levels, rows, cols = field.shape
    comps = vert_weight.shape[0]
    count_gx = lax.axis_size("gx")
    count_gy = lax.axis_size("gy")
    gx_index = lax.axis_index("gx")
    gy_index = lax.axis_index("gy")
    up_gx = [(i, i + 1) for i in range(count_gx - 1)]
    down_gx = [(i + 1, i) for i in range(count_gx - 1)]
    up_gy = [(i, i + 1) for i in range(count_gy - 1)]
    down_gy = [(i + 1, i) for i in range(count_gy - 1)]
    pairs = lambda di, dj: [
        ((i + di) * count_gy + j + dj, i * count_gy + j)
        for i in range(count_gx)
        for j in range(count_gy)
        if 0 <= i + di < count_gx and 0 <= j + dj < count_gy
    ]
    both = ("gx", "gy")
    south = lax.ppermute(field[:, :HALO, :], "gy", down_gy)
    north = lax.ppermute(field[:, rows - HALO :, :], "gy", up_gy)
    east = lax.ppermute(field[:, :, :HALO], "gx", down_gx)
    west = lax.ppermute(field[:, :, cols - HALO :], "gx", up_gx)
    south_east = lax.ppermute(field[:, :HALO, :HALO], both, pairs(1, 1))
    south_west = lax.ppermute(field[:, :HALO, cols - HALO :], both, pairs(-1, 1))
    north_east = lax.ppermute(field[:, rows - HALO :, :HALO], both, pairs(1, -1))
    north_west = lax.ppermute(field[:, rows - HALO :, cols - HALO :], both, pairs(-1, -1))
    gap = jnp.zeros((levels, rows, 128 - 2 * HALO), field.dtype)
    lanes = jnp.concatenate([east, gap, west], axis=2)
    corner_gap = jnp.zeros((levels, HALO, 128 - 2 * HALO), field.dtype)
    halo_rows = jnp.concatenate(
        [
            jnp.concatenate([south, south_east, corner_gap, south_west], axis=2),
            jnp.concatenate([north, north_east, corner_gap, north_west], axis=2),
        ],
        axis=1,
    )
    height = rows + 2 * HALO
    width = cols + 128
    index = jnp.stack([gy_index, gx_index]).astype(jnp.int32)
    blocks = levels // LEVEL_BLOCK
    smem = pl.BlockSpec(memory_space=pltpu.SMEM)
    out, flux = pl.pallas_call(
        functools.partial(diffusion_kernel, count_gy * rows, count_gx * cols),
        grid=(blocks,),
        in_specs=[
            smem,
            smem,
            pl.BlockSpec((LEVEL_BLOCK, rows, cols), lambda b: (b, 0, 0)),
            pl.BlockSpec((LEVEL_BLOCK, rows, 128), lambda b: (b, 0, 0)),
            pl.BlockSpec((LEVEL_BLOCK, 2 * HALO, width), lambda b: (b, 0, 0)),
            smem,
        ],
        out_specs=[
            pl.BlockSpec((LEVEL_BLOCK, rows, cols), lambda b: (b, 0, 0)),
            pl.BlockSpec((comps, rows, cols), lambda b: (0, 0, 0)),
        ],
        out_shape=[
            jax.ShapeDtypeStruct(field.shape, field.dtype),
            jax.ShapeDtypeStruct((comps, rows, cols), jnp.float32),
        ],
        compiler_params=pltpu.CompilerParams(dimension_semantics=("arbitrary",)),
        cost_estimate=pl.CostEstimate(
            flops=levels * height * width * STEPS * 10,
            transcendentals=0,
            bytes_accessed=2 * field.size * 4,
        ),
    )(atm_kappa, vert_weight, field, lanes, halo_rows, index)
    return out, flux


def strip_sum(acc):
    return acc.sum(axis=0, keepdims=True).sum(axis=1, keepdims=True)


def cg_kernel(
    rounds, index_ref, rhs_stack, coded_stack, height_out, residual_out,
    rhs_ref, coded_ref, height_ref, residual_ref, pad_ref, dir_ref, img_ref,
):
    rows, cols = rhs_ref.shape
    tile_rows, tile_cols = height_out.shape
    gy = index_ref[0]
    gx = index_ref[1]

    def place(k, carry):
        gy_off = 0
        gx_off = 0
        for bit, (axis, distance) in enumerate(rounds):
            flag = lax.shift_right_logical(k, bit) & 1
            if axis == "gy":
                gy_off = gy_off + flag * distance
            else:
                gx_off = gx_off + flag * distance
        r0 = pl.multiple_of(lax.bitwise_xor(gy, gy_off) * tile_rows, tile_rows)
        c0 = pl.multiple_of(lax.bitwise_xor(gx, gx_off) * tile_cols, tile_cols)
        rhs_ref[pl.ds(r0, tile_rows), pl.ds(c0, tile_cols)] = rhs_stack[k]
        coded_ref[pl.ds(r0, tile_rows), pl.ds(c0, tile_cols)] = coded_stack[k]
        return carry

    lax.fori_loop(0, rhs_stack.shape[0], place, 0, unroll=4)
    strips = rows // 8
    zeros = jnp.zeros((8, cols), jnp.float32)
    pad_ref[0:8, :] = zeros
    pad_ref[rows + 8 : rows + 16, :] = zeros
    row = lax.broadcasted_iota(jnp.int32, (8, cols), 0)
    col = lax.broadcasted_iota(jnp.int32, (8, cols), 1)

    def at(k, offset=0):
        return pl.ds(pl.multiple_of(k * 8 + offset, 8), 8)

    def init(k, acc):
        v = rhs_ref[at(k), :]
        m = (coded_ref[at(k), :] >= 0.0).astype(jnp.float32)
        residual_ref[at(k), :] = v
        dir_ref[at(k), :] = v
        height_ref[at(k), :] = jnp.zeros_like(v)
        pad_ref[at(k, 8), :] = m * v
        return acc + v * v

    def image(k, acc):
        prev = pad_ref[at(k), :]
        cur = pad_ref[at(k, 8), :]
        nxt = pad_ref[at(k, 16), :]
        south = jnp.where(row == 7, pltpu.roll(nxt, 7, 0), pltpu.roll(cur, 7, 0))
        north = jnp.where(row == 0, pltpu.roll(prev, 1, 0), pltpu.roll(cur, 1, 0))
        east = jnp.where(col == cols - 1, 0.0, pltpu.roll(cur, cols - 1, 1))
        west = jnp.where(col == 0, 0.0, pltpu.roll(cur, 1, 1))
        beside = south + north + east + west
        ot = coded_ref[at(k), :]
        m = (ot >= 0.0).astype(jnp.float32)
        v = dir_ref[at(k), :]
        w = m * ((4.0 + ot) * v - beside) + (1.0 - m) * v
        img_ref[at(k), :] = w
        return acc + v * w

    norm_now = strip_sum(lax.fori_loop(0, strips, init, zeros, unroll=8))
    for step in range(ITERS):
        alpha = norm_now / strip_sum(lax.fori_loop(0, strips, image, zeros, unroll=8))

        def update(k, acc):
            v = dir_ref[at(k), :]
            height_ref[at(k), :] = height_ref[at(k), :] + alpha * v
            r = residual_ref[at(k), :] - alpha * img_ref[at(k), :]
            residual_ref[at(k), :] = r
            return acc + r * r

        norm_next = strip_sum(lax.fori_loop(0, strips, update, zeros, unroll=8))
        beta = norm_next / norm_now

        def direct(k, carry):
            d = residual_ref[at(k), :] + beta * dir_ref[at(k), :]
            dir_ref[at(k), :] = d
            m = (coded_ref[at(k), :] >= 0.0).astype(jnp.float32)
            pad_ref[at(k, 8), :] = m * d
            return carry

        if step < ITERS - 1:
            lax.fori_loop(0, strips, direct, 0, unroll=8)
        norm_now = norm_next
    r0 = pl.multiple_of(gy * tile_rows, tile_rows)
    c0 = pl.multiple_of(gx * tile_cols, tile_cols)
    height_out[...] = height_ref[pl.ds(r0, tile_rows), pl.ds(c0, tile_cols)]
    residual_out[...] = residual_ref[pl.ds(r0, tile_rows), pl.ds(c0, tile_cols)]


def solve_grid(rhs_stack, coded_stack, rounds):
    parts, tile_rows, tile_cols = rhs_stack.shape
    rows = lax.axis_size("gy") * tile_rows
    cols = lax.axis_size("gx") * tile_cols
    index = jnp.stack([lax.axis_index("gy"), lax.axis_index("gx")]).astype(jnp.int32)
    whole = pl.BlockSpec(memory_space=pltpu.VMEM)
    grid = pltpu.VMEM((rows, cols), jnp.float32)
    return pl.pallas_call(
        functools.partial(cg_kernel, rounds),
        in_specs=[pl.BlockSpec(memory_space=pltpu.SMEM), whole, whole],
        out_specs=[whole, whole],
        out_shape=[jax.ShapeDtypeStruct((tile_rows, tile_cols), jnp.float32)] * 2,
        scratch_shapes=[grid, grid, grid, grid, pltpu.VMEM((rows + 16, cols), jnp.float32), grid, grid],
    )(index, rhs_stack, coded_stack)


def body(
    atm_state, atm_kappa, vert_weight, remap_src, remap_count, remap_weight, land_mask, ocean_term
):
    levels, tile_lat, tile_lon = atm_state.shape
    kappa = atm_kappa[:, None, None]
    count_gx = lax.axis_size("gx")
    count_gy = lax.axis_size("gy")
    rounds = gather_rounds()
    coded_all = stack_gather(jnp.where(land_mask != 0, ocean_term, -1.0), rounds)
    field, flux = diffuse(atm_state, atm_kappa, vert_weight)
    flux = flux.reshape(flux.shape[0], tile_lat * tile_lon)
    ocean_blocks, lists, width, _ = remap_weight.shape
    comps = vert_weight.shape[0]
    own_blocks = tile_lat * tile_lon // width
    blocks = flux.astype(jnp.bfloat16).reshape(comps, own_blocks, width).transpose(1, 0, 2)
    devices = count_gx * count_gy
    gx_index = lax.axis_index("gx")
    gy_index = lax.axis_index("gy")
    me_index = gx_index * count_gy + gy_index
    east_index = (gx_index + 1) % count_gx * count_gy + gy_index
    west_index = (gx_index + count_gx - 1) % count_gx * count_gy + gy_index
    entries = ocean_blocks * lists
    slots = 2 * land_mask.shape[0]
    src_all = remap_src.reshape(devices, entries)
    live_all = (
        jnp.arange(lists, dtype=jnp.int32)[None, None, :]
        < remap_count.reshape(devices, ocean_blocks)[:, :, None]
    ).reshape(devices, entries)
    owner_all = src_all // own_blocks
    inside_all = src_all % own_blocks
    mine_owner = lax.dynamic_slice_in_dim(owner_all, me_index, 1, 0)[0]
    mine_inside = lax.dynamic_slice_in_dim(inside_all, me_index, 1, 0)[0]
    mine_live = lax.dynamic_slice_in_dim(live_all, me_index, 1, 0)[0]
    from_east = mine_live & (mine_owner == east_index)
    from_self = mine_live & (mine_owner == me_index)
    local_part = blocks[jnp.where(from_self, mine_inside, 0)]
    west_owner = lax.dynamic_slice_in_dim(owner_all, west_index, 1, 0)[0]
    west_inside = lax.dynamic_slice_in_dim(inside_all, west_index, 1, 0)[0]
    west_live = lax.dynamic_slice_in_dim(live_all, west_index, 1, 0)[0]
    wanted = (west_live & (west_owner == me_index)).astype(jnp.int32)
    wanted_rank = jnp.cumsum(wanted) - 1
    slot_ids = jnp.arange(slots, dtype=jnp.int32)
    picker = wanted[None, :] * (wanted_rank[None, :] == slot_ids[:, None]).astype(jnp.int32)
    send_index = jnp.sum(picker * west_inside[None, :], axis=1)
    send_valid = jnp.sum(picker, axis=1).astype(jnp.bfloat16)
    outgoing = blocks[send_index] * send_valid[:, None, None]
    incoming = shifted(outgoing, "gx", -1)
    east_int = from_east.astype(jnp.int32)
    east_rank = jnp.cumsum(east_int) - 1
    remote_part = incoming[jnp.where(from_east, east_rank, 0)]
    gathered = jnp.where(
        from_self[:, None, None],
        local_part,
        jnp.where(from_east[:, None, None], remote_part, jnp.zeros_like(local_part)),
    )
    gathered = gathered.reshape(ocean_blocks, lists, comps, width)
    ocean_rows, ocean_cols = land_mask.shape
    remapped = jnp.einsum(
        "bkij,bkcj->cbi", remap_weight, gathered, preferred_element_type=jnp.float32
    )
    ocean_flux = remapped.reshape(comps, ocean_rows, ocean_cols)
    rhs_tile = land_mask.astype(jnp.float32) * (ocean_flux[0] + ocean_flux[1])
    rhs = stack_gather(rhs_tile, rounds)
    height, residual = solve_grid(rhs, coded_all, rounds)
    return (field, ocean_flux, height, residual)


def solution(mesh):
    return jax.shard_map(
        body,
        mesh=mesh,
        in_specs=(
            P(None, "gy", "gx"),
            P(),
            P(),
            P(),
            P(),
            P(("gx", "gy"), None, None, None),
            P("gy", "gx"),
            P("gy", "gx"),
        ),
        out_specs=(P(None, "gy", "gx"), P(None, "gy", "gx"), P("gy", "gx"), P("gy", "gx")),
        check_vma=False,
    )
```
